128 devices in a mesh: blk: 64 (over z, x_lo, y, core), split: 2 (over x_hi).
Axes of the slice: x: 4 (x_hi: 2, x_lo: 2; x = x_hi * 2 + x_lo), y: 4, z: 4, core: 2. Of those that a mesh axis runs over, the one named last changes fastest.
Arguments:
- queries: bfloat16 [16384, 1024], P('blk'), may hold values from -400 to 400
- keys: bfloat16 [16384, 64], P(('blk', 'split')), may hold values from -5 to 5
- values: bfloat16 [16384, 64], P(('blk', 'split')), may hold values from -5 to 5
- out_grad: bfloat16 [16384, 1024], P('blk'), may hold values from -5 to 5
- block_lists: int32 [128, 48], P('blk'), may hold values from 0 to 127, as said below
Outputs:
- attended: bfloat16 [16384, 1024], P('blk')
- query_grad: bfloat16 [16384, 1024], P('blk')
- key_grad: bfloat16 [16384, 64], P(('blk', 'split'))
- value_grad: bfloat16 [16384, 64], P(('blk', 'split'))
The draws below stay inside these ranges and needn't reach their ends.
Inputs may be any that keep to these rules, and one draw needn't show every extreme that they name: `block_lists`: row a names blocks a, a - 1 and a + 1 (modulo 128); a block named twice in a row counts once.
All inputs are finite; a program needn't handle non-finite values.
Results may differ from the reference program's by a relative error of at most 0.019.
Values may be sent and summed in bfloat16 or wider, within the bound.
No kernel may reach another device: no remote copies, remote signals or barrier semaphores. Data moves between devices by JAX's collectives and lax.ppermute only.
A program may use at most 64 MiB of HBM per device.

```python
import math
import jax
import jax.numpy as jnp
from jax import lax

HEADS = 16
HEAD_DIM = 64
D = 1024
BLOCK = 128
NNZ = 48
QBD = 2
NQB = 128
TOKENS = 16384


def shared_keys(key):
    drawn = jax.random.normal(jax.random.fold_in(key, 11), (TOKENS, HEAD_DIM), jnp.float32)
    return jnp.clip(drawn, -4.5, 4.5)


def draw_keys(key, part):
    drawn_keys = shared_keys(key)
    return drawn_keys.astype(jnp.bfloat16)


def draw_queries(key, part):
    drawn = 2.5 * jax.random.normal(jax.random.fold_in(key, 12), (TOKENS, HEADS * HEAD_DIM), jnp.float32)
    drawn_rows = jnp.clip(drawn, -12.0, 12.0)
    return jnp.clip(drawn_rows, -400.0, 400.0).astype(jnp.bfloat16)


def draw_block_lists(key, part):
    block_ids = jnp.arange(NQB, dtype=jnp.int32)
    levels = jax.random.randint(jax.random.fold_in(key, 21), (NQB // QBD,), 0, 4)
    row_level = levels[block_ids // QBD]
    live_count = 3 + (NNZ - 3) * (1 + 3 * row_level) // 10
    nearby = (block_ids[:, None] + jax.random.randint(jax.random.fold_in(key, 22), (NQB, NNZ), -12, 13)) % NQB
    distant = jax.random.randint(jax.random.fold_in(key, 23), (NQB, NNZ), 0, NQB)
    pick_far = jax.random.randint(jax.random.fold_in(key, 24), (NQB, NNZ), 0, 3) == 0
    mixed = jnp.where(pick_far, distant, nearby)
    columns = jnp.arange(NNZ, dtype=jnp.int32)[None, :]
    entries = jnp.where(columns < live_count[:, None], mixed, block_ids[:, None])
    entries = jnp.where(columns == 0, block_ids[:, None], entries)
    entries = jnp.where(columns == 1, ((block_ids - 1) % NQB)[:, None], entries)
    entries = jnp.where(columns == 2, ((block_ids + 1) % NQB)[:, None], entries)
    return entries.astype(jnp.int32)


def block_levels(rng, dims, pieces, smallest, largest):
    def one(axis_at, blocks):
        draws = jax.random.uniform(jax.random.fold_in(jax.random.fold_in(rng, 6), axis_at), (blocks,), jnp.float32, smallest / len(pieces), largest / len(pieces))
        return jnp.repeat(jnp.exp(draws), dims[axis_at] // blocks).reshape((-1,) + (1,) * (len(dims) - axis_at - 1))

    level = one(*pieces[0])
    for cut in pieces[1:]:
        level = level * one(*cut)
    return level


def gaussian(key, shape, width, limit, split=(), kind=jnp.bfloat16):
    values = width * jax.random.normal(key, shape, jnp.float32)
    if split:
        values = values * block_levels(key, shape, split, -0.22, 0.18)
    return jnp.clip(values, -limit, limit).astype(kind)


def setup_inputs(seed: int = 0) -> dict:
    seeds = jax.random.split(jax.random.key(seed), 6)
    return {
        "queries": draw_queries(jax.random.fold_in(seeds[5], 71), 0),
        "keys": draw_keys(jax.random.fold_in(seeds[5], 71), 0),
        "values": gaussian(seeds[2], (TOKENS, HEAD_DIM), 1.0, 5.0, ((0, 128),)),
        "out_grad": gaussian(seeds[3], (TOKENS, D), 1.0, 5.0, ((0, 64),)),
        "block_lists": draw_block_lists(jax.random.fold_in(seeds[5], 71), 0),
    }


lowest_score = -1e+30

def reference(queries, keys, values, out_grad, block_lists):
    block_total = block_lists.shape[0]
    row_count = BLOCK * HEADS
    scale_value = 1.0 / math.sqrt(HEAD_DIM)
    key_blocks = keys.reshape(block_total, BLOCK, HEAD_DIM)
    value_blocks = values.reshape(block_total, BLOCK, HEAD_DIM)
    query_blocks = queries.reshape(block_total, row_count, HEAD_DIM)
    grad_blocks = out_grad.reshape(block_total, row_count, HEAD_DIM)
    positions = jnp.arange(NNZ, dtype=jnp.int32)

    def visit_block(running, block_index):
        key_acc, value_acc = running
        chosen = block_lists[block_index]
        matches = chosen[:, None] == chosen[None, :]
        earlier = jnp.any(jnp.logical_and(matches, positions[None, :] < positions[:, None]), axis=1)
        column_keep = jnp.repeat(jnp.logical_not(earlier), BLOCK)
        near_keys = key_blocks[chosen].reshape(NNZ * BLOCK, HEAD_DIM)
        near_values = value_blocks[chosen].reshape(NNZ * BLOCK, HEAD_DIM)
        query_rows = query_blocks[block_index]
        grad_rows = grad_blocks[block_index]
        scores = jnp.dot(query_rows, near_keys.T, preferred_element_type=jnp.float32) * scale_value
        scores = jnp.where(column_keep[None, :], scores, lowest_score)
        row_max = lax.optimization_barrier(jnp.max(scores, axis=1))
        numerator = jnp.where(column_keep[None, :], jnp.exp(scores - row_max[:, None]), 0.0)
        totals = lax.optimization_barrier(jnp.sum(numerator, axis=1))
        outputs = jnp.dot(numerator.astype(jnp.bfloat16), near_values, preferred_element_type=jnp.float32) / totals[:, None]
        log_total = row_max + jnp.log(totals)
        row_delta = lax.optimization_barrier(jnp.sum(grad_rows.astype(jnp.float32) * outputs, axis=1))
        probs_full = jnp.where(column_keep[None, :], jnp.exp(scores - log_total[:, None]), 0.0)
        probs_low = probs_full.astype(jnp.bfloat16)
        value_part = jnp.dot(probs_low.T, grad_rows, preferred_element_type=jnp.float32)
        prob_grad = jnp.dot(grad_rows, near_values.T, preferred_element_type=jnp.float32)
        score_grad = (probs_full * (prob_grad - row_delta[:, None])).astype(jnp.bfloat16)
        query_part = jnp.dot(score_grad, near_keys, preferred_element_type=jnp.float32) * scale_value
        key_part = jnp.dot(score_grad.T, query_rows, preferred_element_type=jnp.float32) * scale_value
        key_acc = key_acc.at[chosen].add(key_part.reshape(NNZ, BLOCK, HEAD_DIM))
        value_acc = value_acc.at[chosen].add(value_part.reshape(NNZ, BLOCK, HEAD_DIM))
        return ((key_acc, value_acc), (outputs.astype(jnp.bfloat16), query_part.astype(jnp.bfloat16)))
    start_acc = jnp.zeros((block_total, BLOCK, HEAD_DIM), jnp.float32)
    (key_acc, value_acc), (attended, query_grad) = lax.scan(visit_block, (start_acc, start_acc), jnp.arange(block_total, dtype=jnp.int32))
    attended = attended.reshape(block_total * BLOCK, HEADS * HEAD_DIM)
    query_grad = query_grad.reshape(block_total * BLOCK, HEADS * HEAD_DIM)
    key_grad = key_acc.reshape(block_total * BLOCK, HEAD_DIM).astype(jnp.bfloat16)
    value_grad = value_acc.reshape(block_total * BLOCK, HEAD_DIM).astype(jnp.bfloat16)
    return (attended, query_grad, key_grad, value_grad)
```

```python
import math

import jax
import jax.numpy as jnp
from jax import lax
from jax.experimental import pallas as pl
from jax.experimental.pallas import tpu as pltpu
from jax.sharding import PartitionSpec as P

HEADS = 16
HEAD_DIM = 64
BLOCK = 128

SCALE = 1.0 / math.sqrt(HEAD_DIM)
LOWEST = -1e30
VMEM_LIMIT = 60 * 1024 * 1024


def _smem():
    return pl.BlockSpec(memory_space=pltpu.SMEM)


def _vmem():
    return pl.BlockSpec(memory_space=pltpu.VMEM)


def _forward_kernel(lists_ref, keep_ref, q_ref, k_ref, v_ref, do_ref,
                    o_ref, lse_ref, delta_ref, m_sc, l_sc, acc_sc):
    query_count, slots = lists_ref.shape
    for qb in range(query_count):
        m_sc[...] = jnp.full(m_sc.shape, LOWEST, jnp.float32)
        l_sc[...] = jnp.zeros(l_sc.shape, jnp.float32)
        acc_sc[...] = jnp.zeros(acc_sc.shape, jnp.float32)

        def body(j, carry):
            @pl.when(keep_ref[qb, j] != 0)
            def _():
                b = lists_ref[qb, j]
                k = k_ref[b]
                v = v_ref[b]
                s = lax.dot_general(
                    q_ref[qb], k, (((1,), (1,)), ((), ())),
                    preferred_element_type=jnp.float32) * SCALE
                m_prev = m_sc[...]
                m_new = jnp.maximum(m_prev, jnp.max(s, axis=1, keepdims=True))
                alpha = jnp.exp(m_prev - m_new)
                p = jnp.exp(s - m_new)
                l_sc[...] = alpha * l_sc[...] + jnp.sum(p, axis=1, keepdims=True)
                acc_sc[...] = alpha * acc_sc[...] + jnp.dot(
                    p.astype(jnp.bfloat16), v, preferred_element_type=jnp.float32)
                m_sc[...] = m_new
            return carry

        lax.fori_loop(0, slots, body, 0)
        out = acc_sc[...] / l_sc[...]
        o_ref[qb] = out.astype(jnp.bfloat16)
        lse_ref[qb] = m_sc[...] + jnp.log(l_sc[...])
        delta_ref[qb] = jnp.sum(do_ref[qb].astype(jnp.float32) * out, axis=1, keepdims=True)


def _backward_kernel(lists_ref, keep_ref, q_ref, k_ref, v_ref, do_ref, lse_ref, delta_ref,
                     dq_ref, dk_ref, dv_ref, dq_sc):
    query_count, slots = lists_ref.shape
    dk_ref[...] = jnp.zeros(dk_ref.shape, jnp.float32)
    dv_ref[...] = jnp.zeros(dv_ref.shape, jnp.float32)
    for qb in range(query_count):
        dq_sc[...] = jnp.zeros(dq_sc.shape, jnp.float32)

        def body(j, carry):
            @pl.when(keep_ref[qb, j] != 0)
            def _():
                b = lists_ref[qb, j]
                k = k_ref[b]
                v = v_ref[b]
                q = q_ref[qb]
                do = do_ref[qb]
                s = lax.dot_general(
                    q, k, (((1,), (1,)), ((), ())),
                    preferred_element_type=jnp.float32) * SCALE
                p = jnp.exp(s - lse_ref[qb])
                dv_ref[b] += lax.dot_general(
                    p.astype(jnp.bfloat16), do, (((0,), (0,)), ((), ())),
                    preferred_element_type=jnp.float32)
                dp = lax.dot_general(
                    do, v, (((1,), (1,)), ((), ())),
                    preferred_element_type=jnp.float32)
                ds = (p * (dp - delta_ref[qb])).astype(jnp.bfloat16)
                dq_sc[...] += jnp.dot(ds, k, preferred_element_type=jnp.float32)
                dk_ref[b] += lax.dot_general(
                    ds, q, (((0,), (0,)), ((), ())),
                    preferred_element_type=jnp.float32)
            return carry

        lax.fori_loop(0, slots, body, 0)
        dq_ref[qb] = (dq_sc[...] * SCALE).astype(jnp.bfloat16)


def attend_local(q_rows, do_rows, key_blocks, value_blocks, lists, keep):
    query_count, rows, _ = q_rows.shape
    block_total = key_blocks.shape[0]
    f32 = jnp.float32
    o_rows, lse, delta = pl.pallas_call(
        _forward_kernel,
        out_shape=(
            jax.ShapeDtypeStruct((query_count, rows, HEAD_DIM), jnp.bfloat16),
            jax.ShapeDtypeStruct((query_count, rows, 1), f32),
            jax.ShapeDtypeStruct((query_count, rows, 1), f32),
        ),
        in_specs=[_smem(), _smem(), _vmem(), _vmem(), _vmem(), _vmem()],
        out_specs=(_vmem(), _vmem(), _vmem()),
        scratch_shapes=[
            pltpu.VMEM((rows, 1), f32),
            pltpu.VMEM((rows, 1), f32),
            pltpu.VMEM((rows, HEAD_DIM), f32),
        ],
        compiler_params=pltpu.CompilerParams(vmem_limit_bytes=VMEM_LIMIT),
    )(lists, keep, q_rows, key_blocks, value_blocks, do_rows)
    dq_rows, dk_blocks, dv_blocks = pl.pallas_call(
        _backward_kernel,
        out_shape=(
            jax.ShapeDtypeStruct((query_count, rows, HEAD_DIM), jnp.bfloat16),
            jax.ShapeDtypeStruct((block_total, BLOCK, HEAD_DIM), f32),
            jax.ShapeDtypeStruct((block_total, BLOCK, HEAD_DIM), f32),
        ),
        in_specs=[_smem(), _smem()] + [_vmem()] * 6,
        out_specs=(_vmem(), _vmem(), _vmem()),
        scratch_shapes=[pltpu.VMEM((rows, HEAD_DIM), f32)],
        compiler_params=pltpu.CompilerParams(vmem_limit_bytes=VMEM_LIMIT),
    )(lists, keep, q_rows, key_blocks, value_blocks, do_rows, lse, delta)
    return o_rows, dq_rows, dk_blocks, dv_blocks


def first_occurrence(block_lists):
    slots = block_lists.shape[1]
    positions = jnp.arange(slots, dtype=jnp.int32)
    matches = block_lists[:, :, None] == block_lists[:, None, :]
    earlier = jnp.any(matches & (positions[None, None, :] < positions[None, :, None]), axis=2)
    return jnp.logical_not(earlier).astype(jnp.int32)


def local(queries, keys, values, out_grad, block_lists):
    query_count = block_lists.shape[0]
    token_rows = queries.shape[0]
    split_size = lax.axis_size("split")
    split_place = lax.axis_index("split")
    width = queries.shape[1] // split_size
    heads_here = width // HEAD_DIM

    kv_all = lax.all_gather(jnp.stack([keys, values]), ("blk", "split"), axis=1, tiled=True)
    block_total = kv_all.shape[1] // BLOCK
    key_blocks = kv_all[0].reshape(block_total, BLOCK, HEAD_DIM)
    value_blocks = kv_all[1].reshape(block_total, BLOCK, HEAD_DIM)

    def my_heads(x):
        part = lax.dynamic_slice_in_dim(x, split_place * width, width, axis=1)
        return part.reshape(query_count, BLOCK * heads_here, HEAD_DIM)

    lists = block_lists.astype(jnp.int32)
    keep = first_occurrence(lists)
    o_rows, dq_rows, dk_blocks, dv_blocks = attend_local(
        my_heads(queries), my_heads(out_grad), key_blocks, value_blocks, lists, keep)

    attended = lax.all_gather(o_rows.reshape(token_rows, width), "split", axis=1, tiled=True)
    query_grad = lax.all_gather(dq_rows.reshape(token_rows, width), "split", axis=1, tiled=True)
    partial_kv = jnp.stack([
        dk_blocks.reshape(block_total * BLOCK, HEAD_DIM),
        dv_blocks.reshape(block_total * BLOCK, HEAD_DIM),
    ])
    owned = lax.psum_scatter(partial_kv, ("blk", "split"), scatter_dimension=1, tiled=True)
    key_grad = (owned[0] * SCALE).astype(jnp.bfloat16)
    value_grad = owned[1].astype(jnp.bfloat16)
    return (attended, query_grad, key_grad, value_grad)


def solution(mesh):
    placed = (
        P("blk", None),
        P(("blk", "split"), None),
        P(("blk", "split"), None),
        P("blk", None),
        P("blk", None),
    )
    return jax.shard_map(
        local,
        mesh=mesh,
        in_specs=placed,
        out_specs=(
            P("blk", None),
            P("blk", None),
            P(("blk", "split"), None),
            P(("blk", "split"), None),
        ),
        check_vma=False,
    )
```

```python
import math

import jax
import numpy as np
import jax.numpy as jnp
from jax import lax
from jax.experimental import pallas as pl
from jax.experimental.pallas import tpu as pltpu
from jax.sharding import PartitionSpec as P

HEADS = 16
HEAD_DIM = 64
BLOCK = 128

SCALE = 1.0 / math.sqrt(HEAD_DIM)
LOWEST = -1e30
VMEM_LIMIT = 60 * 1024 * 1024


def _smem():
    return pl.BlockSpec(memory_space=pltpu.SMEM)


def _vmem():
    return pl.BlockSpec(memory_space=pltpu.VMEM)


def _forward_kernel(lists_ref, keep_ref, q_ref, k_ref, v_ref, do_ref,
                    o_ref, lse_ref, delta_ref, m_sc, l_sc, acc_sc):
    query_count, slots = lists_ref.shape
    for qb in range(query_count):
        m_sc[...] = jnp.full(m_sc.shape, LOWEST, jnp.float32)
        l_sc[...] = jnp.zeros(l_sc.shape, jnp.float32)
        acc_sc[...] = jnp.zeros(acc_sc.shape, jnp.float32)

        def body(j, carry):
            @pl.when(keep_ref[qb, j] != 0)
            def _():
                b = lists_ref[qb, j]
                k = k_ref[b]
                v = v_ref[b]
                s = lax.dot_general(
                    q_ref[qb], k, (((1,), (1,)), ((), ())),
                    preferred_element_type=jnp.float32) * SCALE
                m_prev = m_sc[...]
                m_new = jnp.maximum(m_prev, jnp.max(s, axis=1, keepdims=True))
                alpha = jnp.exp(m_prev - m_new)
                p = jnp.exp(s - m_new)
                l_sc[...] = alpha * l_sc[...] + jnp.sum(p, axis=1, keepdims=True)
                acc_sc[...] = alpha * acc_sc[...] + jnp.dot(
                    p.astype(jnp.bfloat16), v, preferred_element_type=jnp.float32)
                m_sc[...] = m_new
            return carry

        lax.fori_loop(0, slots, body, 0)
        out = acc_sc[...] / l_sc[...]
        o_ref[qb] = out.astype(jnp.bfloat16)
        lse_ref[qb] = m_sc[...] + jnp.log(l_sc[...])
        delta_ref[qb] = jnp.sum(do_ref[qb].astype(jnp.float32) * out, axis=1, keepdims=True)


def _backward_kernel(lists_ref, keep_ref, q_ref, k_ref, v_ref, do_ref, lse_ref, delta_ref,
                     dq_ref, dk_ref, dv_ref, dq_sc):
    query_count, slots = lists_ref.shape
    dk_ref[...] = jnp.zeros(dk_ref.shape, jnp.float32)
    dv_ref[...] = jnp.zeros(dv_ref.shape, jnp.float32)
    for qb in range(query_count):
        dq_sc[...] = jnp.zeros(dq_sc.shape, jnp.float32)

        def body(j, carry):
            @pl.when(keep_ref[qb, j] != 0)
            def _():
                b = lists_ref[qb, j]
                k = k_ref[b]
                v = v_ref[b]
                q = q_ref[qb]
                do = do_ref[qb]
                s = lax.dot_general(
                    q, k, (((1,), (1,)), ((), ())),
                    preferred_element_type=jnp.float32) * SCALE
                p = jnp.exp(s - lse_ref[qb])
                dv_ref[b] += lax.dot_general(
                    p.astype(jnp.bfloat16), do, (((0,), (0,)), ((), ())),
                    preferred_element_type=jnp.float32)
                dp = lax.dot_general(
                    do, v, (((1,), (1,)), ((), ())),
                    preferred_element_type=jnp.float32)
                ds = (p * (dp - delta_ref[qb])).astype(jnp.bfloat16)
                dq_sc[...] += jnp.dot(ds, k, preferred_element_type=jnp.float32)
                dk_ref[b] += lax.dot_general(
                    ds, q, (((0,), (0,)), ((), ())),
                    preferred_element_type=jnp.float32)
            return carry

        lax.fori_loop(0, slots, body, 0)
        dq_ref[qb] = (dq_sc[...] * SCALE).astype(jnp.bfloat16)


def attend_local(q_rows, do_rows, key_blocks, value_blocks, lists, keep):
    query_count, rows, _ = q_rows.shape
    block_total = key_blocks.shape[0]
    f32 = jnp.float32
    o_rows, lse, delta = pl.pallas_call(
        _forward_kernel,
        out_shape=(
            jax.ShapeDtypeStruct((query_count, rows, HEAD_DIM), jnp.bfloat16),
            jax.ShapeDtypeStruct((query_count, rows, 1), f32),
            jax.ShapeDtypeStruct((query_count, rows, 1), f32),
        ),
        in_specs=[_smem(), _smem(), _vmem(), _vmem(), _vmem(), _vmem()],
        out_specs=(_vmem(), _vmem(), _vmem()),
        scratch_shapes=[
            pltpu.VMEM((rows, 1), f32),
            pltpu.VMEM((rows, 1), f32),
            pltpu.VMEM((rows, HEAD_DIM), f32),
        ],
        compiler_params=pltpu.CompilerParams(vmem_limit_bytes=VMEM_LIMIT),
    )(lists, keep, q_rows, key_blocks, value_blocks, do_rows)
    dq_rows, dk_blocks, dv_blocks = pl.pallas_call(
        _backward_kernel,
        out_shape=(
            jax.ShapeDtypeStruct((query_count, rows, HEAD_DIM), jnp.bfloat16),
            jax.ShapeDtypeStruct((block_total, BLOCK, HEAD_DIM), f32),
            jax.ShapeDtypeStruct((block_total, BLOCK, HEAD_DIM), f32),
        ),
        in_specs=[_smem(), _smem()] + [_vmem()] * 6,
        out_specs=(_vmem(), _vmem(), _vmem()),
        scratch_shapes=[pltpu.VMEM((rows, HEAD_DIM), f32)],
        compiler_params=pltpu.CompilerParams(vmem_limit_bytes=VMEM_LIMIT),
    )(lists, keep, q_rows, key_blocks, value_blocks, do_rows, lse, delta)
    return o_rows, dq_rows, dk_blocks, dv_blocks


def first_occurrence(block_lists):
    slots = block_lists.shape[1]
    positions = jnp.arange(slots, dtype=jnp.int32)
    matches = block_lists[:, :, None] == block_lists[:, None, :]
    earlier = jnp.any(matches & (positions[None, None, :] < positions[None, :, None]), axis=2)
    return jnp.logical_not(earlier).astype(jnp.int32)


def device_table(mesh):
    flat = mesh.devices.reshape(-1)
    table = np.array([[*d.coords, d.core_on_chip] for d in flat], dtype=np.int32)
    sizes = table.max(axis=0) + 1
    stages = [(1, int(sizes[1])), (0, int(sizes[0])), (2, int(sizes[2])), (3, int(sizes[3]))]
    stages = [(axis, size) for axis, size in stages if size > 1]
    where = {tuple(row): index for index, row in enumerate(table.tolist())}

    def pairs(axis, shift):
        out = []
        for index, row in enumerate(table.tolist()):
            dest = list(row)
            dest[axis] = (row[axis] + shift) % int(sizes[axis])
            out.append((index, where[tuple(dest)]))
        return out

    return table, stages, pairs


def make_local(mesh):
    table_np, stages, pairs = device_table(mesh)
    axes = ("blk", "split")

    def gather_blocks(piece):
        buf = piece[None]
        for axis, size in stages:
            pieces = [buf]
            for shift in range(1, size):
                pieces.append(lax.ppermute(buf, axes, pairs(axis, size - shift)))
            buf = jnp.stack(pieces)
        return buf.reshape((-1,) + piece.shape)

    def scatter_sum(part, piece_shape):
        part = part.reshape(tuple(size for _, size in reversed(stages)) + piece_shape)
        for axis, size in reversed(stages):
            total = part[0]
            for shift in range(1, size):
                sent = part[shift].astype(jnp.bfloat16)
                total = total + lax.ppermute(sent, axes, pairs(axis, shift)).astype(jnp.float32)
            part = total
        return part

    def local(queries, keys, values, out_grad, block_lists):
        query_count = block_lists.shape[0]
        token_rows = queries.shape[0]
        split_size = lax.axis_size("split")
        split_place = lax.axis_index("split")
        me = lax.axis_index("blk") * split_size + split_place
        width = queries.shape[1] // split_size
        heads_here = width // HEAD_DIM

        table = jnp.asarray(table_np)
        own = table[me]

        kv_held = gather_blocks(jnp.concatenate([keys, values], axis=1))
        block_total = kv_held.shape[0]
        key_blocks = kv_held[:, :, :HEAD_DIM]
        value_blocks = kv_held[:, :, HEAD_DIM:]

        def held_at(block):
            coords = table[block]
            position = jnp.zeros_like(block)
            stride = 1
            for axis, size in stages:
                position = position + ((coords[..., axis] - own[axis]) % size) * stride
                stride *= size
            return position

        def my_heads(x):
            part = lax.dynamic_slice_in_dim(x, split_place * width, width, axis=1)
            return part.reshape(query_count, BLOCK * heads_here, HEAD_DIM)

        lists = block_lists.astype(jnp.int32)
        keep = first_occurrence(lists)
        o_rows, dq_rows, dk_blocks, dv_blocks = attend_local(
            my_heads(queries), my_heads(out_grad), key_blocks, value_blocks,
            held_at(lists), keep)

        def join_halves(rows):
            mine = rows.reshape(token_rows, width)
            other = lax.ppermute(mine, "split", [(i, (i + 1) % split_size) for i in range(split_size)])
            return jnp.where(split_place == 0,
                             jnp.concatenate([mine, other], axis=1),
                             jnp.concatenate([other, mine], axis=1))

        attended = join_halves(o_rows)
        query_grad = join_halves(dq_rows)
        partial_kv = jnp.concatenate([dk_blocks, dv_blocks], axis=2)
        owned = scatter_sum(partial_kv, (BLOCK, 2 * HEAD_DIM))
        key_grad = (owned[:, :HEAD_DIM] * SCALE).astype(jnp.bfloat16)
        value_grad = owned[:, HEAD_DIM:].astype(jnp.bfloat16)
        return (attended, query_grad, key_grad, value_grad)

    return local


def solution(mesh):
    placed = (
        P("blk", None),
        P(("blk", "split"), None),
        P(("blk", "split"), None),
        P("blk", None),
        P("blk", None),
    )
    return jax.shard_map(
        make_local(mesh),
        mesh=mesh,
        in_specs=placed,
        out_specs=(
            P("blk", None),
            P("blk", None),
            P(("blk", "split"), None),
            P(("blk", "split"), None),
        ),
        check_vma=False,
    )
```

```python
import math

import jax
import numpy as np
import jax.numpy as jnp
from jax import lax
from jax.experimental import pallas as pl
from jax.experimental.pallas import tpu as pltpu
from jax.sharding import PartitionSpec as P

HEADS = 16
HEAD_DIM = 64
BLOCK = 128

SCALE = 1.0 / math.sqrt(HEAD_DIM)
LOWEST = -1e30
VMEM_LIMIT = 60 * 1024 * 1024


def _smem():
    return pl.BlockSpec(memory_space=pltpu.SMEM)


def _vmem():
    return pl.BlockSpec(memory_space=pltpu.VMEM)


def _nn(a, b):
    return jnp.dot(a, b, preferred_element_type=jnp.float32)


def _nt(a, b):
    return lax.dot_general(a, b, (((1,), (1,)), ((), ())), preferred_element_type=jnp.float32)


def _forward_kernel(lists_ref, keep_ref, q_ref, k_ref, vt_ref, dot_ref,
                    ot_ref, lse_ref, delta_ref, m_sc, l_sc, acc_sc):
    query_count, slots = lists_ref.shape
    for qb in range(query_count):
        m_sc[...] = jnp.full(m_sc.shape, LOWEST, jnp.float32)
        l_sc[...] = jnp.zeros(l_sc.shape, jnp.float32)
        acc_sc[...] = jnp.zeros(acc_sc.shape, jnp.float32)

        def body(j, carry):
            @pl.when(keep_ref[qb, j] != 0)
            def _():
                b = lists_ref[qb, j]
                st = _nt(k_ref[b], q_ref[qb]) * SCALE
                m_prev = m_sc[...]
                m_new = jnp.maximum(m_prev, jnp.max(st, axis=0, keepdims=True))
                alpha = jnp.exp(m_prev - m_new)
                pt = jnp.exp(st - m_new)
                l_sc[...] = alpha * l_sc[...] + jnp.sum(pt, axis=0, keepdims=True)
                acc_sc[...] = alpha * acc_sc[...] + _nn(vt_ref[b], pt.astype(jnp.bfloat16))
                m_sc[...] = m_new
            return carry

        lax.fori_loop(0, slots, body, 0)
        out = acc_sc[...] / l_sc[...]
        ot_ref[qb] = out.astype(jnp.bfloat16)
        lse_ref[qb] = m_sc[...] + jnp.log(l_sc[...])
        delta_ref[qb] = jnp.sum(dot_ref[qb].astype(jnp.float32) * out, axis=0, keepdims=True)


def _backward_kernel(lists_ref, keep_ref, q_ref, k_ref, kt_ref, v_ref, do_ref, lse_ref, delta_ref,
                     dqt_ref, dk_ref, dv_ref, dq_sc):
    query_count, slots = lists_ref.shape
    dk_ref[...] = jnp.zeros(dk_ref.shape, jnp.float32)
    dv_ref[...] = jnp.zeros(dv_ref.shape, jnp.float32)
    for qb in range(query_count):
        dq_sc[...] = jnp.zeros(dq_sc.shape, jnp.float32)

        def body(j, carry):
            @pl.when(keep_ref[qb, j] != 0)
            def _():
                b = lists_ref[qb, j]
                q = q_ref[qb]
                do = do_ref[qb]
                st = _nt(k_ref[b], q) * SCALE
                pt = jnp.exp(st - lse_ref[qb])
                dv_ref[b] += _nn(pt.astype(jnp.bfloat16), do)
                dpt = _nt(v_ref[b], do)
                dst = (pt * (dpt - delta_ref[qb])).astype(jnp.bfloat16)
                dq_sc[...] += _nn(kt_ref[b], dst)
                dk_ref[b] += _nn(dst, q)
            return carry

        lax.fori_loop(0, slots, body, 0)
        dqt_ref[qb] = (dq_sc[...] * SCALE).astype(jnp.bfloat16)


def attend_local(q_rows, do_rows, key_blocks, value_blocks, lists, keep):
    query_count, rows, _ = q_rows.shape
    block_total = key_blocks.shape[0]
    f32 = jnp.float32
    key_t = jnp.swapaxes(key_blocks, 1, 2)
    value_t = jnp.swapaxes(value_blocks, 1, 2)
    do_t = jnp.swapaxes(do_rows, 1, 2)
    o_t, lse, delta = pl.pallas_call(
        _forward_kernel,
        out_shape=(
            jax.ShapeDtypeStruct((query_count, HEAD_DIM, rows), jnp.bfloat16),
            jax.ShapeDtypeStruct((query_count, 1, rows), f32),
            jax.ShapeDtypeStruct((query_count, 1, rows), f32),
        ),
        in_specs=[_smem(), _smem(), _vmem(), _vmem(), _vmem(), _vmem()],
        out_specs=(_vmem(), _vmem(), _vmem()),
        scratch_shapes=[
            pltpu.VMEM((1, rows), f32),
            pltpu.VMEM((1, rows), f32),
            pltpu.VMEM((HEAD_DIM, rows), f32),
        ],
        compiler_params=pltpu.CompilerParams(vmem_limit_bytes=VMEM_LIMIT),
    )(lists, keep, q_rows, key_blocks, value_t, do_t)
    dq_t, dk_blocks, dv_blocks = pl.pallas_call(
        _backward_kernel,
        out_shape=(
            jax.ShapeDtypeStruct((query_count, HEAD_DIM, rows), jnp.bfloat16),
            jax.ShapeDtypeStruct((block_total, BLOCK, HEAD_DIM), f32),
            jax.ShapeDtypeStruct((block_total, BLOCK, HEAD_DIM), f32),
        ),
        in_specs=[_smem(), _smem()] + [_vmem()] * 7,
        out_specs=(_vmem(), _vmem(), _vmem()),
        scratch_shapes=[pltpu.VMEM((HEAD_DIM, rows), f32)],
        compiler_params=pltpu.CompilerParams(vmem_limit_bytes=VMEM_LIMIT),
    )(lists, keep, q_rows, key_blocks, key_t, value_blocks, do_rows, lse, delta)
    return jnp.swapaxes(o_t, 1, 2), jnp.swapaxes(dq_t, 1, 2), dk_blocks, dv_blocks


def first_occurrence(block_lists):
    slots = block_lists.shape[1]
    positions = jnp.arange(slots, dtype=jnp.int32)
    matches = block_lists[:, :, None] == block_lists[:, None, :]
    earlier = jnp.any(matches & (positions[None, None, :] < positions[None, :, None]), axis=2)
    return jnp.logical_not(earlier).astype(jnp.int32)


def device_table(mesh):
    flat = mesh.devices.reshape(-1)
    table = np.array([[*d.coords, d.core_on_chip] for d in flat], dtype=np.int32)
    sizes = table.max(axis=0) + 1
    stages = [(1, int(sizes[1])), (0, int(sizes[0])), (2, int(sizes[2])), (3, int(sizes[3]))]
    stages = [(axis, size) for axis, size in stages if size > 1]
    where = {tuple(row): index for index, row in enumerate(table.tolist())}

    def pairs(axis, shift):
        out = []
        for index, row in enumerate(table.tolist()):
            dest = list(row)
            dest[axis] = (row[axis] + shift) % int(sizes[axis])
            out.append((index, where[tuple(dest)]))
        return out

    return table, stages, pairs


def make_local(mesh):
    table_np, stages, pairs = device_table(mesh)
    axes = ("blk", "split")

    def gather_blocks(piece):
        buf = piece[None]
        for axis, size in stages:
            pieces = [buf]
            for shift in range(1, size):
                pieces.append(lax.ppermute(buf, axes, pairs(axis, size - shift)))
            buf = jnp.stack(pieces)
        return buf.reshape((-1,) + piece.shape)

    def scatter_sum(part, piece_shape):
        part = part.reshape(tuple(size for _, size in reversed(stages)) + piece_shape)
        for axis, size in reversed(stages):
            total = part[0]
            for shift in range(1, size):
                sent = part[shift].astype(jnp.bfloat16)
                total = total + lax.ppermute(sent, axes, pairs(axis, shift)).astype(jnp.float32)
            part = total
        return part

    def local(queries, keys, values, out_grad, block_lists):
        query_count = block_lists.shape[0]
        token_rows = queries.shape[0]
        split_size = lax.axis_size("split")
        split_place = lax.axis_index("split")
        me = lax.axis_index("blk") * split_size + split_place
        width = queries.shape[1] // split_size
        heads_here = width // HEAD_DIM

        table = jnp.asarray(table_np)
        own = table[me]

        kv_held = gather_blocks(jnp.concatenate([keys, values], axis=1))
        block_total = kv_held.shape[0]
        key_blocks = kv_held[:, :, :HEAD_DIM]
        value_blocks = kv_held[:, :, HEAD_DIM:]

        def held_at(block):
            coords = table[block]
            position = jnp.zeros_like(block)
            stride = 1
            for axis, size in stages:
                position = position + ((coords[..., axis] - own[axis]) % size) * stride
                stride *= size
            return position

        def my_heads(x):
            part = lax.dynamic_slice_in_dim(x, split_place * width, width, axis=1)
            return part.reshape(query_count, BLOCK * heads_here, HEAD_DIM)

        lists = block_lists.astype(jnp.int32)
        keep = first_occurrence(lists)
        o_rows, dq_rows, dk_blocks, dv_blocks = attend_local(
            my_heads(queries), my_heads(out_grad), key_blocks, value_blocks,
            held_at(lists), keep)

        def join_halves(rows):
            mine = rows.reshape(token_rows, width)
            other = lax.ppermute(mine, "split", [(i, (i + 1) % split_size) for i in range(split_size)])
            return jnp.where(split_place == 0,
                             jnp.concatenate([mine, other], axis=1),
                             jnp.concatenate([other, mine], axis=1))

        attended = join_halves(o_rows)
        query_grad = join_halves(dq_rows)
        partial_kv = jnp.concatenate([dk_blocks, dv_blocks], axis=2)
        owned = scatter_sum(partial_kv, (BLOCK, 2 * HEAD_DIM))
        key_grad = (owned[:, :HEAD_DIM] * SCALE).astype(jnp.bfloat16)
        value_grad = owned[:, HEAD_DIM:].astype(jnp.bfloat16)
        return (attended, query_grad, key_grad, value_grad)

    return local


def solution(mesh):
    placed = (
        P("blk", None),
        P(("blk", "split"), None),
        P(("blk", "split"), None),
        P("blk", None),
        P("blk", None),
    )
    return jax.shard_map(
        make_local(mesh),
        mesh=mesh,
        in_specs=placed,
        out_specs=(
            P("blk", None),
            P("blk", None),
            P(("blk", "split"), None),
            P(("blk", "split"), None),
        ),
        check_vma=False,
    )
```

```python
import math

import jax
import numpy as np
import jax.numpy as jnp
from jax import lax
from jax.experimental import pallas as pl
from jax.experimental.pallas import tpu as pltpu
from jax.sharding import PartitionSpec as P

HEADS = 16
HEAD_DIM = 64
BLOCK = 128

SCALE = 1.0 / math.sqrt(HEAD_DIM)
LOWEST = -1e30
VMEM_LIMIT = 60 * 1024 * 1024


def _smem():
    return pl.BlockSpec(memory_space=pltpu.SMEM)


def _vmem():
    return pl.BlockSpec(memory_space=pltpu.VMEM)


def _nn(a, b):
    return jnp.dot(a, b, preferred_element_type=jnp.float32)


def _nt(a, b):
    return lax.dot_general(a, b, (((1,), (1,)), ((), ())), preferred_element_type=jnp.float32)


def _rows_of(kvt_ref, b, first):
    tile = kvt_ref[b, first:first + HEAD_DIM, :].astype(jnp.float32)
    return jnp.transpose(tile).astype(jnp.bfloat16)


def _forward_kernel(lists_ref, keep_ref, q_ref, kvt_ref, dot_ref,
                    ot_ref, lse_ref, delta_ref, m_sc, l_sc, acc_sc):
    query_count, slots = lists_ref.shape
    for qb in range(query_count):
        m_sc[...] = jnp.full(m_sc.shape, LOWEST, jnp.float32)
        l_sc[...] = jnp.zeros(l_sc.shape, jnp.float32)
        acc_sc[...] = jnp.zeros(acc_sc.shape, jnp.float32)

        def body(j, carry):
            @pl.when(keep_ref[qb, j] != 0)
            def _():
                b = lists_ref[qb, j]
                st = _nt(_rows_of(kvt_ref, b, 0), q_ref[qb]) * SCALE
                m_prev = m_sc[...]
                m_new = jnp.maximum(m_prev, jnp.max(st, axis=0, keepdims=True))
                alpha = jnp.exp(m_prev - m_new)
                pt = jnp.exp(st - m_new)
                l_sc[...] = alpha * l_sc[...] + jnp.sum(pt, axis=0, keepdims=True)
                acc_sc[...] = alpha * acc_sc[...] + _nn(
                    kvt_ref[b, HEAD_DIM:, :], pt.astype(jnp.bfloat16))
                m_sc[...] = m_new
            return carry

        lax.fori_loop(0, slots, body, 0)
        out = acc_sc[...] / l_sc[...]
        ot_ref[qb] = out.astype(jnp.bfloat16)
        lse_ref[qb] = m_sc[...] + jnp.log(l_sc[...])
        delta_ref[qb] = jnp.sum(dot_ref[qb].astype(jnp.float32) * out, axis=0, keepdims=True)


def _backward_kernel(lists_ref, keep_ref, q_ref, kvt_ref, do_ref, lse_ref, delta_ref,
                     dqt_ref, dk_ref, dv_ref, dq_sc):
    query_count, slots = lists_ref.shape
    dk_ref[...] = jnp.zeros(dk_ref.shape, jnp.float32)
    dv_ref[...] = jnp.zeros(dv_ref.shape, jnp.float32)
    for qb in range(query_count):
        dq_sc[...] = jnp.zeros(dq_sc.shape, jnp.float32)

        def body(j, carry):
            @pl.when(keep_ref[qb, j] != 0)
            def _():
                b = lists_ref[qb, j]
                q = q_ref[qb]
                do = do_ref[qb]
                st = _nt(_rows_of(kvt_ref, b, 0), q) * SCALE
                pt = jnp.exp(st - lse_ref[qb])
                dv_ref[b] += _nn(pt.astype(jnp.bfloat16), do)
                dpt = _nt(_rows_of(kvt_ref, b, HEAD_DIM), do)
                dst = (pt * (dpt - delta_ref[qb])).astype(jnp.bfloat16)
                dq_sc[...] += _nn(kvt_ref[b, :HEAD_DIM, :], dst)
                dk_ref[b] += _nn(dst, q)
            return carry

        lax.fori_loop(0, slots, body, 0)
        dqt_ref[qb] = (dq_sc[...] * SCALE).astype(jnp.bfloat16)


def attend_local(q_rows, do_rows, kv_t, lists, keep):
    query_count, rows, _ = q_rows.shape
    block_total = kv_t.shape[0]
    f32 = jnp.float32
    do_t = jnp.swapaxes(do_rows, 1, 2)
    o_t, lse, delta = pl.pallas_call(
        _forward_kernel,
        out_shape=(
            jax.ShapeDtypeStruct((query_count, HEAD_DIM, rows), jnp.bfloat16),
            jax.ShapeDtypeStruct((query_count, 1, rows), f32),
            jax.ShapeDtypeStruct((query_count, 1, rows), f32),
        ),
        in_specs=[_smem(), _smem(), _vmem(), _vmem(), _vmem()],
        out_specs=(_vmem(), _vmem(), _vmem()),
        scratch_shapes=[
            pltpu.VMEM((1, rows), f32),
            pltpu.VMEM((1, rows), f32),
            pltpu.VMEM((HEAD_DIM, rows), f32),
        ],
        compiler_params=pltpu.CompilerParams(vmem_limit_bytes=VMEM_LIMIT),
    )(lists, keep, q_rows, kv_t, do_t)
    dq_t, dk_blocks, dv_blocks = pl.pallas_call(
        _backward_kernel,
        out_shape=(
            jax.ShapeDtypeStruct((query_count, HEAD_DIM, rows), jnp.bfloat16),
            jax.ShapeDtypeStruct((block_total, BLOCK, HEAD_DIM), f32),
            jax.ShapeDtypeStruct((block_total, BLOCK, HEAD_DIM), f32),
        ),
        in_specs=[_smem(), _smem()] + [_vmem()] * 5,
        out_specs=(_vmem(), _vmem(), _vmem()),
        scratch_shapes=[pltpu.VMEM((HEAD_DIM, rows), f32)],
        compiler_params=pltpu.CompilerParams(vmem_limit_bytes=VMEM_LIMIT),
    )(lists, keep, q_rows, kv_t, do_rows, lse, delta)
    return jnp.swapaxes(o_t, 1, 2), jnp.swapaxes(dq_t, 1, 2), dk_blocks, dv_blocks


def first_occurrence(block_lists):
    slots = block_lists.shape[1]
    positions = jnp.arange(slots, dtype=jnp.int32)
    matches = block_lists[:, :, None] == block_lists[:, None, :]
    earlier = jnp.any(matches & (positions[None, None, :] < positions[None, :, None]), axis=2)
    return jnp.logical_not(earlier).astype(jnp.int32)


def device_table(mesh):
    flat = mesh.devices.reshape(-1)
    table = np.array([[*d.coords, d.core_on_chip] for d in flat], dtype=np.int32)
    sizes = table.max(axis=0) + 1
    stages = [(1, int(sizes[1])), (0, int(sizes[0])), (2, int(sizes[2])), (3, int(sizes[3]))]
    stages = [(axis, size) for axis, size in stages if size > 1]
    where = {tuple(row): index for index, row in enumerate(table.tolist())}

    def pairs(axis, shift):
        out = []
        for index, row in enumerate(table.tolist()):
            dest = list(row)
            dest[axis] = (row[axis] + shift) % int(sizes[axis])
            out.append((index, where[tuple(dest)]))
        return out

    return table, stages, pairs


def make_local(mesh):
    table_np, stages, pairs = device_table(mesh)
    axes = ("blk", "split")

    def gather_blocks(piece):
        buf = piece[None]
        for axis, size in stages:
            pieces = [buf]
            for shift in range(1, size):
                pieces.append(lax.ppermute(buf, axes, pairs(axis, size - shift)))
            buf = jnp.concatenate(pieces, axis=0)
        return buf

    def scatter_sum(part, piece_shape):
        part = part.reshape(tuple(size for _, size in reversed(stages)) + piece_shape)
        for axis, size in reversed(stages):
            total = part[0]
            for shift in range(1, size):
                sent = part[shift].astype(jnp.bfloat16)
                total = total + lax.ppermute(sent, axes, pairs(axis, shift)).astype(jnp.float32)
            part = total
        return part

    def local(queries, keys, values, out_grad, block_lists):
        query_count = block_lists.shape[0]
        token_rows = queries.shape[0]
        split_size = lax.axis_size("split")
        split_place = lax.axis_index("split")
        me = lax.axis_index("blk") * split_size + split_place
        width = queries.shape[1] // split_size
        heads_here = width // HEAD_DIM

        table = jnp.asarray(table_np)
        own = table[me]

        kv_t = gather_blocks(jnp.concatenate([keys.T, values.T], axis=0))
        block_total = kv_t.shape[0]

        def held_at(block):
            coords = table[block]
            position = jnp.zeros_like(block)
            stride = 1
            for axis, size in stages:
                position = position + ((coords[..., axis] - own[axis]) % size) * stride
                stride *= size
            return position

        def my_heads(x):
            part = lax.dynamic_slice_in_dim(x, split_place * width, width, axis=1)
            return part.reshape(query_count, BLOCK * heads_here, HEAD_DIM)

        lists = block_lists.astype(jnp.int32)
        keep = first_occurrence(lists)
        o_rows, dq_rows, dk_blocks, dv_blocks = attend_local(
            my_heads(queries), my_heads(out_grad), kv_t, held_at(lists), keep)

        def join_halves(rows):
            mine = rows.reshape(token_rows, width)
            other = lax.ppermute(mine, "split", [(i, (i + 1) % split_size) for i in range(split_size)])
            return jnp.where(split_place == 0,
                             jnp.concatenate([mine, other], axis=1),
                             jnp.concatenate([other, mine], axis=1))

        attended = join_halves(o_rows)
        query_grad = join_halves(dq_rows)
        partial_kv = jnp.concatenate([dk_blocks, dv_blocks], axis=2)
        owned = scatter_sum(partial_kv, (BLOCK, 2 * HEAD_DIM))
        key_grad = (owned[:, :HEAD_DIM] * SCALE).astype(jnp.bfloat16)
        value_grad = owned[:, HEAD_DIM:].astype(jnp.bfloat16)
        return (attended, query_grad, key_grad, value_grad)

    return local


def solution(mesh):
    placed = (
        P("blk", None),
        P(("blk", "split"), None),
        P(("blk", "split"), None),
        P("blk", None),
        P("blk", None),
    )
    return jax.shard_map(
        make_local(mesh),
        mesh=mesh,
        in_specs=placed,
        out_specs=(
            P("blk", None),
            P("blk", None),
            P(("blk", "split"), None),
            P(("blk", "split"), None),
        ),
        check_vma=False,
    )
```

```python
import math

import jax
import numpy as np
import jax.numpy as jnp
from jax import lax
from jax.experimental import pallas as pl
from jax.experimental.pallas import tpu as pltpu
from jax.sharding import PartitionSpec as P

HEADS = 16
HEAD_DIM = 64
BLOCK = 128

SCALE = 1.0 / math.sqrt(HEAD_DIM)
LOWEST = -1e30
VMEM_LIMIT = 60 * 1024 * 1024


def _smem():
    return pl.BlockSpec(memory_space=pltpu.SMEM)


def _vmem():
    return pl.BlockSpec(memory_space=pltpu.VMEM)


def _nn(a, b):
    return jnp.dot(a, b, preferred_element_type=jnp.float32)


def _nt(a, b):
    return lax.dot_general(a, b, (((1,), (1,)), ((), ())), preferred_element_type=jnp.float32)


def _rows_of(kvt_ref, b, first):
    tile = kvt_ref[b, first:first + HEAD_DIM, :].astype(jnp.float32)
    return jnp.transpose(tile).astype(jnp.bfloat16)


def _forward_kernel(lists_ref, keep_ref, q_ref, kvt_ref, dot_ref,
                    ot_ref, lse_ref, delta_ref, m_sc, l_sc, acc_sc):
    query_count, slots = lists_ref.shape
    for qb in range(query_count):
        m_sc[...] = jnp.full(m_sc.shape, LOWEST, jnp.float32)
        l_sc[...] = jnp.zeros(l_sc.shape, jnp.float32)
        acc_sc[...] = jnp.zeros(acc_sc.shape, jnp.float32)

        def body(j, carry):
            @pl.when(keep_ref[qb, j] != 0)
            def _():
                b = lists_ref[qb, j]
                st = _nt(_rows_of(kvt_ref, b, 0), q_ref[qb]) * SCALE
                m_prev = m_sc[...]
                m_new = jnp.maximum(m_prev, jnp.max(st, axis=0, keepdims=True))
                alpha = jnp.exp(m_prev - m_new)
                pt = jnp.exp(st - m_new)
                l_sc[...] = alpha * l_sc[...] + jnp.sum(pt, axis=0, keepdims=True)
                acc_sc[...] = alpha * acc_sc[...] + _nn(
                    kvt_ref[b, HEAD_DIM:, :], pt.astype(jnp.bfloat16))
                m_sc[...] = m_new
            return carry

        lax.fori_loop(0, slots, body, 0)
        out = acc_sc[...] / l_sc[...]
        ot_ref[qb] = out.astype(jnp.bfloat16)
        lse_ref[qb] = m_sc[...] + jnp.log(l_sc[...])
        delta_ref[qb] = jnp.sum(dot_ref[qb].astype(jnp.float32) * out, axis=0, keepdims=True)


def _backward_kernel(lists_ref, keep_ref, q_ref, kvt_ref, do_ref, lse_ref, delta_ref,
                     dqt_ref, dkvt_ref, dq_sc):
    query_count, slots = lists_ref.shape
    dkvt_ref[...] = jnp.zeros(dkvt_ref.shape, jnp.float32)
    for qb in range(query_count):
        dq_sc[...] = jnp.zeros(dq_sc.shape, jnp.float32)

        def body(j, carry):
            @pl.when(keep_ref[qb, j] != 0)
            def _():
                b = lists_ref[qb, j]
                q = q_ref[qb]
                do = do_ref[qb]
                st = _nt(_rows_of(kvt_ref, b, 0), q) * SCALE
                pt = jnp.exp(st - lse_ref[qb])
                dkvt_ref[b, HEAD_DIM:, :] += jnp.transpose(_nn(pt.astype(jnp.bfloat16), do))
                dpt = _nt(_rows_of(kvt_ref, b, HEAD_DIM), do)
                dst = (pt * (dpt - delta_ref[qb])).astype(jnp.bfloat16)
                dq_sc[...] += _nn(kvt_ref[b, :HEAD_DIM, :], dst)
                dkvt_ref[b, :HEAD_DIM, :] += jnp.transpose(_nn(dst, q))
            return carry

        lax.fori_loop(0, slots, body, 0)
        dqt_ref[qb] = (dq_sc[...] * SCALE).astype(jnp.bfloat16)


def attend_local(q_rows, do_rows, kv_t, lists, keep):
    query_count, rows, _ = q_rows.shape
    block_total = kv_t.shape[0]
    f32 = jnp.float32
    do_t = jnp.swapaxes(do_rows, 1, 2)
    o_t, lse, delta = pl.pallas_call(
        _forward_kernel,
        out_shape=(
            jax.ShapeDtypeStruct((query_count, HEAD_DIM, rows), jnp.bfloat16),
            jax.ShapeDtypeStruct((query_count, 1, rows), f32),
            jax.ShapeDtypeStruct((query_count, 1, rows), f32),
        ),
        in_specs=[_smem(), _smem(), _vmem(), _vmem(), _vmem()],
        out_specs=(_vmem(), _vmem(), _vmem()),
        scratch_shapes=[
            pltpu.VMEM((1, rows), f32),
            pltpu.VMEM((1, rows), f32),
            pltpu.VMEM((HEAD_DIM, rows), f32),
        ],
        compiler_params=pltpu.CompilerParams(vmem_limit_bytes=VMEM_LIMIT),
    )(lists, keep, q_rows, kv_t, do_t)
    dq_t, dkv_t = pl.pallas_call(
        _backward_kernel,
        out_shape=(
            jax.ShapeDtypeStruct((query_count, HEAD_DIM, rows), jnp.bfloat16),
            jax.ShapeDtypeStruct((block_total, 2 * HEAD_DIM, BLOCK), f32),
        ),
        in_specs=[_smem(), _smem()] + [_vmem()] * 5,
        out_specs=(_vmem(), _vmem()),
        scratch_shapes=[pltpu.VMEM((HEAD_DIM, rows), f32)],
        compiler_params=pltpu.CompilerParams(vmem_limit_bytes=VMEM_LIMIT),
    )(lists, keep, q_rows, kv_t, do_rows, lse, delta)
    return jnp.swapaxes(o_t, 1, 2), jnp.swapaxes(dq_t, 1, 2), dkv_t


def first_occurrence(block_lists):
    slots = block_lists.shape[1]
    positions = jnp.arange(slots, dtype=jnp.int32)
    matches = block_lists[:, :, None] == block_lists[:, None, :]
    earlier = jnp.any(matches & (positions[None, None, :] < positions[None, :, None]), axis=2)
    return jnp.logical_not(earlier).astype(jnp.int32)


def device_table(mesh):
    flat = mesh.devices.reshape(-1)
    table = np.array([[*d.coords, d.core_on_chip] for d in flat], dtype=np.int32)
    sizes = table.max(axis=0) + 1
    stages = [(1, int(sizes[1])), (0, int(sizes[0])), (2, int(sizes[2])), (3, int(sizes[3]))]
    stages = [(axis, size) for axis, size in stages if size > 1]
    where = {tuple(row): index for index, row in enumerate(table.tolist())}

    def pairs(axis, shift):
        out = []
        for index, row in enumerate(table.tolist()):
            dest = list(row)
            dest[axis] = (row[axis] + shift) % int(sizes[axis])
            out.append((index, where[tuple(dest)]))
        return out

    return table, stages, pairs


def make_local(mesh):
    table_np, stages, pairs = device_table(mesh)
    axes = ("blk", "split")

    def gather_blocks(piece):
        buf = piece[None]
        for axis, size in stages:
            pieces = [buf]
            for shift in range(1, size):
                pieces.append(lax.ppermute(buf, axes, pairs(axis, size - shift)))
            buf = jnp.concatenate(pieces, axis=0)
        return buf

    def scatter_sum(part, piece_shape):
        part = part.reshape(tuple(size for _, size in reversed(stages)) + piece_shape)
        for axis, size in reversed(stages):
            total = part[0]
            for shift in range(1, size):
                sent = part[shift].astype(jnp.bfloat16)
                total = total + lax.ppermute(sent, axes, pairs(axis, shift)).astype(jnp.float32)
            part = total
        return part

    def local(queries, keys, values, out_grad, block_lists):
        query_count = block_lists.shape[0]
        token_rows = queries.shape[0]
        split_size = lax.axis_size("split")
        split_place = lax.axis_index("split")
        me = lax.axis_index("blk") * split_size + split_place
        width = queries.shape[1] // split_size
        heads_here = width // HEAD_DIM

        table = jnp.asarray(table_np)
        own = table[me]

        kv_t = gather_blocks(jnp.concatenate([keys.T, values.T], axis=0))
        block_total = kv_t.shape[0]

        def held_at(block):
            coords = table[block]
            position = jnp.zeros_like(block)
            stride = 1
            for axis, size in stages:
                position = position + ((coords[..., axis] - own[axis]) % size) * stride
                stride *= size
            return position

        def my_heads(x):
            part = lax.dynamic_slice_in_dim(x, split_place * width, width, axis=1)
            return part.reshape(query_count, BLOCK * heads_here, HEAD_DIM)

        lists = block_lists.astype(jnp.int32)
        keep = first_occurrence(lists)
        o_rows, dq_rows, dkv_t = attend_local(
            my_heads(queries), my_heads(out_grad), kv_t, held_at(lists), keep)

        def join_halves(rows):
            mine = rows.reshape(token_rows, width)
            other = lax.ppermute(mine, "split", [(i, (i + 1) % split_size) for i in range(split_size)])
            return jnp.where(split_place == 0,
                             jnp.concatenate([mine, other], axis=1),
                             jnp.concatenate([other, mine], axis=1))

        attended = join_halves(o_rows)
        query_grad = join_halves(dq_rows)
        owned = scatter_sum(dkv_t, (2 * HEAD_DIM, BLOCK))
        key_grad = (owned[:HEAD_DIM].T * SCALE).astype(jnp.bfloat16)
        value_grad = owned[HEAD_DIM:].T.astype(jnp.bfloat16)
        return (attended, query_grad, key_grad, value_grad)

    return local


def solution(mesh):
    placed = (
        P("blk", None),
        P(("blk", "split"), None),
        P(("blk", "split"), None),
        P("blk", None),
        P("blk", None),
    )
    return jax.shard_map(
        make_local(mesh),
        mesh=mesh,
        in_specs=placed,
        out_specs=(
            P("blk", None),
            P("blk", None),
            P(("blk", "split"), None),
            P(("blk", "split"), None),
        ),
        check_vma=False,
    )
```

```python
import math

import jax
import numpy as np
import jax.numpy as jnp
from jax import lax
from jax.experimental import pallas as pl
from jax.experimental.pallas import tpu as pltpu
from jax.sharding import PartitionSpec as P

HEADS = 16
HEAD_DIM = 64
BLOCK = 128

SCALE = 1.0 / math.sqrt(HEAD_DIM)
LOWEST = -1e30
VMEM_LIMIT = 60 * 1024 * 1024


def _smem():
    return pl.BlockSpec(memory_space=pltpu.SMEM)


def _vmem():
    return pl.BlockSpec(memory_space=pltpu.VMEM)


def _nn(a, b):
    return jnp.dot(a, b, preferred_element_type=jnp.float32)


def _nt(a, b):
    return lax.dot_general(a, b, (((1,), (1,)), ((), ())), preferred_element_type=jnp.float32)


def _rows_of(kvt_ref, b, first):
    tile = kvt_ref[b, first:first + HEAD_DIM, :].astype(jnp.float32)
    return jnp.transpose(tile).astype(jnp.bfloat16)


def _forward_kernel(lists_ref, keep_ref, qt_ref, kvt_ref, dot_ref,
                    ot_ref, lse_ref, delta_ref, m_sc, l_sc, acc_sc):
    query_count, slots = lists_ref.shape
    for qb in range(query_count):
        m_sc[...] = jnp.full(m_sc.shape, LOWEST, jnp.float32)
        l_sc[...] = jnp.zeros(l_sc.shape, jnp.float32)
        acc_sc[...] = jnp.zeros(acc_sc.shape, jnp.float32)

        def body(j, carry):
            @pl.when(keep_ref[qb, j] != 0)
            def _():
                b = lists_ref[qb, j]
                st = _nn(_rows_of(kvt_ref, b, 0), qt_ref[qb]) * SCALE
                m_prev = m_sc[...]
                m_new = jnp.maximum(m_prev, jnp.max(st, axis=0, keepdims=True))
                alpha = jnp.exp(m_prev - m_new)
                pt = jnp.exp(st - m_new)
                l_sc[...] = alpha * l_sc[...] + jnp.sum(pt, axis=0, keepdims=True)
                acc_sc[...] = alpha * acc_sc[...] + _nn(
                    kvt_ref[b, HEAD_DIM:, :], pt.astype(jnp.bfloat16))
                m_sc[...] = m_new
            return carry

        lax.fori_loop(0, slots, body, 0)
        out = acc_sc[...] / l_sc[...]
        ot_ref[qb] = out.astype(jnp.bfloat16)
        lse_ref[qb] = m_sc[...] + jnp.log(l_sc[...])
        delta_ref[qb] = jnp.sum(dot_ref[qb].astype(jnp.float32) * out, axis=0, keepdims=True)


def _backward_kernel(lists_ref, keep_ref, q_ref, qt_ref, kvt_ref, do_ref, dot_ref, lse_ref, delta_ref,
                     dqt_ref, dkvt_ref, dq_sc):
    query_count, slots = lists_ref.shape
    dkvt_ref[...] = jnp.zeros(dkvt_ref.shape, jnp.float32)
    for qb in range(query_count):
        dq_sc[...] = jnp.zeros(dq_sc.shape, jnp.float32)

        def body(j, carry):
            @pl.when(keep_ref[qb, j] != 0)
            def _():
                b = lists_ref[qb, j]
                q = q_ref[qb]
                do = do_ref[qb]
                st = _nn(_rows_of(kvt_ref, b, 0), qt_ref[qb]) * SCALE
                pt = jnp.exp(st - lse_ref[qb])
                dkvt_ref[b, HEAD_DIM:, :] += jnp.transpose(_nn(pt.astype(jnp.bfloat16), do))
                dpt = _nn(_rows_of(kvt_ref, b, HEAD_DIM), dot_ref[qb])
                dst = (pt * (dpt - delta_ref[qb])).astype(jnp.bfloat16)
                dq_sc[...] += _nn(kvt_ref[b, :HEAD_DIM, :], dst)
                dkvt_ref[b, :HEAD_DIM, :] += jnp.transpose(_nn(dst, q))
            return carry

        lax.fori_loop(0, slots, body, 0)
        dqt_ref[qb] = (dq_sc[...] * SCALE).astype(jnp.bfloat16)


def attend_local(q_rows, do_rows, kv_t, lists, keep):
    query_count, rows, _ = q_rows.shape
    block_total = kv_t.shape[0]
    f32 = jnp.float32
    do_t = jnp.swapaxes(do_rows, 1, 2)
    q_t = jnp.swapaxes(q_rows, 1, 2)
    o_t, lse, delta = pl.pallas_call(
        _forward_kernel,
        out_shape=(
            jax.ShapeDtypeStruct((query_count, HEAD_DIM, rows), jnp.bfloat16),
            jax.ShapeDtypeStruct((query_count, 1, rows), f32),
            jax.ShapeDtypeStruct((query_count, 1, rows), f32),
        ),
        in_specs=[_smem(), _smem(), _vmem(), _vmem(), _vmem()],
        out_specs=(_vmem(), _vmem(), _vmem()),
        scratch_shapes=[
            pltpu.VMEM((1, rows), f32),
            pltpu.VMEM((1, rows), f32),
            pltpu.VMEM((HEAD_DIM, rows), f32),
        ],
        compiler_params=pltpu.CompilerParams(vmem_limit_bytes=VMEM_LIMIT),
    )(lists, keep, q_t, kv_t, do_t)
    dq_t, dkv_t = pl.pallas_call(
        _backward_kernel,
        out_shape=(
            jax.ShapeDtypeStruct((query_count, HEAD_DIM, rows), jnp.bfloat16),
            jax.ShapeDtypeStruct((block_total, 2 * HEAD_DIM, BLOCK), f32),
        ),
        in_specs=[_smem(), _smem()] + [_vmem()] * 7,
        out_specs=(_vmem(), _vmem()),
        scratch_shapes=[pltpu.VMEM((HEAD_DIM, rows), f32)],
        compiler_params=pltpu.CompilerParams(vmem_limit_bytes=VMEM_LIMIT),
    )(lists, keep, q_rows, q_t, kv_t, do_rows, do_t, lse, delta)
    return jnp.swapaxes(o_t, 1, 2), jnp.swapaxes(dq_t, 1, 2), dkv_t


def first_occurrence(block_lists):
    slots = block_lists.shape[1]
    positions = jnp.arange(slots, dtype=jnp.int32)
    matches = block_lists[:, :, None] == block_lists[:, None, :]
    earlier = jnp.any(matches & (positions[None, None, :] < positions[None, :, None]), axis=2)
    return jnp.logical_not(earlier).astype(jnp.int32)


def device_table(mesh):
    flat = mesh.devices.reshape(-1)
    table = np.array([[*d.coords, d.core_on_chip] for d in flat], dtype=np.int32)
    sizes = table.max(axis=0) + 1
    stages = [(1, int(sizes[1])), (0, int(sizes[0])), (2, int(sizes[2])), (3, int(sizes[3]))]
    stages = [(axis, size) for axis, size in stages if size > 1]
    where = {tuple(row): index for index, row in enumerate(table.tolist())}

    def pairs(axis, shift):
        out = []
        for index, row in enumerate(table.tolist()):
            dest = list(row)
            dest[axis] = (row[axis] + shift) % int(sizes[axis])
            out.append((index, where[tuple(dest)]))
        return out

    return table, stages, pairs


def make_local(mesh):
    table_np, stages, pairs = device_table(mesh)
    axes = ("blk", "split")

    def gather_blocks(piece):
        buf = piece[None]
        for axis, size in stages:
            pieces = [buf]
            for shift in range(1, size):
                pieces.append(lax.ppermute(buf, axes, pairs(axis, size - shift)))
            buf = jnp.concatenate(pieces, axis=0)
        return buf

    def scatter_sum(part, piece_shape):
        part = part.reshape(tuple(size for _, size in reversed(stages)) + piece_shape)
        for axis, size in reversed(stages):
            total = part[0]
            for shift in range(1, size):
                sent = part[shift].astype(jnp.bfloat16)
                total = total + lax.ppermute(sent, axes, pairs(axis, shift)).astype(jnp.float32)
            part = total
        return part

    def local(queries, keys, values, out_grad, block_lists):
        query_count = block_lists.shape[0]
        token_rows = queries.shape[0]
        split_size = lax.axis_size("split")
        split_place = lax.axis_index("split")
        me = lax.axis_index("blk") * split_size + split_place
        width = queries.shape[1] // split_size
        heads_here = width // HEAD_DIM

        table = jnp.asarray(table_np)
        own = table[me]

        kv_t = gather_blocks(jnp.concatenate([keys.T, values.T], axis=0))
        block_total = kv_t.shape[0]

        def held_at(block):
            coords = table[block]
            position = jnp.zeros_like(block)
            stride = 1
            for axis, size in stages:
                position = position + ((coords[..., axis] - own[axis]) % size) * stride
                stride *= size
            return position

        def my_heads(x):
            part = lax.dynamic_slice_in_dim(x, split_place * width, width, axis=1)
            return part.reshape(query_count, BLOCK * heads_here, HEAD_DIM)

        lists = block_lists.astype(jnp.int32)
        keep = first_occurrence(lists)
        o_rows, dq_rows, dkv_t = attend_local(
            my_heads(queries), my_heads(out_grad), kv_t, held_at(lists), keep)

        def join_halves(rows):
            mine = rows.reshape(token_rows, width)
            other = lax.ppermute(mine, "split", [(i, (i + 1) % split_size) for i in range(split_size)])
            return jnp.where(split_place == 0,
                             jnp.concatenate([mine, other], axis=1),
                             jnp.concatenate([other, mine], axis=1))

        attended = join_halves(o_rows)
        query_grad = join_halves(dq_rows)
        owned = scatter_sum(dkv_t, (2 * HEAD_DIM, BLOCK))
        key_grad = (owned[:HEAD_DIM].T * SCALE).astype(jnp.bfloat16)
        value_grad = owned[HEAD_DIM:].T.astype(jnp.bfloat16)
        return (attended, query_grad, key_grad, value_grad)

    return local


def solution(mesh):
    placed = (
        P("blk", None),
        P(("blk", "split"), None),
        P(("blk", "split"), None),
        P("blk", None),
        P("blk", None),
    )
    return jax.shard_map(
        make_local(mesh),
        mesh=mesh,
        in_specs=placed,
        out_specs=(
            P("blk", None),
            P("blk", None),
            P(("blk", "split"), None),
            P(("blk", "split"), None),
        ),
        check_vma=False,
    )
```

```python
import math

import jax
import numpy as np
import jax.numpy as jnp
from jax import lax
from jax.experimental import pallas as pl
from jax.experimental.pallas import tpu as pltpu
from jax.sharding import PartitionSpec as P

HEADS = 16
HEAD_DIM = 64
BLOCK = 128

SCALE = 1.0 / math.sqrt(HEAD_DIM)
LOWEST = -1e30
VMEM_LIMIT = 60 * 1024 * 1024


def _smem():
    return pl.BlockSpec(memory_space=pltpu.SMEM)


def _vmem():
    return pl.BlockSpec(memory_space=pltpu.VMEM)


def _nn(a, b):
    return jnp.dot(a, b, preferred_element_type=jnp.float32)


def _nt(a, b):
    return lax.dot_general(a, b, (((1,), (1,)), ((), ())), preferred_element_type=jnp.float32)


def _rows_of(kvt_ref, b, first):
    tile = kvt_ref[b, first:first + HEAD_DIM, :].astype(jnp.float32)
    return jnp.transpose(tile).astype(jnp.bfloat16)


def _pair_rows(kvt_ref, blocks, first):
    return jnp.concatenate([_rows_of(kvt_ref, b, first) for b in blocks], axis=0)


def _pair_cols(kvt_ref, blocks, first):
    return jnp.concatenate([kvt_ref[b, first:first + HEAD_DIM, :] for b in blocks], axis=1)


def _visit_slots(count_ref, qb, visit):
    count = count_ref[qb, 0]
    pairs = count // 2

    def body(i, carry):
        @pl.when(i < pairs)
        def _():
            visit((2 * i, 2 * i + 1))
        return carry

    lax.fori_loop(0, count_ref.shape[1] // 2, body, 0)

    @pl.when(count % 2 == 1)
    def _():
        visit((count - 1,))


def _forward_kernel(lists_ref, count_ref, qt_ref, kvt_ref, dot_ref,
                    ot_ref, lse_ref, delta_ref, m_sc, l_sc, acc_sc):
    query_count = lists_ref.shape[0]
    for qb in range(query_count):
        m_sc[...] = jnp.full(m_sc.shape, LOWEST, jnp.float32)
        l_sc[...] = jnp.zeros(l_sc.shape, jnp.float32)
        acc_sc[...] = jnp.zeros(acc_sc.shape, jnp.float32)

        def visit(slots, qb=qb):
            blocks = [lists_ref[qb, j] for j in slots]
            st = _nn(_pair_rows(kvt_ref, blocks, 0), qt_ref[qb]) * SCALE
            m_prev = m_sc[...]
            m_new = jnp.maximum(m_prev, jnp.max(st, axis=0, keepdims=True))
            alpha = jnp.exp(m_prev - m_new)
            pt = jnp.exp(st - m_new)
            l_sc[...] = alpha * l_sc[...] + jnp.sum(pt, axis=0, keepdims=True)
            acc_sc[...] = alpha * acc_sc[...] + _nn(
                _pair_cols(kvt_ref, blocks, HEAD_DIM), pt.astype(jnp.bfloat16))
            m_sc[...] = m_new

        _visit_slots(count_ref, qb, visit)
        out = acc_sc[...] / l_sc[...]
        ot_ref[qb] = out.astype(jnp.bfloat16)
        lse_ref[qb] = m_sc[...] + jnp.log(l_sc[...])
        delta_ref[qb] = jnp.sum(dot_ref[qb].astype(jnp.float32) * out, axis=0, keepdims=True)


def _backward_kernel(lists_ref, count_ref, q_ref, qt_ref, kvt_ref, do_ref, dot_ref, lse_ref,
                     delta_ref, dqt_ref, dkvt_ref, dq_sc):
    query_count = lists_ref.shape[0]
    dkvt_ref[...] = jnp.zeros(dkvt_ref.shape, jnp.float32)
    for qb in range(query_count):
        dq_sc[...] = jnp.zeros(dq_sc.shape, jnp.float32)

        def visit(slots, qb=qb):
            blocks = [lists_ref[qb, j] for j in slots]
            st = _nn(_pair_rows(kvt_ref, blocks, 0), qt_ref[qb]) * SCALE
            pt = jnp.exp(st - lse_ref[qb])
            dvt = jnp.transpose(_nn(pt.astype(jnp.bfloat16), do_ref[qb]))
            dpt = _nn(_pair_rows(kvt_ref, blocks, HEAD_DIM), dot_ref[qb])
            dst = (pt * (dpt - delta_ref[qb])).astype(jnp.bfloat16)
            dq_sc[...] += _nn(_pair_cols(kvt_ref, blocks, 0), dst)
            dkt = jnp.transpose(_nn(dst, q_ref[qb]))
            for place, b in enumerate(blocks):
                cols = slice(place * BLOCK, (place + 1) * BLOCK)
                dkvt_ref[b, :HEAD_DIM, :] += dkt[:, cols]
                dkvt_ref[b, HEAD_DIM:, :] += dvt[:, cols]

        _visit_slots(count_ref, qb, visit)
        dqt_ref[qb] = (dq_sc[...] * SCALE).astype(jnp.bfloat16)


def attend_local(q_rows, do_rows, kv_t, lists, keep):
    order = jnp.argsort(1 - keep, axis=1, stable=True)
    lists = jnp.take_along_axis(lists, order, axis=1)
    keep = jnp.broadcast_to(jnp.sum(keep, axis=1, keepdims=True), lists.shape).astype(jnp.int32)
    query_count, rows, _ = q_rows.shape
    block_total = kv_t.shape[0]
    f32 = jnp.float32
    do_t = jnp.swapaxes(do_rows, 1, 2)
    q_t = jnp.swapaxes(q_rows, 1, 2)
    o_t, lse, delta = pl.pallas_call(
        _forward_kernel,
        out_shape=(
            jax.ShapeDtypeStruct((query_count, HEAD_DIM, rows), jnp.bfloat16),
            jax.ShapeDtypeStruct((query_count, 1, rows), f32),
            jax.ShapeDtypeStruct((query_count, 1, rows), f32),
        ),
        in_specs=[_smem(), _smem(), _vmem(), _vmem(), _vmem()],
        out_specs=(_vmem(), _vmem(), _vmem()),
        scratch_shapes=[
            pltpu.VMEM((1, rows), f32),
            pltpu.VMEM((1, rows), f32),
            pltpu.VMEM((HEAD_DIM, rows), f32),
        ],
        compiler_params=pltpu.CompilerParams(vmem_limit_bytes=VMEM_LIMIT),
    )(lists, keep, q_t, kv_t, do_t)
    dq_t, dkv_t = pl.pallas_call(
        _backward_kernel,
        out_shape=(
            jax.ShapeDtypeStruct((query_count, HEAD_DIM, rows), jnp.bfloat16),
            jax.ShapeDtypeStruct((block_total, 2 * HEAD_DIM, BLOCK), f32),
        ),
        in_specs=[_smem(), _smem()] + [_vmem()] * 7,
        out_specs=(_vmem(), _vmem()),
        scratch_shapes=[pltpu.VMEM((HEAD_DIM, rows), f32)],
        compiler_params=pltpu.CompilerParams(vmem_limit_bytes=VMEM_LIMIT),
    )(lists, keep, q_rows, q_t, kv_t, do_rows, do_t, lse, delta)
    return jnp.swapaxes(o_t, 1, 2), jnp.swapaxes(dq_t, 1, 2), dkv_t


def first_occurrence(block_lists):
    slots = block_lists.shape[1]
    positions = jnp.arange(slots, dtype=jnp.int32)
    matches = block_lists[:, :, None] == block_lists[:, None, :]
    earlier = jnp.any(matches & (positions[None, None, :] < positions[None, :, None]), axis=2)
    return jnp.logical_not(earlier).astype(jnp.int32)


def device_table(mesh):
    flat = mesh.devices.reshape(-1)
    table = np.array([[*d.coords, d.core_on_chip] for d in flat], dtype=np.int32)
    sizes = table.max(axis=0) + 1
    stages = [(1, int(sizes[1])), (0, int(sizes[0])), (2, int(sizes[2])), (3, int(sizes[3]))]
    stages = [(axis, size) for axis, size in stages if size > 1]
    where = {tuple(row): index for index, row in enumerate(table.tolist())}

    def pairs(axis, shift):
        out = []
        for index, row in enumerate(table.tolist()):
            dest = list(row)
            dest[axis] = (row[axis] + shift) % int(sizes[axis])
            out.append((index, where[tuple(dest)]))
        return out

    return table, stages, pairs


def make_local(mesh):
    table_np, stages, pairs = device_table(mesh)
    axes = ("blk", "split")

    def gather_blocks(piece):
        buf = piece[None]
        for axis, size in stages:
            pieces = [buf]
            for shift in range(1, size):
                pieces.append(lax.ppermute(buf, axes, pairs(axis, size - shift)))
            buf = jnp.concatenate(pieces, axis=0)
        return buf

    def scatter_sum(part, piece_shape):
        part = part.reshape(tuple(size for _, size in reversed(stages)) + piece_shape)
        for axis, size in reversed(stages):
            total = part[0]
            for shift in range(1, size):
                sent = part[shift].astype(jnp.bfloat16)
                total = total + lax.ppermute(sent, axes, pairs(axis, shift)).astype(jnp.float32)
            part = total
        return part

    def local(queries, keys, values, out_grad, block_lists):
        query_count = block_lists.shape[0]
        token_rows = queries.shape[0]
        split_size = lax.axis_size("split")
        split_place = lax.axis_index("split")
        me = lax.axis_index("blk") * split_size + split_place
        width = queries.shape[1] // split_size
        heads_here = width // HEAD_DIM

        table = jnp.asarray(table_np)
        own = table[me]

        kv_t = gather_blocks(jnp.concatenate([keys.T, values.T], axis=0))
        block_total = kv_t.shape[0]

        def held_at(block):
            coords = table[block]
            position = jnp.zeros_like(block)
            stride = 1
            for axis, size in stages:
                position = position + ((coords[..., axis] - own[axis]) % size) * stride
                stride *= size
            return position

        def my_heads(x):
            part = lax.dynamic_slice_in_dim(x, split_place * width, width, axis=1)
            return part.reshape(query_count, BLOCK * heads_here, HEAD_DIM)

        lists = block_lists.astype(jnp.int32)
        keep = first_occurrence(lists)
        o_rows, dq_rows, dkv_t = attend_local(
            my_heads(queries), my_heads(out_grad), kv_t, held_at(lists), keep)

        def join_halves(rows):
            mine = rows.reshape(token_rows, width)
            other = lax.ppermute(mine, "split", [(i, (i + 1) % split_size) for i in range(split_size)])
            return jnp.where(split_place == 0,
                             jnp.concatenate([mine, other], axis=1),
                             jnp.concatenate([other, mine], axis=1))

        attended = join_halves(o_rows)
        query_grad = join_halves(dq_rows)
        owned = scatter_sum(dkv_t, (2 * HEAD_DIM, BLOCK))
        key_grad = (owned[:HEAD_DIM].T * SCALE).astype(jnp.bfloat16)
        value_grad = owned[HEAD_DIM:].T.astype(jnp.bfloat16)
        return (attended, query_grad, key_grad, value_grad)

    return local


def solution(mesh):
    placed = (
        P("blk", None),
        P(("blk", "split"), None),
        P(("blk", "split"), None),
        P("blk", None),
        P("blk", None),
    )
    return jax.shard_map(
        make_local(mesh),
        mesh=mesh,
        in_specs=placed,
        out_specs=(
            P("blk", None),
            P("blk", None),
            P(("blk", "split"), None),
            P(("blk", "split"), None),
        ),
        check_vma=False,
    )
```

```python
import math

import jax
import numpy as np
import jax.numpy as jnp
from jax import lax
from jax.experimental import pallas as pl
from jax.experimental.pallas import tpu as pltpu
from jax.sharding import PartitionSpec as P

HEADS = 16
HEAD_DIM = 64
BLOCK = 128

SCALE = 1.0 / math.sqrt(HEAD_DIM)
LOWEST = -1e30
VMEM_LIMIT = 60 * 1024 * 1024


def _smem():
    return pl.BlockSpec(memory_space=pltpu.SMEM)


def _vmem():
    return pl.BlockSpec(memory_space=pltpu.VMEM)


def _nn(a, b):
    return jnp.dot(a, b, preferred_element_type=jnp.float32)


def _nt(a, b):
    return lax.dot_general(a, b, (((1,), (1,)), ((), ())), preferred_element_type=jnp.float32)


def _rows_of(kvt_ref, b, first):
    tile = kvt_ref[b, first:first + HEAD_DIM, :].astype(jnp.float32)
    return jnp.transpose(tile).astype(jnp.bfloat16)


def _pair_rows(kvt_ref, blocks, first):
    return jnp.concatenate([_rows_of(kvt_ref, b, first) for b in blocks], axis=0)


def _pair_cols(kvt_ref, blocks, first):
    return jnp.concatenate([kvt_ref[b, first:first + HEAD_DIM, :] for b in blocks], axis=1)


def _visit_slots(count_ref, qb, visit, group=4):
    count = count_ref[qb, 0]
    groups = count // group

    def body(i, carry):
        @pl.when(i < groups)
        def _():
            visit(tuple(group * i + t for t in range(group)))
        return carry

    lax.fori_loop(0, count_ref.shape[1] // group, body, 0)
    done = groups * group
    rest = count - done

    @pl.when(rest >= 2)
    def _():
        visit((done, done + 1))

    @pl.when(rest % 2 == 1)
    def _():
        visit((count - 1,))


def _forward_kernel(lists_ref, count_ref, qt_ref, kvt_ref, dot_ref,
                    ot_ref, lse_ref, delta_ref, m_sc, l_sc, acc_sc):
    query_count = lists_ref.shape[0]
    for qb in range(query_count):
        m_sc[...] = jnp.full(m_sc.shape, LOWEST, jnp.float32)
        l_sc[...] = jnp.zeros(l_sc.shape, jnp.float32)
        acc_sc[...] = jnp.zeros(acc_sc.shape, jnp.float32)

        def visit(slots, qb=qb):
            blocks = [lists_ref[qb, j] for j in slots]
            st = _nn(_pair_rows(kvt_ref, blocks, 0), qt_ref[qb]) * SCALE
            m_prev = m_sc[...]
            m_new = jnp.maximum(m_prev, jnp.max(st, axis=0, keepdims=True))
            alpha = jnp.exp(m_prev - m_new)
            pt = jnp.exp(st - m_new)
            l_sc[...] = alpha * l_sc[...] + jnp.sum(pt, axis=0, keepdims=True)
            acc_sc[...] = alpha * acc_sc[...] + _nn(
                _pair_cols(kvt_ref, blocks, HEAD_DIM), pt.astype(jnp.bfloat16))
            m_sc[...] = m_new

        _visit_slots(count_ref, qb, visit)
        out = acc_sc[...] / l_sc[...]
        ot_ref[qb] = out.astype(jnp.bfloat16)
        lse_ref[qb] = m_sc[...] + jnp.log(l_sc[...])
        delta_ref[qb] = jnp.sum(dot_ref[qb].astype(jnp.float32) * out, axis=0, keepdims=True)


def _backward_kernel(lists_ref, count_ref, q_ref, qt_ref, kvt_ref, do_ref, dot_ref, lse_ref,
                     delta_ref, dqt_ref, dkvt_ref, dq_sc):
    query_count = lists_ref.shape[0]
    dkvt_ref[...] = jnp.zeros(dkvt_ref.shape, jnp.float32)
    for qb in range(query_count):
        dq_sc[...] = jnp.zeros(dq_sc.shape, jnp.float32)

        def visit(slots, qb=qb):
            blocks = [lists_ref[qb, j] for j in slots]
            st = _nn(_pair_rows(kvt_ref, blocks, 0), qt_ref[qb]) * SCALE
            pt = jnp.exp(st - lse_ref[qb])
            dvt = jnp.transpose(_nn(pt.astype(jnp.bfloat16), do_ref[qb]))
            dpt = _nn(_pair_rows(kvt_ref, blocks, HEAD_DIM), dot_ref[qb])
            dst = (pt * (dpt - delta_ref[qb])).astype(jnp.bfloat16)
            dq_sc[...] += _nn(_pair_cols(kvt_ref, blocks, 0), dst)
            dkt = jnp.transpose(_nn(dst, q_ref[qb]))
            for place, b in enumerate(blocks):
                cols = slice(place * BLOCK, (place + 1) * BLOCK)
                dkvt_ref[b, :HEAD_DIM, :] += dkt[:, cols]
                dkvt_ref[b, HEAD_DIM:, :] += dvt[:, cols]

        _visit_slots(count_ref, qb, visit)
        dqt_ref[qb] = (dq_sc[...] * SCALE).astype(jnp.bfloat16)


def attend_local(q_rows, do_rows, kv_t, lists, keep):
    order = jnp.argsort(1 - keep, axis=1, stable=True)
    lists = jnp.take_along_axis(lists, order, axis=1)
    keep = jnp.broadcast_to(jnp.sum(keep, axis=1, keepdims=True), lists.shape).astype(jnp.int32)
    query_count, rows, _ = q_rows.shape
    block_total = kv_t.shape[0]
    f32 = jnp.float32
    do_t = jnp.swapaxes(do_rows, 1, 2)
    q_t = jnp.swapaxes(q_rows, 1, 2)
    o_t, lse, delta = pl.pallas_call(
        _forward_kernel,
        out_shape=(
            jax.ShapeDtypeStruct((query_count, HEAD_DIM, rows), jnp.bfloat16),
            jax.ShapeDtypeStruct((query_count, 1, rows), f32),
            jax.ShapeDtypeStruct((query_count, 1, rows), f32),
        ),
        in_specs=[_smem(), _smem(), _vmem(), _vmem(), _vmem()],
        out_specs=(_vmem(), _vmem(), _vmem()),
        scratch_shapes=[
            pltpu.VMEM((1, rows), f32),
            pltpu.VMEM((1, rows), f32),
            pltpu.VMEM((HEAD_DIM, rows), f32),
        ],
        compiler_params=pltpu.CompilerParams(vmem_limit_bytes=VMEM_LIMIT),
    )(lists, keep, q_t, kv_t, do_t)
    dq_t, dkv_t = pl.pallas_call(
        _backward_kernel,
        out_shape=(
            jax.ShapeDtypeStruct((query_count, HEAD_DIM, rows), jnp.bfloat16),
            jax.ShapeDtypeStruct((block_total, 2 * HEAD_DIM, BLOCK), f32),
        ),
        in_specs=[_smem(), _smem()] + [_vmem()] * 7,
        out_specs=(_vmem(), _vmem()),
        scratch_shapes=[pltpu.VMEM((HEAD_DIM, rows), f32)],
        compiler_params=pltpu.CompilerParams(vmem_limit_bytes=VMEM_LIMIT),
    )(lists, keep, q_rows, q_t, kv_t, do_rows, do_t, lse, delta)
    return jnp.swapaxes(o_t, 1, 2), jnp.swapaxes(dq_t, 1, 2), dkv_t


def first_occurrence(block_lists):
    slots = block_lists.shape[1]
    positions = jnp.arange(slots, dtype=jnp.int32)
    matches = block_lists[:, :, None] == block_lists[:, None, :]
    earlier = jnp.any(matches & (positions[None, None, :] < positions[None, :, None]), axis=2)
    return jnp.logical_not(earlier).astype(jnp.int32)


def device_table(mesh):
    flat = mesh.devices.reshape(-1)
    table = np.array([[*d.coords, d.core_on_chip] for d in flat], dtype=np.int32)
    sizes = table.max(axis=0) + 1
    stages = [(1, int(sizes[1])), (0, int(sizes[0])), (2, int(sizes[2])), (3, int(sizes[3]))]
    stages = [(axis, size) for axis, size in stages if size > 1]
    where = {tuple(row): index for index, row in enumerate(table.tolist())}

    def pairs(axis, shift):
        out = []
        for index, row in enumerate(table.tolist()):
            dest = list(row)
            dest[axis] = (row[axis] + shift) % int(sizes[axis])
            out.append((index, where[tuple(dest)]))
        return out

    return table, stages, pairs


def make_local(mesh):
    table_np, stages, pairs = device_table(mesh)
    axes = ("blk", "split")

    def gather_blocks(piece):
        buf = piece[None]
        for axis, size in stages:
            pieces = [buf]
            for shift in range(1, size):
                pieces.append(lax.ppermute(buf, axes, pairs(axis, size - shift)))
            buf = jnp.concatenate(pieces, axis=0)
        return buf

    def scatter_sum(part, piece_shape):
        part = part.reshape(tuple(size for _, size in reversed(stages)) + piece_shape)
        for axis, size in reversed(stages):
            total = part[0]
            for shift in range(1, size):
                sent = part[shift].astype(jnp.bfloat16)
                total = total + lax.ppermute(sent, axes, pairs(axis, shift)).astype(jnp.float32)
            part = total
        return part

    def local(queries, keys, values, out_grad, block_lists):
        query_count = block_lists.shape[0]
        token_rows = queries.shape[0]
        split_size = lax.axis_size("split")
        split_place = lax.axis_index("split")
        me = lax.axis_index("blk") * split_size + split_place
        width = queries.shape[1] // split_size
        heads_here = width // HEAD_DIM

        table = jnp.asarray(table_np)
        own = table[me]

        kv_t = gather_blocks(jnp.concatenate([keys.T, values.T], axis=0))
        block_total = kv_t.shape[0]

        def held_at(block):
            coords = table[block]
            position = jnp.zeros_like(block)
            stride = 1
            for axis, size in stages:
                position = position + ((coords[..., axis] - own[axis]) % size) * stride
                stride *= size
            return position

        def my_heads(x):
            part = lax.dynamic_slice_in_dim(x, split_place * width, width, axis=1)
            return part.reshape(query_count, BLOCK * heads_here, HEAD_DIM)

        lists = block_lists.astype(jnp.int32)
        keep = first_occurrence(lists)
        o_rows, dq_rows, dkv_t = attend_local(
            my_heads(queries), my_heads(out_grad), kv_t, held_at(lists), keep)

        def join_halves(rows):
            mine = rows.reshape(token_rows, width)
            other = lax.ppermute(mine, "split", [(i, (i + 1) % split_size) for i in range(split_size)])
            return jnp.where(split_place == 0,
                             jnp.concatenate([mine, other], axis=1),
                             jnp.concatenate([other, mine], axis=1))

        attended = join_halves(o_rows)
        query_grad = join_halves(dq_rows)
        owned = scatter_sum(dkv_t, (2 * HEAD_DIM, BLOCK))
        key_grad = (owned[:HEAD_DIM].T * SCALE).astype(jnp.bfloat16)
        value_grad = owned[HEAD_DIM:].T.astype(jnp.bfloat16)
        return (attended, query_grad, key_grad, value_grad)

    return local


def solution(mesh):
    placed = (
        P("blk", None),
        P(("blk", "split"), None),
        P(("blk", "split"), None),
        P("blk", None),
        P("blk", None),
    )
    return jax.shard_map(
        make_local(mesh),
        mesh=mesh,
        in_specs=placed,
        out_specs=(
            P("blk", None),
            P("blk", None),
            P(("blk", "split"), None),
            P(("blk", "split"), None),
        ),
        check_vma=False,
    )
```

```python
import math

import jax
import numpy as np
import jax.numpy as jnp
from jax import lax
from jax.experimental import pallas as pl
from jax.experimental.pallas import tpu as pltpu
from jax.sharding import PartitionSpec as P

HEADS = 16
HEAD_DIM = 64
BLOCK = 128

SCALE = 1.0 / math.sqrt(HEAD_DIM)
LOWEST = -1e30
VMEM_LIMIT = 60 * 1024 * 1024


def _smem():
    return pl.BlockSpec(memory_space=pltpu.SMEM)


def _vmem():
    return pl.BlockSpec(memory_space=pltpu.VMEM)


def _nn(a, b):
    return jnp.dot(a, b, preferred_element_type=jnp.float32)


def _nt(a, b):
    return lax.dot_general(a, b, (((1,), (1,)), ((), ())), preferred_element_type=jnp.float32)


def _rows_of(kvt_ref, b, first):
    tile = kvt_ref[b, first:first + HEAD_DIM, :].astype(jnp.float32)
    return jnp.transpose(tile).astype(jnp.bfloat16)


def _pair_rows(kvt_ref, blocks, first):
    return jnp.concatenate([_rows_of(kvt_ref, b, first) for b in blocks], axis=0)


def _pair_cols(kvt_ref, blocks, first):
    return jnp.concatenate([kvt_ref[b, first:first + HEAD_DIM, :] for b in blocks], axis=1)


def _visit_slots(count_ref, qb, visit, group=4):
    count = count_ref[qb, 0]
    groups = count // group

    def body(i, carry):
        @pl.when(i < groups)
        def _():
            visit(tuple(group * i + t for t in range(group)))
        return carry

    lax.fori_loop(0, count_ref.shape[1] // group, body, 0)
    done = groups * group
    rest = count - done

    @pl.when(rest >= 2)
    def _():
        visit((done, done + 1))

    @pl.when(rest % 2 == 1)
    def _():
        visit((count - 1,))


def _forward_kernel(lists_ref, count_ref, qt_ref, kvt_ref, dot_ref,
                    ot_ref, lse_ref, delta_ref, m_sc, l_sc, acc_sc):
    query_count = lists_ref.shape[0]
    def per_query(qb, carry):
        m_sc[...] = jnp.full(m_sc.shape, LOWEST, jnp.float32)
        l_sc[...] = jnp.zeros(l_sc.shape, jnp.float32)
        acc_sc[...] = jnp.zeros(acc_sc.shape, jnp.float32)

        def visit(slots, qb=qb):
            blocks = [lists_ref[qb, j] for j in slots]
            st = _nn(_pair_rows(kvt_ref, blocks, 0), qt_ref[qb]) * SCALE
            m_prev = m_sc[...]
            m_new = jnp.maximum(m_prev, jnp.max(st, axis=0, keepdims=True))
            alpha = jnp.exp(m_prev - m_new)
            pt = jnp.exp(st - m_new)
            l_sc[...] = alpha * l_sc[...] + jnp.sum(pt, axis=0, keepdims=True)
            acc_sc[...] = alpha * acc_sc[...] + _nn(
                _pair_cols(kvt_ref, blocks, HEAD_DIM), pt.astype(jnp.bfloat16))
            m_sc[...] = m_new

        _visit_slots(count_ref, qb, visit)
        out = acc_sc[...] / l_sc[...]
        ot_ref[qb] = out.astype(jnp.bfloat16)
        lse_ref[qb] = m_sc[...] + jnp.log(l_sc[...])
        delta_ref[qb] = jnp.sum(dot_ref[qb].astype(jnp.float32) * out, axis=0, keepdims=True)
        return carry

    lax.fori_loop(0, query_count, per_query, 0)


def _backward_kernel(lists_ref, count_ref, q_ref, qt_ref, kvt_ref, do_ref, dot_ref, lse_ref,
                     delta_ref, dqt_ref, dkvt_ref, dq_sc):
    query_count = lists_ref.shape[0]
    dkvt_ref[...] = jnp.zeros(dkvt_ref.shape, jnp.float32)
    def per_query(qb, carry):
        dq_sc[...] = jnp.zeros(dq_sc.shape, jnp.float32)

        def visit(slots, qb=qb):
            blocks = [lists_ref[qb, j] for j in slots]
            st = _nn(_pair_rows(kvt_ref, blocks, 0), qt_ref[qb]) * SCALE
            pt = jnp.exp(st - lse_ref[qb])
            dvt = jnp.transpose(_nn(pt.astype(jnp.bfloat16), do_ref[qb]))
            dpt = _nn(_pair_rows(kvt_ref, blocks, HEAD_DIM), dot_ref[qb])
            dst = (pt * (dpt - delta_ref[qb])).astype(jnp.bfloat16)
            dq_sc[...] += _nn(_pair_cols(kvt_ref, blocks, 0), dst)
            dkt = jnp.transpose(_nn(dst, q_ref[qb]))
            for place, b in enumerate(blocks):
                cols = slice(place * BLOCK, (place + 1) * BLOCK)
                dkvt_ref[b, :HEAD_DIM, :] += dkt[:, cols]
                dkvt_ref[b, HEAD_DIM:, :] += dvt[:, cols]

        _visit_slots(count_ref, qb, visit)
        dqt_ref[qb] = (dq_sc[...] * SCALE).astype(jnp.bfloat16)
        return carry

    lax.fori_loop(0, query_count, per_query, 0)


def attend_local(q_rows, do_rows, kv_t, lists, keep):
    order = jnp.argsort(1 - keep, axis=1, stable=True)
    lists = jnp.take_along_axis(lists, order, axis=1)
    keep = jnp.broadcast_to(jnp.sum(keep, axis=1, keepdims=True), lists.shape).astype(jnp.int32)
    query_count, rows, _ = q_rows.shape
    block_total = kv_t.shape[0]
    f32 = jnp.float32
    do_t = jnp.swapaxes(do_rows, 1, 2)
    q_t = jnp.swapaxes(q_rows, 1, 2)
    o_t, lse, delta = pl.pallas_call(
        _forward_kernel,
        out_shape=(
            jax.ShapeDtypeStruct((query_count, HEAD_DIM, rows), jnp.bfloat16),
            jax.ShapeDtypeStruct((query_count, 1, rows), f32),
            jax.ShapeDtypeStruct((query_count, 1, rows), f32),
        ),
        in_specs=[_smem(), _smem(), _vmem(), _vmem(), _vmem()],
        out_specs=(_vmem(), _vmem(), _vmem()),
        scratch_shapes=[
            pltpu.VMEM((1, rows), f32),
            pltpu.VMEM((1, rows), f32),
            pltpu.VMEM((HEAD_DIM, rows), f32),
        ],
        compiler_params=pltpu.CompilerParams(vmem_limit_bytes=VMEM_LIMIT),
    )(lists, keep, q_t, kv_t, do_t)
    dq_t, dkv_t = pl.pallas_call(
        _backward_kernel,
        out_shape=(
            jax.ShapeDtypeStruct((query_count, HEAD_DIM, rows), jnp.bfloat16),
            jax.ShapeDtypeStruct((block_total, 2 * HEAD_DIM, BLOCK), f32),
        ),
        in_specs=[_smem(), _smem()] + [_vmem()] * 7,
        out_specs=(_vmem(), _vmem()),
        scratch_shapes=[pltpu.VMEM((HEAD_DIM, rows), f32)],
        compiler_params=pltpu.CompilerParams(vmem_limit_bytes=VMEM_LIMIT),
    )(lists, keep, q_rows, q_t, kv_t, do_rows, do_t, lse, delta)
    return jnp.swapaxes(o_t, 1, 2), jnp.swapaxes(dq_t, 1, 2), dkv_t


def first_occurrence(block_lists):
    slots = block_lists.shape[1]
    positions = jnp.arange(slots, dtype=jnp.int32)
    matches = block_lists[:, :, None] == block_lists[:, None, :]
    earlier = jnp.any(matches & (positions[None, None, :] < positions[None, :, None]), axis=2)
    return jnp.logical_not(earlier).astype(jnp.int32)


def device_table(mesh):
    flat = mesh.devices.reshape(-1)
    table = np.array([[*d.coords, d.core_on_chip] for d in flat], dtype=np.int32)
    sizes = table.max(axis=0) + 1
    orders = [(1, 0, 2), (2, 1, 0), (0, 2, 1)]
    stage_sets = [[(axis, int(sizes[axis])) for axis in order + (3,) if sizes[axis] > 1]
                  for order in orders]
    where = {tuple(row): index for index, row in enumerate(table.tolist())}

    def pairs(axis, shift):
        out = []
        for index, row in enumerate(table.tolist()):
            dest = list(row)
            dest[axis] = (row[axis] + shift) % int(sizes[axis])
            out.append((index, where[tuple(dest)]))
        return out

    return table, stage_sets, pairs


CHUNK_ROWS = (48, 48, 32)


def make_local(mesh):
    table_np, stage_sets, pairs = device_table(mesh)
    stages = stage_sets[0]
    axes = ("blk", "split")

    def gather_blocks(piece, order):
        buf = piece[None]
        for axis, size in order:
            pieces = [buf]
            for shift in range(1, size):
                pieces.append(lax.ppermute(buf, axes, pairs(axis, size - shift)))
            buf = jnp.concatenate(pieces, axis=0)
        return buf

    def reorder(buf, order_from, order_to):
        dims_from = [axis for axis, _ in reversed(order_from)]
        dims_to = [axis for axis, _ in reversed(order_to)]
        if dims_from == dims_to:
            return buf
        sizes = [size for _, size in reversed(order_from)]
        inner = buf.shape[1:]
        held = buf.reshape(tuple(sizes) + inner)
        perm = [dims_from.index(axis) for axis in dims_to]
        perm += list(range(len(sizes), len(sizes) + len(inner)))
        return jnp.transpose(held, perm).reshape(buf.shape)

    def scatter_sum(part, order):
        piece_shape = part.shape[1:]
        part = part.reshape(tuple(size for _, size in reversed(order)) + piece_shape)
        for axis, size in reversed(order):
            total = part[0]
            for shift in range(1, size):
                sent = part[shift].astype(jnp.bfloat16)
                total = total + lax.ppermute(sent, axes, pairs(axis, shift)).astype(jnp.float32)
            part = total
        return part

    def chunk_bounds():
        first = 0
        for rows in CHUNK_ROWS:
            yield first, first + rows
            first += rows

    def gather_all(piece):
        held = []
        for (lo, hi), order in zip(chunk_bounds(), stage_sets):
            held.append(reorder(gather_blocks(piece[lo:hi], order), order, stages))
        return jnp.concatenate(held, axis=1)

    def scatter_all(part):
        owned = []
        for (lo, hi), order in zip(chunk_bounds(), stage_sets):
            owned.append(scatter_sum(reorder(part[:, lo:hi], stages, order), order))
        return jnp.concatenate(owned, axis=0)

    def local(queries, keys, values, out_grad, block_lists):
        query_count = block_lists.shape[0]
        token_rows = queries.shape[0]
        split_size = lax.axis_size("split")
        split_place = lax.axis_index("split")
        me = lax.axis_index("blk") * split_size + split_place
        width = queries.shape[1] // split_size
        heads_here = width // HEAD_DIM

        table = jnp.asarray(table_np)
        own = table[me]

        kv_t = gather_all(jnp.concatenate([keys.T, values.T], axis=0))
        block_total = kv_t.shape[0]

        def held_at(block):
            coords = table[block]
            position = jnp.zeros_like(block)
            stride = 1
            for axis, size in stages:
                position = position + ((coords[..., axis] - own[axis]) % size) * stride
                stride *= size
            return position

        def my_heads(x):
            part = lax.dynamic_slice_in_dim(x, split_place * width, width, axis=1)
            return part.reshape(query_count, BLOCK * heads_here, HEAD_DIM)

        lists = block_lists.astype(jnp.int32)
        keep = first_occurrence(lists)
        o_rows, dq_rows, dkv_t = attend_local(
            my_heads(queries), my_heads(out_grad), kv_t, held_at(lists), keep)

        def join_halves(rows):
            mine = rows.reshape(token_rows, width)
            other = lax.ppermute(mine, "split", [(i, (i + 1) % split_size) for i in range(split_size)])
            return jnp.where(split_place == 0,
                             jnp.concatenate([mine, other], axis=1),
                             jnp.concatenate([other, mine], axis=1))

        attended = join_halves(o_rows)
        query_grad = join_halves(dq_rows)
        owned = scatter_all(dkv_t)
        key_grad = (owned[:HEAD_DIM].T * SCALE).astype(jnp.bfloat16)
        value_grad = owned[HEAD_DIM:].T.astype(jnp.bfloat16)
        return (attended, query_grad, key_grad, value_grad)

    return local


def solution(mesh):
    placed = (
        P("blk", None),
        P(("blk", "split"), None),
        P(("blk", "split"), None),
        P("blk", None),
        P("blk", None),
    )
    return jax.shard_map(
        make_local(mesh),
        mesh=mesh,
        in_specs=placed,
        out_specs=(
            P("blk", None),
            P("blk", None),
            P(("blk", "split"), None),
            P(("blk", "split"), None),
        ),
        check_vma=False,
    )
```

```python
import math

import jax
import numpy as np
import jax.numpy as jnp
from jax import lax
from jax.experimental import pallas as pl
from jax.experimental.pallas import tpu as pltpu
from jax.sharding import PartitionSpec as P

HEADS = 16
HEAD_DIM = 64
BLOCK = 128

SCALE = 1.0 / math.sqrt(HEAD_DIM)
LOWEST = -1e30
VMEM_LIMIT = 60 * 1024 * 1024


def _smem():
    return pl.BlockSpec(memory_space=pltpu.SMEM)


def _vmem():
    return pl.BlockSpec(memory_space=pltpu.VMEM)


def _nn(a, b):
    return jnp.dot(a, b, preferred_element_type=jnp.float32)


def _nt(a, b):
    return lax.dot_general(a, b, (((1,), (1,)), ((), ())), preferred_element_type=jnp.float32)


def _rows_of(kvt_ref, b, first):
    tile = kvt_ref[b, first:first + HEAD_DIM, :].astype(jnp.float32)
    return jnp.transpose(tile).astype(jnp.bfloat16)


def _pair_rows(kvt_ref, blocks, first):
    return jnp.concatenate([_rows_of(kvt_ref, b, first) for b in blocks], axis=0)


def _pair_cols(kvt_ref, blocks, first):
    return jnp.concatenate([kvt_ref[b, first:first + HEAD_DIM, :] for b in blocks], axis=1)


def _visit_slots(count_ref, qb, visit, group=8):
    count = count_ref[qb, 0]
    groups = count // group

    def body(i, carry):
        @pl.when(i < groups)
        def _():
            visit(tuple(group * i + t for t in range(group)))
        return carry

    lax.fori_loop(0, count_ref.shape[1] // group, body, 0)
    done = groups * group
    size = group // 2
    while size >= 1:
        @pl.when((count - done) >= size)
        def _(done=done, size=size):
            visit(tuple(done + t for t in range(size)))
        done = done + jnp.where((count - done) >= size, size, 0)
        size //= 2


def _forward_kernel(lists_ref, count_ref, qt_ref, kvt_ref, dot_ref,
                    ot_ref, lse_ref, delta_ref, m_sc, l_sc, acc_sc):
    query_count = lists_ref.shape[0]
    def per_query(qb, carry):
        m_sc[...] = jnp.full(m_sc.shape, LOWEST, jnp.float32)
        l_sc[...] = jnp.zeros(l_sc.shape, jnp.float32)
        acc_sc[...] = jnp.zeros(acc_sc.shape, jnp.float32)

        def visit(slots, qb=qb):
            blocks = [lists_ref[qb, j] for j in slots]
            st = _nn(_pair_rows(kvt_ref, blocks, 0), qt_ref[qb]) * SCALE
            m_prev = m_sc[...]
            m_new = jnp.maximum(m_prev, jnp.max(st, axis=0, keepdims=True))
            alpha = jnp.exp(m_prev - m_new)
            pt = jnp.exp(st - m_new)
            l_sc[...] = alpha * l_sc[...] + jnp.sum(pt, axis=0, keepdims=True)
            acc_sc[...] = alpha * acc_sc[...] + _nn(
                _pair_cols(kvt_ref, blocks, HEAD_DIM), pt.astype(jnp.bfloat16))
            m_sc[...] = m_new

        _visit_slots(count_ref, qb, visit)
        out = acc_sc[...] / l_sc[...]
        ot_ref[qb] = out.astype(jnp.bfloat16)
        lse_ref[qb] = m_sc[...] + jnp.log(l_sc[...])
        delta_ref[qb] = jnp.sum(dot_ref[qb].astype(jnp.float32) * out, axis=0, keepdims=True)
        return carry

    lax.fori_loop(0, query_count, per_query, 0)


def _backward_kernel(lists_ref, count_ref, q_ref, qt_ref, kvt_ref, do_ref, dot_ref, lse_ref,
                     delta_ref, dqt_ref, dkvt_ref, dq_sc):
    query_count = lists_ref.shape[0]
    dkvt_ref[...] = jnp.zeros(dkvt_ref.shape, jnp.float32)
    def per_query(qb, carry):
        dq_sc[...] = jnp.zeros(dq_sc.shape, jnp.float32)

        def visit(slots, qb=qb):
            blocks = [lists_ref[qb, j] for j in slots]
            st = _nn(_pair_rows(kvt_ref, blocks, 0), qt_ref[qb]) * SCALE
            pt = jnp.exp(st - lse_ref[qb])
            dvt = jnp.transpose(_nn(pt.astype(jnp.bfloat16), do_ref[qb]))
            dpt = _nn(_pair_rows(kvt_ref, blocks, HEAD_DIM), dot_ref[qb])
            dst = (pt * (dpt - delta_ref[qb])).astype(jnp.bfloat16)
            dq_sc[...] += _nn(_pair_cols(kvt_ref, blocks, 0), dst)
            dkt = jnp.transpose(_nn(dst, q_ref[qb]))
            for place, b in enumerate(blocks):
                cols = slice(place * BLOCK, (place + 1) * BLOCK)
                dkvt_ref[b, :HEAD_DIM, :] += dkt[:, cols]
                dkvt_ref[b, HEAD_DIM:, :] += dvt[:, cols]

        _visit_slots(count_ref, qb, visit)
        dqt_ref[qb] = (dq_sc[...] * SCALE).astype(jnp.bfloat16)
        return carry

    lax.fori_loop(0, query_count, per_query, 0)


def attend_local(q_rows, do_rows, kv_t, lists, keep):
    order = jnp.argsort(1 - keep, axis=1, stable=True)
    lists = jnp.take_along_axis(lists, order, axis=1)
    keep = jnp.broadcast_to(jnp.sum(keep, axis=1, keepdims=True), lists.shape).astype(jnp.int32)
    query_count, rows, _ = q_rows.shape
    block_total = kv_t.shape[0]
    f32 = jnp.float32
    do_t = jnp.swapaxes(do_rows, 1, 2)
    q_t = jnp.swapaxes(q_rows, 1, 2)
    o_t, lse, delta = pl.pallas_call(
        _forward_kernel,
        out_shape=(
            jax.ShapeDtypeStruct((query_count, HEAD_DIM, rows), jnp.bfloat16),
            jax.ShapeDtypeStruct((query_count, 1, rows), f32),
            jax.ShapeDtypeStruct((query_count, 1, rows), f32),
        ),
        in_specs=[_smem(), _smem(), _vmem(), _vmem(), _vmem()],
        out_specs=(_vmem(), _vmem(), _vmem()),
        scratch_shapes=[
            pltpu.VMEM((1, rows), f32),
            pltpu.VMEM((1, rows), f32),
            pltpu.VMEM((HEAD_DIM, rows), f32),
        ],
        compiler_params=pltpu.CompilerParams(vmem_limit_bytes=VMEM_LIMIT),
    )(lists, keep, q_t, kv_t, do_t)
    dq_t, dkv_t = pl.pallas_call(
        _backward_kernel,
        out_shape=(
            jax.ShapeDtypeStruct((query_count, HEAD_DIM, rows), jnp.bfloat16),
            jax.ShapeDtypeStruct((block_total, 2 * HEAD_DIM, BLOCK), f32),
        ),
        in_specs=[_smem(), _smem()] + [_vmem()] * 7,
        out_specs=(_vmem(), _vmem()),
        scratch_shapes=[pltpu.VMEM((HEAD_DIM, rows), f32)],
        compiler_params=pltpu.CompilerParams(vmem_limit_bytes=VMEM_LIMIT),
    )(lists, keep, q_rows, q_t, kv_t, do_rows, do_t, lse, delta)
    return jnp.swapaxes(o_t, 1, 2), jnp.swapaxes(dq_t, 1, 2), dkv_t


def first_occurrence(block_lists):
    slots = block_lists.shape[1]
    positions = jnp.arange(slots, dtype=jnp.int32)
    matches = block_lists[:, :, None] == block_lists[:, None, :]
    earlier = jnp.any(matches & (positions[None, None, :] < positions[None, :, None]), axis=2)
    return jnp.logical_not(earlier).astype(jnp.int32)


def device_table(mesh):
    flat = mesh.devices.reshape(-1)
    table = np.array([[*d.coords, d.core_on_chip] for d in flat], dtype=np.int32)
    sizes = table.max(axis=0) + 1
    stages = [(1, int(sizes[1])), (0, int(sizes[0])), (2, int(sizes[2])), (3, int(sizes[3]))]
    stages = [(axis, size) for axis, size in stages if size > 1]
    where = {tuple(row): index for index, row in enumerate(table.tolist())}

    def pairs(axis, shift):
        out = []
        for index, row in enumerate(table.tolist()):
            dest = list(row)
            dest[axis] = (row[axis] + shift) % int(sizes[axis])
            out.append((index, where[tuple(dest)]))
        return out

    return table, stages, pairs


def make_local(mesh):
    table_np, stages, pairs = device_table(mesh)
    axes = ("blk", "split")

    def gather_blocks(piece):
        buf = piece[None]
        for axis, size in stages:
            pieces = [buf]
            for shift in range(1, size):
                pieces.append(lax.ppermute(buf, axes, pairs(axis, size - shift)))
            buf = jnp.concatenate(pieces, axis=0)
        return buf

    def scatter_sum(part, piece_shape):
        part = part.reshape(tuple(size for _, size in reversed(stages)) + piece_shape)
        for axis, size in reversed(stages):
            total = part[0]
            for shift in range(1, size):
                sent = part[shift].astype(jnp.bfloat16)
                total = total + lax.ppermute(sent, axes, pairs(axis, shift)).astype(jnp.float32)
            part = total
        return part

    def local(queries, keys, values, out_grad, block_lists):
        query_count = block_lists.shape[0]
        token_rows = queries.shape[0]
        split_size = lax.axis_size("split")
        split_place = lax.axis_index("split")
        me = lax.axis_index("blk") * split_size + split_place
        width = queries.shape[1] // split_size
        heads_here = width // HEAD_DIM

        table = jnp.asarray(table_np)
        own = table[me]

        kv_t = gather_blocks(jnp.concatenate([keys.T, values.T], axis=0))
        block_total = kv_t.shape[0]

        def held_at(block):
            coords = table[block]
            position = jnp.zeros_like(block)
            stride = 1
            for axis, size in stages:
                position = position + ((coords[..., axis] - own[axis]) % size) * stride
                stride *= size
            return position

        def my_heads(x):
            part = lax.dynamic_slice_in_dim(x, split_place * width, width, axis=1)
            return part.reshape(query_count, BLOCK * heads_here, HEAD_DIM)

        lists = block_lists.astype(jnp.int32)
        keep = first_occurrence(lists)
        o_rows, dq_rows, dkv_t = attend_local(
            my_heads(queries), my_heads(out_grad), kv_t, held_at(lists), keep)

        def join_halves(rows):
            mine = rows.reshape(token_rows, width)
            other = lax.ppermute(mine, "split", [(i, (i + 1) % split_size) for i in range(split_size)])
            return jnp.where(split_place == 0,
                             jnp.concatenate([mine, other], axis=1),
                             jnp.concatenate([other, mine], axis=1))

        attended = join_halves(o_rows)
        query_grad = join_halves(dq_rows)
        owned = scatter_sum(dkv_t, (2 * HEAD_DIM, BLOCK))
        key_grad = (owned[:HEAD_DIM].T * SCALE).astype(jnp.bfloat16)
        value_grad = owned[HEAD_DIM:].T.astype(jnp.bfloat16)
        return (attended, query_grad, key_grad, value_grad)

    return local


def solution(mesh):
    placed = (
        P("blk", None),
        P(("blk", "split"), None),
        P(("blk", "split"), None),
        P("blk", None),
        P("blk", None),
    )
    return jax.shard_map(
        make_local(mesh),
        mesh=mesh,
        in_specs=placed,
        out_specs=(
            P("blk", None),
            P("blk", None),
            P(("blk", "split"), None),
            P(("blk", "split"), None),
        ),
        check_vma=False,
    )
```

```python
import math

import jax
import numpy as np
import jax.numpy as jnp
from jax import lax
from jax.experimental import pallas as pl
from jax.experimental.pallas import tpu as pltpu
from jax.sharding import PartitionSpec as P

HEADS = 16
HEAD_DIM = 64
BLOCK = 128

SCALE = 1.0 / math.sqrt(HEAD_DIM)
LOWEST = -1e30
VMEM_LIMIT = 60 * 1024 * 1024


def _smem():
    return pl.BlockSpec(memory_space=pltpu.SMEM)


def _vmem():
    return pl.BlockSpec(memory_space=pltpu.VMEM)


def _nn(a, b):
    return jnp.dot(a, b, preferred_element_type=jnp.float32)


def _nt(a, b):
    return lax.dot_general(a, b, (((1,), (1,)), ((), ())), preferred_element_type=jnp.float32)


def _rows_of(kvt_ref, b, first):
    tile = kvt_ref[b, first:first + HEAD_DIM, :].astype(jnp.float32)
    return jnp.transpose(tile).astype(jnp.bfloat16)


def _pair_rows(kvt_ref, blocks, first):
    return jnp.concatenate([_rows_of(kvt_ref, b, first) for b in blocks], axis=0)


def _pair_cols(kvt_ref, blocks, first):
    return jnp.concatenate([kvt_ref[b, first:first + HEAD_DIM, :] for b in blocks], axis=1)


def _visit_slots(count_ref, qb, visit, group=8):
    count = count_ref[qb, 0]
    groups = count // group

    def body(i, carry):
        @pl.when(i < groups)
        def _():
            visit(tuple(group * i + t for t in range(group)))
        return carry

    lax.fori_loop(0, count_ref.shape[1] // group, body, 0)
    done = groups * group
    size = group // 2
    while size >= 1:
        @pl.when((count - done) >= size)
        def _(done=done, size=size):
            visit(tuple(done + t for t in range(size)))
        done = done + jnp.where((count - done) >= size, size, 0)
        size //= 2


def _forward_kernel(lists_ref, count_ref, qt_ref, kvt_ref, dot_ref,
                    ot_ref, lse_ref, delta_ref, m_sc, l_sc, acc_sc):
    query_count = lists_ref.shape[0]
    def per_query(qb, carry):
        m_sc[...] = jnp.full(m_sc.shape, LOWEST, jnp.float32)
        l_sc[...] = jnp.zeros(l_sc.shape, jnp.float32)
        acc_sc[...] = jnp.zeros(acc_sc.shape, jnp.float32)

        def visit(slots, qb=qb):
            blocks = [lists_ref[qb, j] for j in slots]
            st = _nn(_pair_rows(kvt_ref, blocks, 0), qt_ref[qb]) * SCALE
            m_prev = m_sc[...]
            m_new = jnp.maximum(m_prev, jnp.max(st, axis=0, keepdims=True))
            alpha = jnp.exp(m_prev - m_new)
            pt = jnp.exp(st - m_new)
            l_sc[...] = alpha * l_sc[...] + jnp.sum(pt, axis=0, keepdims=True)
            acc_sc[...] = alpha * acc_sc[...] + _nn(
                _pair_cols(kvt_ref, blocks, HEAD_DIM), pt.astype(jnp.bfloat16))
            m_sc[...] = m_new

        _visit_slots(count_ref, qb, visit)
        out = acc_sc[...] / l_sc[...]
        ot_ref[qb] = out.astype(jnp.bfloat16)
        lse_ref[qb] = m_sc[...] + jnp.log(l_sc[...])
        delta_ref[qb] = jnp.sum(dot_ref[qb].astype(jnp.float32) * out, axis=0, keepdims=True)
        return carry

    lax.fori_loop(0, query_count, per_query, 0)


def _backward_kernel(lists_ref, count_ref, q_ref, qt_ref, kvt_ref, do_ref, dot_ref, lse_ref,
                     delta_ref, dqt_ref, own_ref, send_ref, dq_sc, dkvt_ref):
    query_count = lists_ref.shape[0]
    dkvt_ref[...] = jnp.zeros(dkvt_ref.shape, jnp.float32)
    def per_query(qb, carry):
        dq_sc[...] = jnp.zeros(dq_sc.shape, jnp.float32)

        def visit(slots, qb=qb):
            blocks = [lists_ref[qb, j] for j in slots]
            st = _nn(_pair_rows(kvt_ref, blocks, 0), qt_ref[qb]) * SCALE
            pt = jnp.exp(st - lse_ref[qb])
            dvt = jnp.transpose(_nn(pt.astype(jnp.bfloat16), do_ref[qb]))
            dpt = _nn(_pair_rows(kvt_ref, blocks, HEAD_DIM), dot_ref[qb])
            dst = (pt * (dpt - delta_ref[qb])).astype(jnp.bfloat16)
            dq_sc[...] += _nn(_pair_cols(kvt_ref, blocks, 0), dst)
            dkt = jnp.transpose(_nn(dst, q_ref[qb]))
            for place, b in enumerate(blocks):
                cols = slice(place * BLOCK, (place + 1) * BLOCK)
                dkvt_ref[b, :HEAD_DIM, :] += dkt[:, cols]
                dkvt_ref[b, HEAD_DIM:, :] += dvt[:, cols]

        _visit_slots(count_ref, qb, visit)
        dqt_ref[qb] = (dq_sc[...] * SCALE).astype(jnp.bfloat16)
        return carry

    lax.fori_loop(0, query_count, per_query, 0)
    held = own_ref.shape[0]

    def hand_over(i, carry):
        own_ref[i] = dkvt_ref[i]
        for part in range(send_ref.shape[0]):
            send_ref[part, i] = dkvt_ref[(part + 1) * held + i].astype(jnp.bfloat16)
        return carry

    lax.fori_loop(0, held, hand_over, 0)


def attend_local(q_rows, do_rows, kv_t, lists, keep, outer):
    order = jnp.argsort(1 - keep, axis=1, stable=True)
    lists = jnp.take_along_axis(lists, order, axis=1)
    keep = jnp.broadcast_to(jnp.sum(keep, axis=1, keepdims=True), lists.shape).astype(jnp.int32)
    query_count, rows, _ = q_rows.shape
    block_total = kv_t.shape[0]
    f32 = jnp.float32
    do_t = jnp.swapaxes(do_rows, 1, 2)
    q_t = jnp.swapaxes(q_rows, 1, 2)
    o_t, lse, delta = pl.pallas_call(
        _forward_kernel,
        out_shape=(
            jax.ShapeDtypeStruct((query_count, HEAD_DIM, rows), jnp.bfloat16),
            jax.ShapeDtypeStruct((query_count, 1, rows), f32),
            jax.ShapeDtypeStruct((query_count, 1, rows), f32),
        ),
        in_specs=[_smem(), _smem(), _vmem(), _vmem(), _vmem()],
        out_specs=(_vmem(), _vmem(), _vmem()),
        scratch_shapes=[
            pltpu.VMEM((1, rows), f32),
            pltpu.VMEM((1, rows), f32),
            pltpu.VMEM((HEAD_DIM, rows), f32),
        ],
        compiler_params=pltpu.CompilerParams(vmem_limit_bytes=VMEM_LIMIT),
    )(lists, keep, q_t, kv_t, do_t)
    held = block_total // outer
    dq_t, own, send = pl.pallas_call(
        _backward_kernel,
        out_shape=(
            jax.ShapeDtypeStruct((query_count, HEAD_DIM, rows), jnp.bfloat16),
            jax.ShapeDtypeStruct((held, 2 * HEAD_DIM, BLOCK), f32),
            jax.ShapeDtypeStruct((outer - 1, held, 2 * HEAD_DIM, BLOCK), jnp.bfloat16),
        ),
        in_specs=[_smem(), _smem()] + [_vmem()] * 7,
        out_specs=(_vmem(), _vmem(), _vmem()),
        scratch_shapes=[
            pltpu.VMEM((HEAD_DIM, rows), f32),
            pltpu.VMEM((block_total, 2 * HEAD_DIM, BLOCK), f32),
        ],
        compiler_params=pltpu.CompilerParams(vmem_limit_bytes=VMEM_LIMIT),
    )(lists, keep, q_rows, q_t, kv_t, do_rows, do_t, lse, delta)
    return jnp.swapaxes(o_t, 1, 2), jnp.swapaxes(dq_t, 1, 2), (own, send)


def first_occurrence(block_lists):
    slots = block_lists.shape[1]
    positions = jnp.arange(slots, dtype=jnp.int32)
    matches = block_lists[:, :, None] == block_lists[:, None, :]
    earlier = jnp.any(matches & (positions[None, None, :] < positions[None, :, None]), axis=2)
    return jnp.logical_not(earlier).astype(jnp.int32)


def device_table(mesh):
    flat = mesh.devices.reshape(-1)
    table = np.array([[*d.coords, d.core_on_chip] for d in flat], dtype=np.int32)
    sizes = table.max(axis=0) + 1
    stages = [(1, int(sizes[1])), (0, int(sizes[0])), (2, int(sizes[2])), (3, int(sizes[3]))]
    stages = [(axis, size) for axis, size in stages if size > 1]
    where = {tuple(row): index for index, row in enumerate(table.tolist())}

    def pairs(axis, shift):
        out = []
        for index, row in enumerate(table.tolist()):
            dest = list(row)
            dest[axis] = (row[axis] + shift) % int(sizes[axis])
            out.append((index, where[tuple(dest)]))
        return out

    return table, stages, pairs


def make_local(mesh):
    table_np, stages, pairs = device_table(mesh)
    axes = ("blk", "split")

    def gather_blocks(piece):
        buf = piece[None]
        for axis, size in stages:
            pieces = [buf]
            for shift in range(1, size):
                pieces.append(lax.ppermute(buf, axes, pairs(axis, size - shift)))
            buf = jnp.concatenate(pieces, axis=0)
        return buf

    def scatter_sum(own, sent_first, piece_shape):
        later = list(reversed(stages))
        first_axis, first_size = later.pop(0)
        part = own
        for shift in range(1, first_size):
            part = part + lax.ppermute(
                sent_first[shift - 1], axes, pairs(first_axis, shift)).astype(jnp.float32)
        part = part.reshape(tuple(size for _, size in later) + piece_shape)
        for axis, size in later:
            total = part[0]
            for shift in range(1, size):
                sent = part[shift].astype(jnp.bfloat16)
                total = total + lax.ppermute(sent, axes, pairs(axis, shift)).astype(jnp.float32)
            part = total
        return part

    def local(queries, keys, values, out_grad, block_lists):
        query_count = block_lists.shape[0]
        token_rows = queries.shape[0]
        split_size = lax.axis_size("split")
        split_place = lax.axis_index("split")
        me = lax.axis_index("blk") * split_size + split_place
        width = queries.shape[1] // split_size
        heads_here = width // HEAD_DIM

        table = jnp.asarray(table_np)
        own = table[me]

        kv_t = gather_blocks(jnp.concatenate([keys.T, values.T], axis=0))
        block_total = kv_t.shape[0]

        def held_at(block):
            coords = table[block]
            position = jnp.zeros_like(block)
            stride = 1
            for axis, size in stages:
                position = position + ((coords[..., axis] - own[axis]) % size) * stride
                stride *= size
            return position

        def my_heads(x):
            part = lax.dynamic_slice_in_dim(x, split_place * width, width, axis=1)
            return part.reshape(query_count, BLOCK * heads_here, HEAD_DIM)

        lists = block_lists.astype(jnp.int32)
        keep = first_occurrence(lists)
        o_rows, dq_rows, dkv_t = attend_local(
            my_heads(queries), my_heads(out_grad), kv_t, held_at(lists), keep, stages[-1][1])

        def join_halves(rows):
            mine = rows.reshape(token_rows, width)
            other = lax.ppermute(mine, "split", [(i, (i + 1) % split_size) for i in range(split_size)])
            return jnp.where(split_place == 0,
                             jnp.concatenate([mine, other], axis=1),
                             jnp.concatenate([other, mine], axis=1))

        attended = join_halves(o_rows)
        query_grad = join_halves(dq_rows)
        owned = scatter_sum(*dkv_t, (2 * HEAD_DIM, BLOCK))
        key_grad = (owned[:HEAD_DIM].T * SCALE).astype(jnp.bfloat16)
        value_grad = owned[HEAD_DIM:].T.astype(jnp.bfloat16)
        return (attended, query_grad, key_grad, value_grad)

    return local


def solution(mesh):
    placed = (
        P("blk", None),
        P(("blk", "split"), None),
        P(("blk", "split"), None),
        P("blk", None),
        P("blk", None),
    )
    return jax.shard_map(
        make_local(mesh),
        mesh=mesh,
        in_specs=placed,
        out_specs=(
            P("blk", None),
            P("blk", None),
            P(("blk", "split"), None),
            P(("blk", "split"), None),
        ),
        check_vma=False,
    )
```

```python
import math

import jax
import numpy as np
import jax.numpy as jnp
from jax import lax
from jax.experimental import pallas as pl
from jax.experimental.pallas import tpu as pltpu
from jax.sharding import PartitionSpec as P

HEADS = 16
HEAD_DIM = 64
BLOCK = 128

SCALE = 1.0 / math.sqrt(HEAD_DIM)
LOWEST = -1e30
VMEM_LIMIT = 60 * 1024 * 1024


def _smem():
    return pl.BlockSpec(memory_space=pltpu.SMEM)


def _vmem():
    return pl.BlockSpec(memory_space=pltpu.VMEM)


def _nn(a, b):
    return jnp.dot(a, b, preferred_element_type=jnp.float32)


def _nt(a, b):
    return lax.dot_general(a, b, (((1,), (1,)), ((), ())), preferred_element_type=jnp.float32)


def _rows_of(kvt_ref, b, first):
    tile = kvt_ref[b, first:first + HEAD_DIM, :].astype(jnp.float32)
    return jnp.transpose(tile).astype(jnp.bfloat16)


def _pair_rows(kvt_ref, blocks, first):
    return jnp.concatenate([_rows_of(kvt_ref, b, first) for b in blocks], axis=0)


def _pair_cols(kvt_ref, blocks, first):
    return jnp.concatenate([kvt_ref[b, first:first + HEAD_DIM, :] for b in blocks], axis=1)


def _visit_slots(count_ref, qb, visit, group=8):
    count = count_ref[qb, 0]
    groups = count // group

    def body(i, carry):
        @pl.when(i < groups)
        def _():
            visit(tuple(group * i + t for t in range(group)))
        return carry

    lax.fori_loop(0, count_ref.shape[1] // group, body, 0)
    done = groups * group
    size = group // 2
    while size >= 1:
        @pl.when((count - done) >= size)
        def _(done=done, size=size):
            visit(tuple(done + t for t in range(size)))
        done = done + jnp.where((count - done) >= size, size, 0)
        size //= 2


def _forward_kernel(lists_ref, count_ref, qt_ref, kvt_ref, dot_ref,
                    ot_ref, lse_ref, delta_ref, m_sc, l_sc, acc_sc):
    query_count = lists_ref.shape[0]
    def per_query(qb, carry):
        m_sc[...] = jnp.full(m_sc.shape, LOWEST, jnp.float32)
        l_sc[...] = jnp.zeros(l_sc.shape, jnp.float32)
        acc_sc[...] = jnp.zeros(acc_sc.shape, jnp.float32)

        def visit(slots, qb=qb):
            blocks = [lists_ref[qb, j] for j in slots]
            st = _nn(_pair_rows(kvt_ref, blocks, 0), qt_ref[qb])
            m_prev = m_sc[...]
            m_new = jnp.maximum(m_prev, jnp.max(st, axis=0, keepdims=True))
            alpha = jnp.exp(m_prev - m_new)
            pt = jnp.exp(st - m_new)
            l_sc[...] = alpha * l_sc[...] + jnp.sum(pt, axis=0, keepdims=True)
            acc_sc[...] = alpha * acc_sc[...] + _nn(
                _pair_cols(kvt_ref, blocks, HEAD_DIM), pt.astype(jnp.bfloat16))
            m_sc[...] = m_new

        _visit_slots(count_ref, qb, visit)
        out = acc_sc[...] / l_sc[...]
        ot_ref[qb] = out.astype(jnp.bfloat16)
        lse_ref[qb] = m_sc[...] + jnp.log(l_sc[...])
        delta_ref[qb] = jnp.sum(dot_ref[qb].astype(jnp.float32) * out, axis=0, keepdims=True)
        return carry

    lax.fori_loop(0, query_count, per_query, 0)


def _backward_kernel(lists_ref, count_ref, q_ref, qt_ref, kvt_ref, do_ref, dot_ref, lse_ref,
                     delta_ref, dqt_ref, own_ref, send_ref, dq_sc, dkvt_ref):
    query_count = lists_ref.shape[0]
    dkvt_ref[...] = jnp.zeros(dkvt_ref.shape, jnp.float32)
    def per_query(qb, carry):
        dq_sc[...] = jnp.zeros(dq_sc.shape, jnp.float32)

        def visit(slots, qb=qb):
            blocks = [lists_ref[qb, j] for j in slots]
            st = _nn(_pair_rows(kvt_ref, blocks, 0), qt_ref[qb])
            pt = jnp.exp(st - lse_ref[qb])
            dvt = jnp.transpose(_nn(pt.astype(jnp.bfloat16), do_ref[qb]))
            dpt = _nn(_pair_rows(kvt_ref, blocks, HEAD_DIM), dot_ref[qb])
            dst = (pt * (dpt - delta_ref[qb])).astype(jnp.bfloat16)
            dq_sc[...] += _nn(_pair_cols(kvt_ref, blocks, 0), dst)
            dkt = jnp.transpose(_nn(dst, q_ref[qb]))
            for place, b in enumerate(blocks):
                cols = slice(place * BLOCK, (place + 1) * BLOCK)
                dkvt_ref[b, :HEAD_DIM, :] += dkt[:, cols]
                dkvt_ref[b, HEAD_DIM:, :] += dvt[:, cols]

        _visit_slots(count_ref, qb, visit)
        dqt_ref[qb] = (dq_sc[...] * SCALE).astype(jnp.bfloat16)
        return carry

    lax.fori_loop(0, query_count, per_query, 0)
    held = own_ref.shape[0]

    def hand_over(i, carry):
        own_ref[i] = dkvt_ref[i]
        for part in range(send_ref.shape[0]):
            send_ref[part, i] = dkvt_ref[(part + 1) * held + i].astype(jnp.bfloat16)
        return carry

    lax.fori_loop(0, held, hand_over, 0)


def attend_local(q_rows, do_rows, kv_t, lists, keep, outer):
    order = jnp.argsort(1 - keep, axis=1, stable=True)
    lists = jnp.take_along_axis(lists, order, axis=1)
    keep = jnp.broadcast_to(jnp.sum(keep, axis=1, keepdims=True), lists.shape).astype(jnp.int32)
    query_count, rows, _ = q_rows.shape
    block_total = kv_t.shape[0]
    f32 = jnp.float32
    do_t = jnp.swapaxes(do_rows, 1, 2)
    q_t = jnp.swapaxes(q_rows, 1, 2) * jnp.asarray(SCALE, q_rows.dtype)
    o_t, lse, delta = pl.pallas_call(
        _forward_kernel,
        out_shape=(
            jax.ShapeDtypeStruct((query_count, HEAD_DIM, rows), jnp.bfloat16),
            jax.ShapeDtypeStruct((query_count, 1, rows), f32),
            jax.ShapeDtypeStruct((query_count, 1, rows), f32),
        ),
        in_specs=[_smem(), _smem(), _vmem(), _vmem(), _vmem()],
        out_specs=(_vmem(), _vmem(), _vmem()),
        scratch_shapes=[
            pltpu.VMEM((1, rows), f32),
            pltpu.VMEM((1, rows), f32),
            pltpu.VMEM((HEAD_DIM, rows), f32),
        ],
        compiler_params=pltpu.CompilerParams(vmem_limit_bytes=VMEM_LIMIT),
    )(lists, keep, q_t, kv_t, do_t)
    held = block_total // outer
    dq_t, own, send = pl.pallas_call(
        _backward_kernel,
        out_shape=(
            jax.ShapeDtypeStruct((query_count, HEAD_DIM, rows), jnp.bfloat16),
            jax.ShapeDtypeStruct((held, 2 * HEAD_DIM, BLOCK), f32),
            jax.ShapeDtypeStruct((outer - 1, held, 2 * HEAD_DIM, BLOCK), jnp.bfloat16),
        ),
        in_specs=[_smem(), _smem()] + [_vmem()] * 7,
        out_specs=(_vmem(), _vmem(), _vmem()),
        scratch_shapes=[
            pltpu.VMEM((HEAD_DIM, rows), f32),
            pltpu.VMEM((block_total, 2 * HEAD_DIM, BLOCK), f32),
        ],
        compiler_params=pltpu.CompilerParams(vmem_limit_bytes=VMEM_LIMIT),
    )(lists, keep, q_rows, q_t, kv_t, do_rows, do_t, lse, delta)
    return jnp.swapaxes(o_t, 1, 2), jnp.swapaxes(dq_t, 1, 2), (own, send)


def first_occurrence(block_lists):
    slots = block_lists.shape[1]
    positions = jnp.arange(slots, dtype=jnp.int32)
    matches = block_lists[:, :, None] == block_lists[:, None, :]
    earlier = jnp.any(matches & (positions[None, None, :] < positions[None, :, None]), axis=2)
    return jnp.logical_not(earlier).astype(jnp.int32)


def device_table(mesh):
    flat = mesh.devices.reshape(-1)
    table = np.array([[*d.coords, d.core_on_chip] for d in flat], dtype=np.int32)
    sizes = table.max(axis=0) + 1
    stages = [(1, int(sizes[1])), (0, int(sizes[0])), (2, int(sizes[2])), (3, int(sizes[3]))]
    stages = [(axis, size) for axis, size in stages if size > 1]
    where = {tuple(row): index for index, row in enumerate(table.tolist())}

    def pairs(axis, shift):
        out = []
        for index, row in enumerate(table.tolist()):
            dest = list(row)
            dest[axis] = (row[axis] + shift) % int(sizes[axis])
            out.append((index, where[tuple(dest)]))
        return out

    return table, stages, pairs


def make_local(mesh):
    table_np, stages, pairs = device_table(mesh)
    axes = ("blk", "split")

    def gather_blocks(piece):
        buf = piece[None]
        for axis, size in stages:
            pieces = [buf]
            for shift in range(1, size):
                pieces.append(lax.ppermute(buf, axes, pairs(axis, size - shift)))
            buf = jnp.concatenate(pieces, axis=0)
        return buf

    def scatter_sum(own, sent_first, piece_shape):
        later = list(reversed(stages))
        first_axis, first_size = later.pop(0)
        part = own
        for shift in range(1, first_size):
            part = part + lax.ppermute(
                sent_first[shift - 1], axes, pairs(first_axis, shift)).astype(jnp.float32)
        part = part.reshape(tuple(size for _, size in later) + piece_shape)
        for axis, size in later:
            total = part[0]
            for shift in range(1, size):
                sent = part[shift].astype(jnp.bfloat16)
                total = total + lax.ppermute(sent, axes, pairs(axis, shift)).astype(jnp.float32)
            part = total
        return part

    def local(queries, keys, values, out_grad, block_lists):
        query_count = block_lists.shape[0]
        token_rows = queries.shape[0]
        split_size = lax.axis_size("split")
        split_place = lax.axis_index("split")
        me = lax.axis_index("blk") * split_size + split_place
        width = queries.shape[1] // split_size
        heads_here = width // HEAD_DIM

        table = jnp.asarray(table_np)
        own = table[me]

        kv_t = gather_blocks(jnp.concatenate([keys.T, values.T], axis=0))
        block_total = kv_t.shape[0]

        def held_at(block):
            coords = table[block]
            position = jnp.zeros_like(block)
            stride = 1
            for axis, size in stages:
                position = position + ((coords[..., axis] - own[axis]) % size) * stride
                stride *= size
            return position

        def my_heads(x):
            part = lax.dynamic_slice_in_dim(x, split_place * width, width, axis=1)
            return part.reshape(query_count, BLOCK * heads_here, HEAD_DIM)

        lists = block_lists.astype(jnp.int32)
        keep = first_occurrence(lists)
        o_rows, dq_rows, dkv_t = attend_local(
            my_heads(queries), my_heads(out_grad), kv_t, held_at(lists), keep, stages[-1][1])

        def join_halves(rows):
            mine = rows.reshape(token_rows, width)
            other = lax.ppermute(mine, "split", [(i, (i + 1) % split_size) for i in range(split_size)])
            return jnp.where(split_place == 0,
                             jnp.concatenate([mine, other], axis=1),
                             jnp.concatenate([other, mine], axis=1))

        attended = join_halves(o_rows)
        query_grad = join_halves(dq_rows)
        owned = scatter_sum(*dkv_t, (2 * HEAD_DIM, BLOCK))
        key_grad = (owned[:HEAD_DIM].T * SCALE).astype(jnp.bfloat16)
        value_grad = owned[HEAD_DIM:].T.astype(jnp.bfloat16)
        return (attended, query_grad, key_grad, value_grad)

    return local


def solution(mesh):
    placed = (
        P("blk", None),
        P(("blk", "split"), None),
        P(("blk", "split"), None),
        P("blk", None),
        P("blk", None),
    )
    return jax.shard_map(
        make_local(mesh),
        mesh=mesh,
        in_specs=placed,
        out_specs=(
            P("blk", None),
            P("blk", None),
            P(("blk", "split"), None),
            P(("blk", "split"), None),
        ),
        check_vma=False,
    )
```

```python
import math

import jax
import numpy as np
import jax.numpy as jnp
from jax import lax
from jax.experimental import pallas as pl
from jax.experimental.pallas import tpu as pltpu
from jax.sharding import PartitionSpec as P

HEADS = 16
HEAD_DIM = 64
BLOCK = 128

SCALE = 1.0 / math.sqrt(HEAD_DIM)
LOWEST = -1e30
VMEM_LIMIT = 60 * 1024 * 1024


def _smem():
    return pl.BlockSpec(memory_space=pltpu.SMEM)


def _vmem():
    return pl.BlockSpec(memory_space=pltpu.VMEM)


def _nn(a, b):
    return jnp.dot(a, b, preferred_element_type=jnp.float32)


def _nt(a, b):
    return lax.dot_general(a, b, (((1,), (1,)), ((), ())), preferred_element_type=jnp.float32)


def _rows_of(kvt_ref, b, first):
    tile = kvt_ref[b, first:first + HEAD_DIM, :].astype(jnp.float32)
    return jnp.transpose(tile).astype(jnp.bfloat16)


def _pair_rows(kvt_ref, blocks, first):
    return jnp.concatenate([_rows_of(kvt_ref, b, first) for b in blocks], axis=0)


def _pair_cols(kvt_ref, blocks, first):
    return jnp.concatenate([kvt_ref[b, first:first + HEAD_DIM, :] for b in blocks], axis=1)


def _visit_slots(count_ref, qb, visit, group=8):
    count = count_ref[qb, 0]
    groups = count // group

    def body(i, carry):
        @pl.when(i < groups)
        def _():
            visit(tuple(group * i + t for t in range(group)))
        return carry

    lax.fori_loop(0, count_ref.shape[1] // group, body, 0)
    done = groups * group
    size = group // 2
    while size >= 1:
        @pl.when((count - done) >= size)
        def _(done=done, size=size):
            visit(tuple(done + t for t in range(size)))
        done = done + jnp.where((count - done) >= size, size, 0)
        size //= 2


def _forward_kernel(lists_ref, count_ref, pos_ref, qt_ref, kvt_ref, dot_ref,
                    ot_ref, lse_ref, delta_ref, m_sc, l_sc, acc_sc):
    query_count = lists_ref.shape[0]
    def per_query(qb, carry):
        m_sc[...] = jnp.full(m_sc.shape, LOWEST, jnp.float32)
        l_sc[...] = jnp.zeros(l_sc.shape, jnp.float32)
        acc_sc[...] = jnp.zeros(acc_sc.shape, jnp.float32)

        def visit(slots, qb=qb):
            blocks = [pos_ref[lists_ref[qb, j]] for j in slots]
            st = _nn(_pair_rows(kvt_ref, blocks, 0), qt_ref[qb]) * SCALE
            m_prev = m_sc[...]
            m_new = jnp.maximum(m_prev, jnp.max(st, axis=0, keepdims=True))
            alpha = jnp.exp(m_prev - m_new)
            pt = jnp.exp(st - m_new)
            l_sc[...] = alpha * l_sc[...] + jnp.sum(pt, axis=0, keepdims=True)
            acc_sc[...] = alpha * acc_sc[...] + _nn(
                _pair_cols(kvt_ref, blocks, HEAD_DIM), pt.astype(jnp.bfloat16))
            m_sc[...] = m_new

        _visit_slots(count_ref, qb, visit)
        out = acc_sc[...] / l_sc[...]
        ot_ref[qb] = out.astype(jnp.bfloat16)
        lse_ref[qb] = m_sc[...] + jnp.log(l_sc[...])
        delta_ref[qb] = jnp.sum(dot_ref[qb].astype(jnp.float32) * out, axis=0, keepdims=True)
        return carry

    lax.fori_loop(0, query_count, per_query, 0)


def _backward_kernel(lists_ref, count_ref, pos_ref, q_ref, qt_ref, kvt_ref, do_ref, dot_ref, lse_ref,
                     delta_ref, dqt_ref, own_ref, send_ref, dq_sc, dkvt_ref):
    query_count = lists_ref.shape[0]
    dkvt_ref[...] = jnp.zeros(dkvt_ref.shape, jnp.float32)
    def per_query(qb, carry):
        dq_sc[...] = jnp.zeros(dq_sc.shape, jnp.float32)

        def visit(slots, qb=qb):
            blocks = [pos_ref[lists_ref[qb, j]] for j in slots]
            st = _nn(_pair_rows(kvt_ref, blocks, 0), qt_ref[qb]) * SCALE
            pt = jnp.exp(st - lse_ref[qb])
            dvt = jnp.transpose(_nn(pt.astype(jnp.bfloat16), do_ref[qb]))
            dpt = _nn(_pair_rows(kvt_ref, blocks, HEAD_DIM), dot_ref[qb])
            dst = (pt * (dpt - delta_ref[qb])).astype(jnp.bfloat16)
            dq_sc[...] += _nn(_pair_cols(kvt_ref, blocks, 0), dst)
            dkt = jnp.transpose(_nn(dst, q_ref[qb]))
            for place, b in enumerate(blocks):
                cols = slice(place * BLOCK, (place + 1) * BLOCK)
                dkvt_ref[b, :HEAD_DIM, :] += dkt[:, cols]
                dkvt_ref[b, HEAD_DIM:, :] += dvt[:, cols]

        _visit_slots(count_ref, qb, visit)
        dqt_ref[qb] = (dq_sc[...] * SCALE).astype(jnp.bfloat16)
        return carry

    lax.fori_loop(0, query_count, per_query, 0)
    held = own_ref.shape[0]

    def hand_over(i, carry):
        own_ref[i] = dkvt_ref[i]
        for part in range(send_ref.shape[0]):
            send_ref[part, i] = dkvt_ref[(part + 1) * held + i].astype(jnp.bfloat16)
        return carry

    lax.fori_loop(0, held, hand_over, 0)


def attend_local(q_rows, do_rows, kv_t, lists, keep, outer, positions):
    slots = lists.shape[1]
    rank = jnp.cumsum(keep, axis=1) - 1
    hit = (rank[:, :, None] == jnp.arange(slots, dtype=jnp.int32)[None, None, :]) & (keep[:, :, None] == 1)
    lists = jnp.sum(jnp.where(hit, lists[:, :, None], 0), axis=1).astype(jnp.int32)
    keep = jnp.broadcast_to(jnp.sum(keep, axis=1, keepdims=True), lists.shape).astype(jnp.int32)
    query_count, rows, _ = q_rows.shape
    block_total = kv_t.shape[0]
    f32 = jnp.float32
    do_t = jnp.swapaxes(do_rows, 1, 2)
    q_t = jnp.swapaxes(q_rows, 1, 2)
    o_t, lse, delta = pl.pallas_call(
        _forward_kernel,
        out_shape=(
            jax.ShapeDtypeStruct((query_count, HEAD_DIM, rows), jnp.bfloat16),
            jax.ShapeDtypeStruct((query_count, 1, rows), f32),
            jax.ShapeDtypeStruct((query_count, 1, rows), f32),
        ),
        in_specs=[_smem(), _smem(), _smem(), _vmem(), _vmem(), _vmem()],
        out_specs=(_vmem(), _vmem(), _vmem()),
        scratch_shapes=[
            pltpu.VMEM((1, rows), f32),
            pltpu.VMEM((1, rows), f32),
            pltpu.VMEM((HEAD_DIM, rows), f32),
        ],
        compiler_params=pltpu.CompilerParams(vmem_limit_bytes=VMEM_LIMIT),
    )(lists, keep, positions, q_t, kv_t, do_t)
    held = block_total // outer
    dq_t, own, send = pl.pallas_call(
        _backward_kernel,
        out_shape=(
            jax.ShapeDtypeStruct((query_count, HEAD_DIM, rows), jnp.bfloat16),
            jax.ShapeDtypeStruct((held, 2 * HEAD_DIM, BLOCK), f32),
            jax.ShapeDtypeStruct((outer - 1, held, 2 * HEAD_DIM, BLOCK), jnp.bfloat16),
        ),
        in_specs=[_smem(), _smem(), _smem()] + [_vmem()] * 7,
        out_specs=(_vmem(), _vmem(), _vmem()),
        scratch_shapes=[
            pltpu.VMEM((HEAD_DIM, rows), f32),
            pltpu.VMEM((block_total, 2 * HEAD_DIM, BLOCK), f32),
        ],
        compiler_params=pltpu.CompilerParams(vmem_limit_bytes=VMEM_LIMIT),
    )(lists, keep, positions, q_rows, q_t, kv_t, do_rows, do_t, lse, delta)
    return jnp.swapaxes(o_t, 1, 2), jnp.swapaxes(dq_t, 1, 2), (own, send)


def first_occurrence(block_lists):
    slots = block_lists.shape[1]
    positions = jnp.arange(slots, dtype=jnp.int32)
    matches = block_lists[:, :, None] == block_lists[:, None, :]
    earlier = jnp.any(matches & (positions[None, None, :] < positions[None, :, None]), axis=2)
    return jnp.logical_not(earlier).astype(jnp.int32)


def device_table(mesh):
    flat = mesh.devices.reshape(-1)
    table = np.array([[*d.coords, d.core_on_chip] for d in flat], dtype=np.int32)
    sizes = table.max(axis=0) + 1
    stages = [(1, int(sizes[1])), (0, int(sizes[0])), (2, int(sizes[2])), (3, int(sizes[3]))]
    stages = [(axis, size) for axis, size in stages if size > 1]
    where = {tuple(row): index for index, row in enumerate(table.tolist())}

    def pairs(axis, shift):
        out = []
        for index, row in enumerate(table.tolist()):
            dest = list(row)
            dest[axis] = (row[axis] + shift) % int(sizes[axis])
            out.append((index, where[tuple(dest)]))
        return out

    return table, stages, pairs


def make_local(mesh):
    table_np, stages, pairs = device_table(mesh)
    axes = ("blk", "split")

    def gather_blocks(piece):
        buf = piece[None]
        for axis, size in stages:
            pieces = [buf]
            for shift in range(1, size):
                pieces.append(lax.ppermute(buf, axes, pairs(axis, size - shift)))
            buf = jnp.concatenate(pieces, axis=0)
        return buf

    def scatter_sum(own, sent_first, piece_shape):
        later = list(reversed(stages))
        first_axis, first_size = later.pop(0)
        part = own
        for shift in range(1, first_size):
            part = part + lax.ppermute(
                sent_first[shift - 1], axes, pairs(first_axis, shift)).astype(jnp.float32)
        part = part.reshape(tuple(size for _, size in later) + piece_shape)
        for axis, size in later:
            total = part[0]
            for shift in range(1, size):
                sent = part[shift].astype(jnp.bfloat16)
                total = total + lax.ppermute(sent, axes, pairs(axis, shift)).astype(jnp.float32)
            part = total
        return part

    def local(queries, keys, values, out_grad, block_lists):
        query_count = block_lists.shape[0]
        token_rows = queries.shape[0]
        split_size = lax.axis_size("split")
        split_place = lax.axis_index("split")
        me = lax.axis_index("blk") * split_size + split_place
        width = queries.shape[1] // split_size
        heads_here = width // HEAD_DIM

        table = jnp.asarray(table_np)
        own = table[me]

        kv_t = gather_blocks(jnp.concatenate([keys.T, values.T], axis=0))
        block_total = kv_t.shape[0]

        def held_at(block):
            coords = table[block]
            position = jnp.zeros_like(block)
            stride = 1
            for axis, size in stages:
                position = position + ((coords[..., axis] - own[axis]) % size) * stride
                stride *= size
            return position

        def my_heads(x):
            part = lax.dynamic_slice_in_dim(x, split_place * width, width, axis=1)
            return part.reshape(query_count, BLOCK * heads_here, HEAD_DIM)

        lists = block_lists.astype(jnp.int32)
        keep = first_occurrence(lists)
        o_rows, dq_rows, dkv_t = attend_local(
            my_heads(queries), my_heads(out_grad), kv_t, lists, keep, stages[-1][1],
            held_at(jnp.arange(block_total, dtype=jnp.int32)))

        def join_halves(rows):
            mine = rows.reshape(token_rows, width)
            other = lax.ppermute(mine, "split", [(i, (i + 1) % split_size) for i in range(split_size)])
            return jnp.where(split_place == 0,
                             jnp.concatenate([mine, other], axis=1),
                             jnp.concatenate([other, mine], axis=1))

        attended = join_halves(o_rows)
        query_grad = join_halves(dq_rows)
        owned = scatter_sum(*dkv_t, (2 * HEAD_DIM, BLOCK))
        key_grad = (owned[:HEAD_DIM].T * SCALE).astype(jnp.bfloat16)
        value_grad = owned[HEAD_DIM:].T.astype(jnp.bfloat16)
        return (attended, query_grad, key_grad, value_grad)

    return local


def solution(mesh):
    placed = (
        P("blk", None),
        P(("blk", "split"), None),
        P(("blk", "split"), None),
        P("blk", None),
        P("blk", None),
    )
    return jax.shard_map(
        make_local(mesh),
        mesh=mesh,
        in_specs=placed,
        out_specs=(
            P("blk", None),
            P("blk", None),
            P(("blk", "split"), None),
            P(("blk", "split"), None),
        ),
        check_vma=False,
    )
```

```python
import math

import jax
import numpy as np
import jax.numpy as jnp
from jax import lax
from jax.experimental import pallas as pl
from jax.experimental.pallas import tpu as pltpu
from jax.sharding import PartitionSpec as P

HEADS = 16
HEAD_DIM = 64
BLOCK = 128

SCALE = 1.0 / math.sqrt(HEAD_DIM)
LOWEST = -1e30
VMEM_LIMIT = 60 * 1024 * 1024


def _smem():
    return pl.BlockSpec(memory_space=pltpu.SMEM)


def _vmem():
    return pl.BlockSpec(memory_space=pltpu.VMEM)


def _nn(a, b):
    return jnp.dot(a, b, preferred_element_type=jnp.float32)


def _nt(a, b):
    return lax.dot_general(a, b, (((1,), (1,)), ((), ())), preferred_element_type=jnp.float32)


def _rows_of(kvt_ref, b, first):
    tile = kvt_ref[b, first:first + HEAD_DIM, :].astype(jnp.float32)
    return jnp.transpose(tile).astype(jnp.bfloat16)


def _pair_rows(kvt_ref, blocks, first):
    return jnp.concatenate([_rows_of(kvt_ref, b, first) for b in blocks], axis=0)


def _pair_cols(kvt_ref, blocks, first):
    return jnp.concatenate([kvt_ref[b, first:first + HEAD_DIM, :] for b in blocks], axis=1)


def _visit_slots(count_ref, qb, visit, group=8):
    count = count_ref[qb, 0]
    groups = count // group

    def body(i, carry):
        @pl.when(i < groups)
        def _():
            visit(tuple(group * i + t for t in range(group)))
        return carry

    lax.fori_loop(0, count_ref.shape[1] // group, body, 0)
    done = groups * group
    size = group // 2
    while size >= 1:
        @pl.when((count - done) >= size)
        def _(done=done, size=size):
            visit(tuple(done + t for t in range(size)))
        done = done + jnp.where((count - done) >= size, size, 0)
        size //= 2


def _forward_kernel(lists_ref, count_ref, pos_ref, qt_ref, kvt_ref, dot_ref,
                    ot_ref, lse_ref, delta_ref, m_sc, l_sc, acc_sc):
    query_count = lists_ref.shape[0]
    def per_query(qb, carry):
        m_sc[...] = jnp.full(m_sc.shape, LOWEST, jnp.float32)
        l_sc[...] = jnp.zeros(l_sc.shape, jnp.float32)
        acc_sc[...] = jnp.zeros(acc_sc.shape, jnp.float32)

        def visit(slots, qb=qb):
            blocks = [pos_ref[lists_ref[qb, j]] for j in slots]
            st = _nn(_pair_rows(kvt_ref, blocks, 0), qt_ref[qb]) * SCALE
            m_prev = m_sc[...]
            m_new = jnp.maximum(m_prev, jnp.max(st, axis=0, keepdims=True))
            alpha = jnp.exp(m_prev - m_new)
            pt = jnp.exp(st - m_new)
            l_sc[...] = alpha * l_sc[...] + jnp.sum(pt, axis=0, keepdims=True)
            acc_sc[...] = alpha * acc_sc[...] + _nn(
                _pair_cols(kvt_ref, blocks, HEAD_DIM), pt.astype(jnp.bfloat16))
            m_sc[...] = m_new

        _visit_slots(count_ref, qb, visit)
        out = acc_sc[...] / l_sc[...]
        ot_ref[qb] = out.astype(jnp.bfloat16)
        lse_ref[qb] = m_sc[...] + jnp.log(l_sc[...])
        delta_ref[qb] = jnp.sum(dot_ref[qb].astype(jnp.float32) * out, axis=0, keepdims=True)
        return carry

    lax.fori_loop(0, query_count, per_query, 0)


def _backward_kernel(lists_ref, count_ref, pos_ref, q_ref, qt_ref, kvt_ref, do_ref, dot_ref, lse_ref,
                     delta_ref, dqt_ref, own_ref, send_ref, dq_sc, dkvt_ref):
    query_count = lists_ref.shape[0]
    dkvt_ref[...] = jnp.zeros(dkvt_ref.shape, jnp.float32)
    def per_query(qb, carry):
        dq_sc[...] = jnp.zeros(dq_sc.shape, jnp.float32)

        def visit(slots, qb=qb):
            blocks = [pos_ref[lists_ref[qb, j]] for j in slots]
            st = _nn(_pair_rows(kvt_ref, blocks, 0), qt_ref[qb]) * SCALE
            pt = jnp.exp(st - lse_ref[qb])
            dvt = jnp.transpose(_nn(pt.astype(jnp.bfloat16), do_ref[qb]))
            dpt = _nn(_pair_rows(kvt_ref, blocks, HEAD_DIM), dot_ref[qb])
            dst = (pt * (dpt - delta_ref[qb])).astype(jnp.bfloat16)
            dq_sc[...] += _nn(_pair_cols(kvt_ref, blocks, 0), dst)
            dkt = jnp.transpose(_nn(dst, q_ref[qb]))
            for place, b in enumerate(blocks):
                cols = slice(place * BLOCK, (place + 1) * BLOCK)
                dkvt_ref[b, :HEAD_DIM, :] += dkt[:, cols]
                dkvt_ref[b, HEAD_DIM:, :] += dvt[:, cols]

        _visit_slots(count_ref, qb, visit)
        dqt_ref[qb] = (dq_sc[...] * SCALE).astype(jnp.bfloat16)
        return carry

    lax.fori_loop(0, query_count, per_query, 0)
    held = own_ref.shape[0]

    def hand_over(i, carry):
        own_ref[i] = dkvt_ref[i]
        for part in range(send_ref.shape[0]):
            send_ref[part, i] = dkvt_ref[(part + 1) * held + i].astype(jnp.bfloat16)
        return carry

    lax.fori_loop(0, held, hand_over, 0)


def attend_local(q_rows, do_rows, kv_t, lists, keep, outer, positions):
    slots = lists.shape[1]
    rank = jnp.cumsum(keep, axis=1) - 1
    hit = (rank[:, :, None] == jnp.arange(slots, dtype=jnp.int32)[None, None, :]) & (keep[:, :, None] == 1)
    lists = jnp.sum(jnp.where(hit, lists[:, :, None], 0), axis=1).astype(jnp.int32)
    keep = jnp.broadcast_to(jnp.sum(keep, axis=1, keepdims=True), lists.shape).astype(jnp.int32)
    query_count, rows, _ = q_rows.shape
    block_total = kv_t.shape[0]
    f32 = jnp.float32
    do_t = jnp.swapaxes(do_rows, 1, 2)
    q_t = jnp.swapaxes(q_rows, 1, 2)
    o_t, lse, delta = pl.pallas_call(
        _forward_kernel,
        out_shape=(
            jax.ShapeDtypeStruct((query_count, HEAD_DIM, rows), jnp.bfloat16),
            jax.ShapeDtypeStruct((query_count, 1, rows), f32),
            jax.ShapeDtypeStruct((query_count, 1, rows), f32),
        ),
        in_specs=[_smem(), _smem(), _smem(), _vmem(), _vmem(), _vmem()],
        out_specs=(_vmem(), _vmem(), _vmem()),
        scratch_shapes=[
            pltpu.VMEM((1, rows), f32),
            pltpu.VMEM((1, rows), f32),
            pltpu.VMEM((HEAD_DIM, rows), f32),
        ],
        compiler_params=pltpu.CompilerParams(vmem_limit_bytes=VMEM_LIMIT),
    )(lists, keep, positions, q_t, kv_t, do_t)
    held = block_total // outer
    dq_t, own, send = pl.pallas_call(
        _backward_kernel,
        out_shape=(
            jax.ShapeDtypeStruct((query_count, HEAD_DIM, rows), jnp.bfloat16),
            jax.ShapeDtypeStruct((held, 2 * HEAD_DIM, BLOCK), f32),
            jax.ShapeDtypeStruct((outer - 1, held, 2 * HEAD_DIM, BLOCK), jnp.bfloat16),
        ),
        in_specs=[_smem(), _smem(), _smem()] + [_vmem()] * 7,
        out_specs=(_vmem(), _vmem(), _vmem()),
        scratch_shapes=[
            pltpu.VMEM((HEAD_DIM, rows), f32),
            pltpu.VMEM((block_total, 2 * HEAD_DIM, BLOCK), f32),
        ],
        compiler_params=pltpu.CompilerParams(vmem_limit_bytes=VMEM_LIMIT),
    )(lists, keep, positions, q_rows, q_t, kv_t, do_rows, do_t, lse, delta)
    return jnp.swapaxes(o_t, 1, 2), jnp.swapaxes(dq_t, 1, 2), (own, send)


def first_occurrence(block_lists):
    slots = block_lists.shape[1]
    positions = jnp.arange(slots, dtype=jnp.int32)
    matches = block_lists[:, :, None] == block_lists[:, None, :]
    earlier = jnp.any(matches & (positions[None, None, :] < positions[None, :, None]), axis=2)
    return jnp.logical_not(earlier).astype(jnp.int32)


def device_table(mesh):
    flat = mesh.devices.reshape(-1)
    table = np.array([[*d.coords, d.core_on_chip] for d in flat], dtype=np.int32)
    sizes = table.max(axis=0) + 1
    stages = [(1, int(sizes[1])), (0, int(sizes[0])), (2, int(sizes[2])), (3, int(sizes[3]))]
    stages = [(axis, size) for axis, size in stages if size > 1]
    where = {tuple(row): index for index, row in enumerate(table.tolist())}

    def pairs(axis, shift):
        out = []
        for index, row in enumerate(table.tolist()):
            dest = list(row)
            dest[axis] = (row[axis] + shift) % int(sizes[axis])
            out.append((index, where[tuple(dest)]))
        return out

    return table, stages, pairs


def make_local(mesh):
    table_np, stages, pairs = device_table(mesh)
    axes = ("blk", "split")

    held_np = np.zeros((table_np.shape[0], table_np.shape[0]), np.int32)
    stride = 1
    for axis, size in stages:
        held_np += ((table_np[None, :, axis] - table_np[:, None, axis]) % size) * stride
        stride *= size

    def gather_blocks(piece):
        buf = piece[None]
        for axis, size in stages:
            pieces = [buf]
            for shift in range(1, size):
                pieces.append(lax.ppermute(buf, axes, pairs(axis, size - shift)))
            buf = jnp.concatenate(pieces, axis=0)
        return buf

    def scatter_sum(own, sent_first, piece_shape):
        later = list(reversed(stages))
        first_axis, first_size = later.pop(0)
        part = own
        for shift in range(1, first_size):
            part = part + lax.ppermute(
                sent_first[shift - 1], axes, pairs(first_axis, shift)).astype(jnp.float32)
        part = part.reshape(tuple(size for _, size in later) + piece_shape)
        for axis, size in later:
            total = part[0]
            for shift in range(1, size):
                sent = part[shift].astype(jnp.bfloat16)
                total = total + lax.ppermute(sent, axes, pairs(axis, shift)).astype(jnp.float32)
            part = total
        return part

    def local(queries, keys, values, out_grad, block_lists):
        query_count = block_lists.shape[0]
        token_rows = queries.shape[0]
        split_size = lax.axis_size("split")
        split_place = lax.axis_index("split")
        me = lax.axis_index("blk") * split_size + split_place
        width = queries.shape[1] // split_size
        heads_here = width // HEAD_DIM

        table = jnp.asarray(table_np)
        own = table[me]

        kv_t = gather_blocks(jnp.concatenate([keys.T, values.T], axis=0))
        block_total = kv_t.shape[0]

        def held_at(block):
            coords = table[block]
            position = jnp.zeros_like(block)
            stride = 1
            for axis, size in stages:
                position = position + ((coords[..., axis] - own[axis]) % size) * stride
                stride *= size
            return position

        def my_heads(x):
            part = lax.dynamic_slice_in_dim(x, split_place * width, width, axis=1)
            return part.reshape(query_count, BLOCK * heads_here, HEAD_DIM)

        lists = block_lists.astype(jnp.int32)
        keep = first_occurrence(lists)
        o_rows, dq_rows, dkv_t = attend_local(
            my_heads(queries), my_heads(out_grad), kv_t, lists, keep, stages[-1][1],
            lax.dynamic_index_in_dim(jnp.asarray(held_np), me, keepdims=False))

        def join_halves(rows):
            mine = rows.reshape(token_rows, width)
            other = lax.ppermute(mine, "split", [(i, (i + 1) % split_size) for i in range(split_size)])
            return jnp.where(split_place == 0,
                             jnp.concatenate([mine, other], axis=1),
                             jnp.concatenate([other, mine], axis=1))

        attended = join_halves(o_rows)
        query_grad = join_halves(dq_rows)
        owned = scatter_sum(*dkv_t, (2 * HEAD_DIM, BLOCK))
        key_grad = (owned[:HEAD_DIM].T * SCALE).astype(jnp.bfloat16)
        value_grad = owned[HEAD_DIM:].T.astype(jnp.bfloat16)
        return (attended, query_grad, key_grad, value_grad)

    return local


def solution(mesh):
    placed = (
        P("blk", None),
        P(("blk", "split"), None),
        P(("blk", "split"), None),
        P("blk", None),
        P("blk", None),
    )
    return jax.shard_map(
        make_local(mesh),
        mesh=mesh,
        in_specs=placed,
        out_specs=(
            P("blk", None),
            P("blk", None),
            P(("blk", "split"), None),
            P(("blk", "split"), None),
        ),
        check_vma=False,
    )
```

```python
import math

import jax
import numpy as np
import jax.numpy as jnp
from jax import lax
from jax.experimental import pallas as pl
from jax.experimental.pallas import tpu as pltpu
from jax.sharding import PartitionSpec as P

HEADS = 16
HEAD_DIM = 64
BLOCK = 128

SCALE = 1.0 / math.sqrt(HEAD_DIM)
LOWEST = -1e30
VMEM_LIMIT = 60 * 1024 * 1024


def _smem():
    return pl.BlockSpec(memory_space=pltpu.SMEM)


def _vmem():
    return pl.BlockSpec(memory_space=pltpu.VMEM)


def _nn(a, b):
    return jnp.dot(a, b, preferred_element_type=jnp.float32)


def _nt(a, b):
    return lax.dot_general(a, b, (((1,), (1,)), ((), ())), preferred_element_type=jnp.float32)


def _rows_of(kvt_ref, b, first):
    tile = kvt_ref[b, first:first + HEAD_DIM, :].astype(jnp.float32)
    return jnp.transpose(tile).astype(jnp.bfloat16)


def _pair_rows(kvt_ref, blocks, first):
    return jnp.concatenate([_rows_of(kvt_ref, b, first) for b in blocks], axis=0)


def _pair_cols(kvt_ref, blocks, first):
    return jnp.concatenate([kvt_ref[b, first:first + HEAD_DIM, :] for b in blocks], axis=1)


def _visit_slots(count_ref, qb, visit, group=8):
    count = count_ref[qb, 0]
    groups = count // group

    def body(i, carry):
        @pl.when(i < groups)
        def _():
            visit(tuple(group * i + t for t in range(group)))
        return carry

    lax.fori_loop(0, count_ref.shape[1] // group, body, 0)
    done = groups * group
    size = group // 2
    while size >= 1:
        @pl.when((count - done) >= size)
        def _(done=done, size=size):
            visit(tuple(done + t for t in range(size)))
        done = done + jnp.where((count - done) >= size, size, 0)
        size //= 2


def _forward_kernel(lists_ref, count_ref, pos_ref, qt_ref, kvt_ref, dot_ref,
                    ot_ref, lse_ref, delta_ref, m_sc, l_sc, acc_sc):
    query_count = lists_ref.shape[0]
    def per_query(qb, carry):
        m_sc[...] = jnp.full(m_sc.shape, LOWEST, jnp.float32)
        l_sc[...] = jnp.zeros(l_sc.shape, jnp.float32)
        acc_sc[...] = jnp.zeros(acc_sc.shape, jnp.float32)

        def visit(slots, qb=qb):
            blocks = [pos_ref[lists_ref[qb, j]] for j in slots]
            st = _nn(_pair_rows(kvt_ref, blocks, 0), qt_ref[qb]) * SCALE
            m_prev = m_sc[...]
            m_new = jnp.maximum(m_prev, jnp.max(st, axis=0, keepdims=True))
            alpha = jnp.exp(m_prev - m_new)
            pt = jnp.exp(st - m_new)
            l_sc[...] = alpha * l_sc[...] + jnp.sum(pt, axis=0, keepdims=True)
            acc_sc[...] = alpha * acc_sc[...] + _nn(
                _pair_cols(kvt_ref, blocks, HEAD_DIM), pt.astype(jnp.bfloat16))
            m_sc[...] = m_new

        _visit_slots(count_ref, qb, visit)
        out = acc_sc[...] / l_sc[...]
        ot_ref[qb] = out.astype(jnp.bfloat16)
        lse_ref[qb] = m_sc[...] + jnp.log(l_sc[...])
        delta_ref[qb] = jnp.sum(dot_ref[qb].astype(jnp.float32) * out, axis=0, keepdims=True)
        return carry

    lax.fori_loop(0, query_count, per_query, 0)


def _backward_kernel(lists_ref, count_ref, pos_ref, q_ref, qt_ref, kvt_ref, do_ref, dot_ref, lse_ref,
                     delta_ref, dqt_ref, own_ref, send_ref, dq_sc, dkvt_ref):
    query_count = lists_ref.shape[0]
    dkvt_ref[...] = jnp.zeros(dkvt_ref.shape, jnp.float32)
    def per_query(qb, carry):
        dq_sc[...] = jnp.zeros(dq_sc.shape, jnp.float32)

        def visit(slots, qb=qb):
            blocks = [pos_ref[lists_ref[qb, j]] for j in slots]
            st = _nn(_pair_rows(kvt_ref, blocks, 0), qt_ref[qb]) * SCALE
            pt = jnp.exp(st - lse_ref[qb])
            dvt = jnp.transpose(_nn(pt.astype(jnp.bfloat16), do_ref[qb]))
            dpt = _nn(_pair_rows(kvt_ref, blocks, HEAD_DIM), dot_ref[qb])
            dst = (pt * (dpt - delta_ref[qb])).astype(jnp.bfloat16)
            dq_sc[...] += _nn(_pair_cols(kvt_ref, blocks, 0), dst)
            dkt = jnp.transpose(_nn(dst, q_ref[qb]))
            for place, b in enumerate(blocks):
                cols = slice(place * BLOCK, (place + 1) * BLOCK)
                dkvt_ref[b, :HEAD_DIM, :] += dkt[:, cols]
                dkvt_ref[b, HEAD_DIM:, :] += dvt[:, cols]

        _visit_slots(count_ref, qb, visit)
        dqt_ref[qb] = (dq_sc[...] * SCALE).astype(jnp.bfloat16)
        return carry

    lax.fori_loop(0, query_count, per_query, 0)
    held = own_ref.shape[0]

    def hand_over(i, carry):
        own_ref[i] = dkvt_ref[i]
        for part in range(send_ref.shape[0]):
            send_ref[part, i] = dkvt_ref[(part + 1) * held + i].astype(jnp.bfloat16)
        return carry

    lax.fori_loop(0, held, hand_over, 0)


def attend_local(q_rows, do_rows, kv_t, lists, keep, outer, positions):
    slots = lists.shape[1]
    rank = jnp.cumsum(keep, axis=1) - 1
    hit = (rank[:, :, None] == jnp.arange(slots, dtype=jnp.int32)[None, None, :]) & (keep[:, :, None] == 1)
    lists = jnp.sum(jnp.where(hit, lists[:, :, None], 0), axis=1).astype(jnp.int32)
    keep = jnp.broadcast_to(jnp.sum(keep, axis=1, keepdims=True), lists.shape).astype(jnp.int32)
    query_count, rows, _ = q_rows.shape
    block_total = kv_t.shape[0]
    f32 = jnp.float32
    do_t = jnp.swapaxes(do_rows, 1, 2)
    q_t = jnp.swapaxes(q_rows, 1, 2)
    o_t, lse, delta = pl.pallas_call(
        _forward_kernel,
        out_shape=(
            jax.ShapeDtypeStruct((query_count, HEAD_DIM, rows), jnp.bfloat16),
            jax.ShapeDtypeStruct((query_count, 1, rows), f32),
            jax.ShapeDtypeStruct((query_count, 1, rows), f32),
        ),
        in_specs=[_smem(), _smem(), _smem(), _vmem(), _vmem(), _vmem()],
        out_specs=(_vmem(), _vmem(), _vmem()),
        scratch_shapes=[
            pltpu.VMEM((1, rows), f32),
            pltpu.VMEM((1, rows), f32),
            pltpu.VMEM((HEAD_DIM, rows), f32),
        ],
        compiler_params=pltpu.CompilerParams(vmem_limit_bytes=VMEM_LIMIT),
    )(lists, keep, positions, q_t, kv_t, do_t)
    held = block_total // outer
    dq_t, own, send = pl.pallas_call(
        _backward_kernel,
        out_shape=(
            jax.ShapeDtypeStruct((query_count, HEAD_DIM, rows), jnp.bfloat16),
            jax.ShapeDtypeStruct((held, 2 * HEAD_DIM, BLOCK), f32),
            jax.ShapeDtypeStruct((outer - 1, held, 2 * HEAD_DIM, BLOCK), jnp.bfloat16),
        ),
        in_specs=[_smem(), _smem(), _smem()] + [_vmem()] * 7,
        out_specs=(_vmem(), _vmem(), _vmem()),
        scratch_shapes=[
            pltpu.VMEM((HEAD_DIM, rows), f32),
            pltpu.VMEM((block_total, 2 * HEAD_DIM, BLOCK), f32),
        ],
        compiler_params=pltpu.CompilerParams(vmem_limit_bytes=VMEM_LIMIT),
    )(lists, keep, positions, q_rows, q_t, kv_t, do_rows, do_t, lse, delta)
    return jnp.swapaxes(o_t, 1, 2), jnp.swapaxes(dq_t, 1, 2), (own, send)


def first_occurrence(block_lists):
    slots = block_lists.shape[1]
    positions = jnp.arange(slots, dtype=jnp.int32)
    matches = block_lists[:, :, None] == block_lists[:, None, :]
    earlier = jnp.any(matches & (positions[None, None, :] < positions[None, :, None]), axis=2)
    return jnp.logical_not(earlier).astype(jnp.int32)


def device_table(mesh):
    flat = mesh.devices.reshape(-1)
    table = np.array([[*d.coords, d.core_on_chip] for d in flat], dtype=np.int32)
    sizes = table.max(axis=0) + 1
    stages = [(1, int(sizes[1])), (0, int(sizes[0])), (2, int(sizes[2])), (3, int(sizes[3]))]
    stages = [(axis, size) for axis, size in stages if size > 1]
    where = {tuple(row): index for index, row in enumerate(table.tolist())}

    def pairs(axis, shift):
        out = []
        for index, row in enumerate(table.tolist()):
            dest = list(row)
            dest[axis] = (row[axis] + shift) % int(sizes[axis])
            out.append((index, where[tuple(dest)]))
        return out

    return table, stages, pairs


def make_local(mesh):
    table_np, stages, pairs = device_table(mesh)
    axes = ("blk", "split")

    held_np = np.zeros((table_np.shape[0], table_np.shape[0]), np.int32)
    stride = 1
    for axis, size in stages:
        held_np += ((table_np[None, :, axis] - table_np[:, None, axis]) % size) * stride
        stride *= size

    def gather_blocks(piece, tie=None):
        buf = piece[None]
        for number, (axis, size) in enumerate(stages):
            if number == 1 and tie is not None:
                buf, tie = lax.optimization_barrier((buf, tie))
            pieces = [buf]
            for shift in range(1, size):
                pieces.append(lax.ppermute(buf, axes, pairs(axis, size - shift)))
            buf = jnp.concatenate(pieces, axis=0)
        return buf, tie

    def scatter_sum(own, sent_first, piece_shape):
        later = list(reversed(stages))
        first_axis, first_size = later.pop(0)
        part = own
        for shift in range(1, first_size):
            part = part + lax.ppermute(
                sent_first[shift - 1], axes, pairs(first_axis, shift)).astype(jnp.float32)
        part = part.reshape(tuple(size for _, size in later) + piece_shape)
        for axis, size in later:
            total = part[0]
            for shift in range(1, size):
                sent = part[shift].astype(jnp.bfloat16)
                total = total + lax.ppermute(sent, axes, pairs(axis, shift)).astype(jnp.float32)
            part = total
        return part

    def local(queries, keys, values, out_grad, block_lists):
        query_count = block_lists.shape[0]
        token_rows = queries.shape[0]
        split_size = lax.axis_size("split")
        split_place = lax.axis_index("split")
        me = lax.axis_index("blk") * split_size + split_place
        width = queries.shape[1] // split_size
        heads_here = width // HEAD_DIM

        table = jnp.asarray(table_np)
        own = table[me]

        def my_heads(x):
            part = lax.dynamic_slice_in_dim(x, split_place * width, width, axis=1)
            return part.reshape(query_count, BLOCK * heads_here, HEAD_DIM)

        lists = block_lists.astype(jnp.int32)
        keep = first_occurrence(lists)
        prepared = (my_heads(queries), my_heads(out_grad), lists, keep,
                    lax.dynamic_index_in_dim(jnp.asarray(held_np), me, keepdims=False))
        kv_t, prepared = gather_blocks(jnp.concatenate([keys.T, values.T], axis=0), prepared)
        q_mine, do_mine, lists, keep, positions = prepared
        block_total = kv_t.shape[0]

        def held_at(block):
            coords = table[block]
            position = jnp.zeros_like(block)
            stride = 1
            for axis, size in stages:
                position = position + ((coords[..., axis] - own[axis]) % size) * stride
                stride *= size
            return position

        def my_heads(x):
            part = lax.dynamic_slice_in_dim(x, split_place * width, width, axis=1)
            return part.reshape(query_count, BLOCK * heads_here, HEAD_DIM)

        o_rows, dq_rows, dkv_t = attend_local(
            q_mine, do_mine, kv_t, lists, keep, stages[-1][1], positions)

        def join_halves(rows):
            mine = rows.reshape(token_rows, width)
            other = lax.ppermute(mine, "split", [(i, (i + 1) % split_size) for i in range(split_size)])
            return jnp.where(split_place == 0,
                             jnp.concatenate([mine, other], axis=1),
                             jnp.concatenate([other, mine], axis=1))

        attended = join_halves(o_rows)
        query_grad = join_halves(dq_rows)
        owned = scatter_sum(*dkv_t, (2 * HEAD_DIM, BLOCK))
        key_grad = (owned[:HEAD_DIM].T * SCALE).astype(jnp.bfloat16)
        value_grad = owned[HEAD_DIM:].T.astype(jnp.bfloat16)
        return (attended, query_grad, key_grad, value_grad)

    return local


def solution(mesh):
    placed = (
        P("blk", None),
        P(("blk", "split"), None),
        P(("blk", "split"), None),
        P("blk", None),
        P("blk", None),
    )
    return jax.shard_map(
        make_local(mesh),
        mesh=mesh,
        in_specs=placed,
        out_specs=(
            P("blk", None),
            P("blk", None),
            P(("blk", "split"), None),
            P(("blk", "split"), None),
        ),
        check_vma=False,
    )
```

```python
import math

import jax
import numpy as np
import jax.numpy as jnp
from jax import lax
from jax.experimental import pallas as pl
from jax.experimental.pallas import tpu as pltpu
from jax.sharding import PartitionSpec as P

HEADS = 16
HEAD_DIM = 64
BLOCK = 128

SCALE = 1.0 / math.sqrt(HEAD_DIM)
LOWEST = -1e30
VMEM_LIMIT = 60 * 1024 * 1024


def _smem():
    return pl.BlockSpec(memory_space=pltpu.SMEM)


def _vmem():
    return pl.BlockSpec(memory_space=pltpu.VMEM)


def _nn(a, b):
    return jnp.dot(a, b, preferred_element_type=jnp.float32)


def _nt(a, b):
    return lax.dot_general(a, b, (((1,), (1,)), ((), ())), preferred_element_type=jnp.float32)


def _rows_of(kvt_ref, b, first):
    tile = kvt_ref[b, first:first + HEAD_DIM, :].astype(jnp.float32)
    return jnp.transpose(tile).astype(jnp.bfloat16)


def _pair_rows(kvt_ref, blocks, first):
    return jnp.concatenate([_rows_of(kvt_ref, b, first) for b in blocks], axis=0)


def _pair_cols(kvt_ref, blocks, first):
    return jnp.concatenate([kvt_ref[b, first:first + HEAD_DIM, :] for b in blocks], axis=1)


def _visit_slots(count_ref, qb, visit, group=8):
    count = count_ref[qb, 0]
    groups = count // group

    def body(i, carry):
        @pl.when(i < groups)
        def _():
            visit(tuple(group * i + t for t in range(group)))
        return carry

    lax.fori_loop(0, count_ref.shape[1] // group, body, 0)
    done = groups * group
    size = group // 2
    while size >= 1:
        @pl.when((count - done) >= size)
        def _(done=done, size=size):
            visit(tuple(done + t for t in range(size)))
        done = done + jnp.where((count - done) >= size, size, 0)
        size //= 2


def _forward_kernel(lists_ref, count_ref, pos_ref, qt_ref, kvt_ref, dot_ref,
                    ot_ref, lse_ref, delta_ref, m_sc, l_sc, acc_sc):
    query_count = lists_ref.shape[0]
    def per_query(qb, carry):
        m_sc[...] = jnp.full(m_sc.shape, LOWEST, jnp.float32)
        l_sc[...] = jnp.zeros(l_sc.shape, jnp.float32)
        acc_sc[...] = jnp.zeros(acc_sc.shape, jnp.float32)

        def visit(slots, qb=qb):
            blocks = [pos_ref[lists_ref[qb, j]] for j in slots]
            st = _nn(_pair_rows(kvt_ref, blocks, 0), qt_ref[qb]) * SCALE
            m_prev = m_sc[...]
            m_new = jnp.maximum(m_prev, jnp.max(st, axis=0, keepdims=True))
            alpha = jnp.exp(m_prev - m_new)
            pt = jnp.exp(st - m_new)
            l_sc[...] = alpha * l_sc[...] + jnp.sum(pt, axis=0, keepdims=True)
            acc_sc[...] = alpha * acc_sc[...] + _nn(
                _pair_cols(kvt_ref, blocks, HEAD_DIM), pt.astype(jnp.bfloat16))
            m_sc[...] = m_new

        _visit_slots(count_ref, qb, visit, group=16)
        out = acc_sc[...] / l_sc[...]
        ot_ref[qb] = out.astype(jnp.bfloat16)
        lse_ref[qb] = m_sc[...] + jnp.log(l_sc[...])
        delta_ref[qb] = jnp.sum(dot_ref[qb].astype(jnp.float32) * out, axis=0, keepdims=True)
        return carry

    lax.fori_loop(0, query_count, per_query, 0)


def _backward_kernel(lists_ref, count_ref, pos_ref, q_ref, qt_ref, kvt_ref, do_ref, dot_ref, lse_ref,
                     delta_ref, dqt_ref, own_ref, send_ref, dq_sc, dkvt_ref):
    query_count = lists_ref.shape[0]
    dkvt_ref[...] = jnp.zeros(dkvt_ref.shape, jnp.float32)
    def per_query(qb, carry):
        dq_sc[...] = jnp.zeros(dq_sc.shape, jnp.float32)

        def visit(slots, qb=qb):
            blocks = [pos_ref[lists_ref[qb, j]] for j in slots]
            st = _nn(_pair_rows(kvt_ref, blocks, 0), qt_ref[qb]) * SCALE
            pt = jnp.exp(st - lse_ref[qb])
            dvt = jnp.transpose(_nn(pt.astype(jnp.bfloat16), do_ref[qb]))
            dpt = _nn(_pair_rows(kvt_ref, blocks, HEAD_DIM), dot_ref[qb])
            dst = (pt * (dpt - delta_ref[qb])).astype(jnp.bfloat16)
            dq_sc[...] += _nn(_pair_cols(kvt_ref, blocks, 0), dst)
            dkt = jnp.transpose(_nn(dst, q_ref[qb]))
            for place, b in enumerate(blocks):
                cols = slice(place * BLOCK, (place + 1) * BLOCK)
                dkvt_ref[b, :HEAD_DIM, :] += dkt[:, cols]
                dkvt_ref[b, HEAD_DIM:, :] += dvt[:, cols]

        _visit_slots(count_ref, qb, visit)
        dqt_ref[qb] = (dq_sc[...] * SCALE).astype(jnp.bfloat16)
        return carry

    lax.fori_loop(0, query_count, per_query, 0)
    held = own_ref.shape[0]

    def hand_over(i, carry):
        own_ref[i] = dkvt_ref[i]
        for part in range(send_ref.shape[0]):
            send_ref[part, i] = dkvt_ref[(part + 1) * held + i].astype(jnp.bfloat16)
        return carry

    lax.fori_loop(0, held, hand_over, 0)


def attend_local(q_rows, do_rows, kv_t, lists, keep, outer, positions):
    slots = lists.shape[1]
    rank = jnp.cumsum(keep, axis=1) - 1
    hit = (rank[:, :, None] == jnp.arange(slots, dtype=jnp.int32)[None, None, :]) & (keep[:, :, None] == 1)
    lists = jnp.sum(jnp.where(hit, lists[:, :, None], 0), axis=1).astype(jnp.int32)
    keep = jnp.broadcast_to(jnp.sum(keep, axis=1, keepdims=True), lists.shape).astype(jnp.int32)
    query_count, rows, _ = q_rows.shape
    block_total = kv_t.shape[0]
    f32 = jnp.float32
    do_t = jnp.swapaxes(do_rows, 1, 2)
    q_t = jnp.swapaxes(q_rows, 1, 2)
    o_t, lse, delta = pl.pallas_call(
        _forward_kernel,
        out_shape=(
            jax.ShapeDtypeStruct((query_count, HEAD_DIM, rows), jnp.bfloat16),
            jax.ShapeDtypeStruct((query_count, 1, rows), f32),
            jax.ShapeDtypeStruct((query_count, 1, rows), f32),
        ),
        in_specs=[_smem(), _smem(), _smem(), _vmem(), _vmem(), _vmem()],
        out_specs=(_vmem(), _vmem(), _vmem()),
        scratch_shapes=[
            pltpu.VMEM((1, rows), f32),
            pltpu.VMEM((1, rows), f32),
            pltpu.VMEM((HEAD_DIM, rows), f32),
        ],
        compiler_params=pltpu.CompilerParams(vmem_limit_bytes=VMEM_LIMIT),
    )(lists, keep, positions, q_t, kv_t, do_t)
    held = block_total // outer
    dq_t, own, send = pl.pallas_call(
        _backward_kernel,
        out_shape=(
            jax.ShapeDtypeStruct((query_count, HEAD_DIM, rows), jnp.bfloat16),
            jax.ShapeDtypeStruct((held, 2 * HEAD_DIM, BLOCK), f32),
            jax.ShapeDtypeStruct((outer - 1, held, 2 * HEAD_DIM, BLOCK), jnp.bfloat16),
        ),
        in_specs=[_smem(), _smem(), _smem()] + [_vmem()] * 7,
        out_specs=(_vmem(), _vmem(), _vmem()),
        scratch_shapes=[
            pltpu.VMEM((HEAD_DIM, rows), f32),
            pltpu.VMEM((block_total, 2 * HEAD_DIM, BLOCK), f32),
        ],
        compiler_params=pltpu.CompilerParams(vmem_limit_bytes=VMEM_LIMIT),
    )(lists, keep, positions, q_rows, q_t, kv_t, do_rows, do_t, lse, delta)
    return jnp.swapaxes(o_t, 1, 2), jnp.swapaxes(dq_t, 1, 2), (own, send)


def first_occurrence(block_lists):
    slots = block_lists.shape[1]
    positions = jnp.arange(slots, dtype=jnp.int32)
    matches = block_lists[:, :, None] == block_lists[:, None, :]
    earlier = jnp.any(matches & (positions[None, None, :] < positions[None, :, None]), axis=2)
    return jnp.logical_not(earlier).astype(jnp.int32)


def device_table(mesh):
    flat = mesh.devices.reshape(-1)
    table = np.array([[*d.coords, d.core_on_chip] for d in flat], dtype=np.int32)
    sizes = table.max(axis=0) + 1
    stages = [(1, int(sizes[1])), (0, int(sizes[0])), (2, int(sizes[2])), (3, int(sizes[3]))]
    stages = [(axis, size) for axis, size in stages if size > 1]
    where = {tuple(row): index for index, row in enumerate(table.tolist())}

    def pairs(axis, shift):
        out = []
        for index, row in enumerate(table.tolist()):
            dest = list(row)
            dest[axis] = (row[axis] + shift) % int(sizes[axis])
            out.append((index, where[tuple(dest)]))
        return out

    return table, stages, pairs


def make_local(mesh):
    table_np, stages, pairs = device_table(mesh)
    axes = ("blk", "split")

    held_np = np.zeros((table_np.shape[0], table_np.shape[0]), np.int32)
    stride = 1
    for axis, size in stages:
        held_np += ((table_np[None, :, axis] - table_np[:, None, axis]) % size) * stride
        stride *= size

    def gather_blocks(piece):
        buf = piece[None]
        for axis, size in stages:
            pieces = [buf]
            for shift in range(1, size):
                pieces.append(lax.ppermute(buf, axes, pairs(axis, size - shift)))
            buf = jnp.concatenate(pieces, axis=0)
        return buf

    def scatter_sum(own, sent_first, piece_shape):
        later = list(reversed(stages))
        first_axis, first_size = later.pop(0)
        part = own
        for shift in range(1, first_size):
            part = part + lax.ppermute(
                sent_first[shift - 1], axes, pairs(first_axis, shift)).astype(jnp.float32)
        part = part.reshape(tuple(size for _, size in later) + piece_shape)
        for axis, size in later:
            total = part[0]
            for shift in range(1, size):
                sent = part[shift].astype(jnp.bfloat16)
                total = total + lax.ppermute(sent, axes, pairs(axis, shift)).astype(jnp.float32)
            part = total
        return part

    def local(queries, keys, values, out_grad, block_lists):
        query_count = block_lists.shape[0]
        token_rows = queries.shape[0]
        split_size = lax.axis_size("split")
        split_place = lax.axis_index("split")
        me = lax.axis_index("blk") * split_size + split_place
        width = queries.shape[1] // split_size
        heads_here = width // HEAD_DIM

        table = jnp.asarray(table_np)
        own = table[me]

        kv_t = gather_blocks(jnp.concatenate([keys.T, values.T], axis=0))
        block_total = kv_t.shape[0]

        def held_at(block):
            coords = table[block]
            position = jnp.zeros_like(block)
            stride = 1
            for axis, size in stages:
                position = position + ((coords[..., axis] - own[axis]) % size) * stride
                stride *= size
            return position

        def my_heads(x):
            part = lax.dynamic_slice_in_dim(x, split_place * width, width, axis=1)
            return part.reshape(query_count, BLOCK * heads_here, HEAD_DIM)

        lists = block_lists.astype(jnp.int32)
        keep = first_occurrence(lists)
        o_rows, dq_rows, dkv_t = attend_local(
            my_heads(queries), my_heads(out_grad), kv_t, lists, keep, stages[-1][1],
            lax.dynamic_index_in_dim(jnp.asarray(held_np), me, keepdims=False))

        def join_halves(rows):
            mine = rows.reshape(token_rows, width)
            other = lax.ppermute(mine, "split", [(i, (i + 1) % split_size) for i in range(split_size)])
            return jnp.where(split_place == 0,
                             jnp.concatenate([mine, other], axis=1),
                             jnp.concatenate([other, mine], axis=1))

        attended = join_halves(o_rows)
        query_grad = join_halves(dq_rows)
        owned = scatter_sum(*dkv_t, (2 * HEAD_DIM, BLOCK))
        key_grad = (owned[:HEAD_DIM].T * SCALE).astype(jnp.bfloat16)
        value_grad = owned[HEAD_DIM:].T.astype(jnp.bfloat16)
        return (attended, query_grad, key_grad, value_grad)

    return local


def solution(mesh):
    placed = (
        P("blk", None),
        P(("blk", "split"), None),
        P(("blk", "split"), None),
        P("blk", None),
        P("blk", None),
    )
    return jax.shard_map(
        make_local(mesh),
        mesh=mesh,
        in_specs=placed,
        out_specs=(
            P("blk", None),
            P("blk", None),
            P(("blk", "split"), None),
            P(("blk", "split"), None),
        ),
        check_vma=False,
    )
```

```python
import math

import jax
import numpy as np
import jax.numpy as jnp
from jax import lax
from jax.experimental import pallas as pl
from jax.experimental.pallas import tpu as pltpu
from jax.sharding import PartitionSpec as P

HEADS = 16
HEAD_DIM = 64
BLOCK = 128

SCALE = 1.0 / math.sqrt(HEAD_DIM)
LOWEST = -1e30
VMEM_LIMIT = 60 * 1024 * 1024


def _smem():
    return pl.BlockSpec(memory_space=pltpu.SMEM)


def _vmem():
    return pl.BlockSpec(memory_space=pltpu.VMEM)


def _nn(a, b):
    return jnp.dot(a, b, preferred_element_type=jnp.float32)


def _nt(a, b):
    return lax.dot_general(a, b, (((1,), (1,)), ((), ())), preferred_element_type=jnp.float32)


def _rows_of(kvt_ref, b, first):
    tile = kvt_ref[b, first:first + HEAD_DIM, :].astype(jnp.float32)
    return jnp.transpose(tile).astype(jnp.bfloat16)


def _pair_rows(kvt_ref, blocks, first):
    return jnp.concatenate([_rows_of(kvt_ref, b, first) for b in blocks], axis=0)


def _pair_cols(kvt_ref, blocks, first):
    return jnp.concatenate([kvt_ref[b, first:first + HEAD_DIM, :] for b in blocks], axis=1)


def _visit_slots(count_ref, qb, visit, group=8):
    count = count_ref[qb, 0]
    groups = count // group

    def body(i, carry):
        @pl.when(i < groups)
        def _():
            visit(tuple(group * i + t for t in range(group)))
        return carry

    lax.fori_loop(0, count_ref.shape[1] // group, body, 0)
    done = groups * group
    size = group // 2
    while size >= 1:
        @pl.when((count - done) >= size)
        def _(done=done, size=size):
            visit(tuple(done + t for t in range(size)))
        done = done + jnp.where((count - done) >= size, size, 0)
        size //= 2


def _forward_kernel(lists_ref, count_ref, pos_ref, qt_ref, kvt_ref, dot_ref,
                    ot_ref, lse_ref, delta_ref, m_sc, l_sc, acc_sc):
    query_count = lists_ref.shape[0]
    def per_query(qb, carry):
        m_sc[...] = jnp.full(m_sc.shape, LOWEST, jnp.float32)
        l_sc[...] = jnp.zeros(l_sc.shape, jnp.float32)
        acc_sc[...] = jnp.zeros(acc_sc.shape, jnp.float32)

        def visit(slots, qb=qb):
            blocks = [pos_ref[lists_ref[qb, j]] for j in slots]
            st = _nn(_pair_rows(kvt_ref, blocks, 0), qt_ref[qb]) * SCALE
            m_prev = m_sc[...]
            m_new = jnp.maximum(m_prev, jnp.max(st, axis=0, keepdims=True))
            alpha = jnp.exp(m_prev - m_new)
            pt = jnp.exp(st - m_new)
            l_sc[...] = alpha * l_sc[...] + jnp.sum(pt, axis=0, keepdims=True)
            acc_sc[...] = alpha * acc_sc[...] + _nn(
                _pair_cols(kvt_ref, blocks, HEAD_DIM), pt.astype(jnp.bfloat16))
            m_sc[...] = m_new

        _visit_slots(count_ref, qb, visit, group=16)
        out = acc_sc[...] / l_sc[...]
        ot_ref[qb] = out.astype(jnp.bfloat16)
        lse_ref[qb] = m_sc[...] + jnp.log(l_sc[...])
        delta_ref[qb] = jnp.sum(dot_ref[qb].astype(jnp.float32) * out, axis=0, keepdims=True)
        return carry

    lax.fori_loop(0, query_count, per_query, 0)


def _backward_kernel(lists_ref, count_ref, pos_ref, q_ref, qt_ref, kvt_ref, do_ref, dot_ref, lse_ref,
                     delta_ref, dqt_ref, own_ref, send_ref, dq_sc, dkvt_ref):
    query_count = lists_ref.shape[0]
    dkvt_ref[...] = jnp.zeros(dkvt_ref.shape, jnp.float32)
    def per_query(qb, carry):
        dq_sc[...] = jnp.zeros(dq_sc.shape, jnp.float32)

        def visit(slots, qb=qb):
            blocks = [pos_ref[lists_ref[qb, j]] for j in slots]
            st = _nn(_pair_rows(kvt_ref, blocks, 0), qt_ref[qb]) * SCALE
            pt = jnp.exp(st - lse_ref[qb])
            dvt = jnp.transpose(_nn(pt.astype(jnp.bfloat16), do_ref[qb]))
            dpt = _nn(_pair_rows(kvt_ref, blocks, HEAD_DIM), dot_ref[qb])
            dst = (pt * (dpt - delta_ref[qb])).astype(jnp.bfloat16)
            dq_sc[...] += _nn(_pair_cols(kvt_ref, blocks, 0), dst)
            dkt = jnp.transpose(_nn(dst, q_ref[qb]))
            for place, b in enumerate(blocks):
                cols = slice(place * BLOCK, (place + 1) * BLOCK)
                dkvt_ref[b, :HEAD_DIM, :] += dkt[:, cols]
                dkvt_ref[b, HEAD_DIM:, :] += dvt[:, cols]

        _visit_slots(count_ref, qb, visit, group=16)
        dqt_ref[qb] = (dq_sc[...] * SCALE).astype(jnp.bfloat16)
        return carry

    lax.fori_loop(0, query_count, per_query, 0)
    held = own_ref.shape[0]

    def hand_over(i, carry):
        own_ref[i] = dkvt_ref[i]
        for part in range(send_ref.shape[0]):
            send_ref[part, i] = dkvt_ref[(part + 1) * held + i].astype(jnp.bfloat16)
        return carry

    lax.fori_loop(0, held, hand_over, 0)


def attend_local(q_rows, do_rows, kv_t, lists, keep, outer, positions):
    slots = lists.shape[1]
    rank = jnp.cumsum(keep, axis=1) - 1
    hit = (rank[:, :, None] == jnp.arange(slots, dtype=jnp.int32)[None, None, :]) & (keep[:, :, None] == 1)
    lists = jnp.sum(jnp.where(hit, lists[:, :, None], 0), axis=1).astype(jnp.int32)
    keep = jnp.broadcast_to(jnp.sum(keep, axis=1, keepdims=True), lists.shape).astype(jnp.int32)
    query_count, rows, _ = q_rows.shape
    block_total = kv_t.shape[0]
    f32 = jnp.float32
    do_t = jnp.swapaxes(do_rows, 1, 2)
    q_t = jnp.swapaxes(q_rows, 1, 2)
    o_t, lse, delta = pl.pallas_call(
        _forward_kernel,
        out_shape=(
            jax.ShapeDtypeStruct((query_count, HEAD_DIM, rows), jnp.bfloat16),
            jax.ShapeDtypeStruct((query_count, 1, rows), f32),
            jax.ShapeDtypeStruct((query_count, 1, rows), f32),
        ),
        in_specs=[_smem(), _smem(), _smem(), _vmem(), _vmem(), _vmem()],
        out_specs=(_vmem(), _vmem(), _vmem()),
        scratch_shapes=[
            pltpu.VMEM((1, rows), f32),
            pltpu.VMEM((1, rows), f32),
            pltpu.VMEM((HEAD_DIM, rows), f32),
        ],
        compiler_params=pltpu.CompilerParams(vmem_limit_bytes=VMEM_LIMIT),
    )(lists, keep, positions, q_t, kv_t, do_t)
    held = block_total // outer
    dq_t, own, send = pl.pallas_call(
        _backward_kernel,
        out_shape=(
            jax.ShapeDtypeStruct((query_count, HEAD_DIM, rows), jnp.bfloat16),
            jax.ShapeDtypeStruct((held, 2 * HEAD_DIM, BLOCK), f32),
            jax.ShapeDtypeStruct((outer - 1, held, 2 * HEAD_DIM, BLOCK), jnp.bfloat16),
        ),
        in_specs=[_smem(), _smem(), _smem()] + [_vmem()] * 7,
        out_specs=(_vmem(), _vmem(), _vmem()),
        scratch_shapes=[
            pltpu.VMEM((HEAD_DIM, rows), f32),
            pltpu.VMEM((block_total, 2 * HEAD_DIM, BLOCK), f32),
        ],
        compiler_params=pltpu.CompilerParams(vmem_limit_bytes=VMEM_LIMIT),
    )(lists, keep, positions, q_rows, q_t, kv_t, do_rows, do_t, lse, delta)
    return jnp.swapaxes(o_t, 1, 2), jnp.swapaxes(dq_t, 1, 2), (own, send)


def first_occurrence(block_lists):
    slots = block_lists.shape[1]
    positions = jnp.arange(slots, dtype=jnp.int32)
    matches = block_lists[:, :, None] == block_lists[:, None, :]
    earlier = jnp.any(matches & (positions[None, None, :] < positions[None, :, None]), axis=2)
    return jnp.logical_not(earlier).astype(jnp.int32)


def device_table(mesh):
    flat = mesh.devices.reshape(-1)
    table = np.array([[*d.coords, d.core_on_chip] for d in flat], dtype=np.int32)
    sizes = table.max(axis=0) + 1
    stages = [(1, int(sizes[1])), (0, int(sizes[0])), (2, int(sizes[2])), (3, int(sizes[3]))]
    stages = [(axis, size) for axis, size in stages if size > 1]
    where = {tuple(row): index for index, row in enumerate(table.tolist())}

    def pairs(axis, shift):
        out = []
        for index, row in enumerate(table.tolist()):
            dest = list(row)
            dest[axis] = (row[axis] + shift) % int(sizes[axis])
            out.append((index, where[tuple(dest)]))
        return out

    return table, stages, pairs


def make_local(mesh):
    table_np, stages, pairs = device_table(mesh)
    axes = ("blk", "split")

    held_np = np.zeros((table_np.shape[0], table_np.shape[0]), np.int32)
    stride = 1
    for axis, size in stages:
        held_np += ((table_np[None, :, axis] - table_np[:, None, axis]) % size) * stride
        stride *= size

    def gather_blocks(piece):
        buf = piece[None]
        for axis, size in stages:
            pieces = [buf]
            for shift in range(1, size):
                pieces.append(lax.ppermute(buf, axes, pairs(axis, size - shift)))
            buf = jnp.concatenate(pieces, axis=0)
        return buf

    def scatter_sum(own, sent_first, piece_shape):
        later = list(reversed(stages))
        first_axis, first_size = later.pop(0)
        part = own
        for shift in range(1, first_size):
            part = part + lax.ppermute(
                sent_first[shift - 1], axes, pairs(first_axis, shift)).astype(jnp.float32)
        part = part.reshape(tuple(size for _, size in later) + piece_shape)
        for axis, size in later:
            total = part[0]
            for shift in range(1, size):
                sent = part[shift].astype(jnp.bfloat16)
                total = total + lax.ppermute(sent, axes, pairs(axis, shift)).astype(jnp.float32)
            part = total
        return part

    def local(queries, keys, values, out_grad, block_lists):
        query_count = block_lists.shape[0]
        token_rows = queries.shape[0]
        split_size = lax.axis_size("split")
        split_place = lax.axis_index("split")
        me = lax.axis_index("blk") * split_size + split_place
        width = queries.shape[1] // split_size
        heads_here = width // HEAD_DIM

        table = jnp.asarray(table_np)
        own = table[me]

        kv_t = gather_blocks(jnp.concatenate([keys.T, values.T], axis=0))
        block_total = kv_t.shape[0]

        def held_at(block):
            coords = table[block]
            position = jnp.zeros_like(block)
            stride = 1
            for axis, size in stages:
                position = position + ((coords[..., axis] - own[axis]) % size) * stride
                stride *= size
            return position

        def my_heads(x):
            part = lax.dynamic_slice_in_dim(x, split_place * width, width, axis=1)
            return part.reshape(query_count, BLOCK * heads_here, HEAD_DIM)

        lists = block_lists.astype(jnp.int32)
        keep = first_occurrence(lists)
        o_rows, dq_rows, dkv_t = attend_local(
            my_heads(queries), my_heads(out_grad), kv_t, lists, keep, stages[-1][1],
            lax.dynamic_index_in_dim(jnp.asarray(held_np), me, keepdims=False))

        def join_halves(rows):
            mine = rows.reshape(token_rows, width)
            other = lax.ppermute(mine, "split", [(i, (i + 1) % split_size) for i in range(split_size)])
            return jnp.where(split_place == 0,
                             jnp.concatenate([mine, other], axis=1),
                             jnp.concatenate([other, mine], axis=1))

        attended = join_halves(o_rows)
        query_grad = join_halves(dq_rows)
        owned = scatter_sum(*dkv_t, (2 * HEAD_DIM, BLOCK))
        key_grad = (owned[:HEAD_DIM].T * SCALE).astype(jnp.bfloat16)
        value_grad = owned[HEAD_DIM:].T.astype(jnp.bfloat16)
        return (attended, query_grad, key_grad, value_grad)

    return local


def solution(mesh):
    placed = (
        P("blk", None),
        P(("blk", "split"), None),
        P(("blk", "split"), None),
        P("blk", None),
        P("blk", None),
    )
    return jax.shard_map(
        make_local(mesh),
        mesh=mesh,
        in_specs=placed,
        out_specs=(
            P("blk", None),
            P("blk", None),
            P(("blk", "split"), None),
            P(("blk", "split"), None),
        ),
        check_vma=False,
    )
```
